128 devices in a mesh: gx: 8 (over y, core), gy: 16 (over x, z).
Axes of the slice: x: 4, y: 4, z: 4, core: 2. Of those that a mesh axis runs over, the one named last changes fastest.
Arguments:
- bricks: bfloat16 [32768, 1536], P(('gx', 'gy')), may hold values from -6 to 6
- brick_target: int32 [32768, 1], P(('gx', 'gy')), may hold values from 0 to 127; in each aligned block of 256 rows (0 to 255, 256 to 511, ...) at most 6 rows name the same one
- brick_slot: int32 [32768], P(('gx', 'gy')), may hold values from 0 to 511
- screen: float32 [256, 1024, 128], P('gx', 'gy'), may hold values from 0.05 to 2
- coarse_guess: float32 [256, 1024, 128], P('gx', 'gy'), may hold values from -18 to 18
Outputs:
- solution_field: float32 [256, 1024, 128], P('gx', 'gy')
- residual: float32 [256, 1024, 128], P('gx', 'gy')
The draws below stay inside these ranges and needn't reach their ends.
Inputs may be any that keep to these rules, and one draw needn't show every extreme that they name: `brick_target`: among the 256 bricks of one device, no target is named more than 6 times, a bound that some block reaches.
All inputs are finite; a program needn't handle non-finite values.
Results may differ from the reference program's by a relative error of at most 0.0003.
Values may be sent and summed in bfloat16 or wider, within the bound.
No kernel may reach another device: no remote copies, remote signals or barrier semaphores. Data moves between devices by JAX's collectives and lax.ppermute only.
A program may use at most 128 MiB of HBM per device.

```python
import math
import jax
import jax.numpy as jnp
import numpy as np

CX = 32
CY = 64
NZ = 128
B_DEV = 256
ITERS = 2
CAP = 6
LB = 512
NX = 256
NY = 1024
BRICKS = 32768
N_GY = 16
DEVICES = 128


def draw_coarse_guess(key, part):
    grid_rows = jnp.arange(NX, dtype=jnp.float32)
    x_ramp = (1.0 + 2.0 * grid_rows / max(NX - 1, 1))[:, None, None]
    noise = jnp.clip(jax.random.normal(key, (NX, NY, NZ), jnp.float32), -6.0, 6.0)
    return x_ramp * noise


def plant(array, stream_key, low, top_value):
    dims = array.shape
    place = [jax.random.randint(jax.random.fold_in(stream_key, axis), (), 0, dims[axis]) for axis in range(len(dims))]
    array = array.at[tuple(place)].set(low)
    longest = dims.index(max(dims))
    place[longest] = (place[longest] + 1) % dims[longest]
    return array.at[tuple(place)].set(top_value)


def block_levels(own_key, shape, shards, low, high):
    factor_of = 1.0
    for position, shards_of in shards:
        steps = jax.random.uniform(jax.random.fold_in(jax.random.fold_in(own_key, 6), position), (shards_of,), jnp.float32, low / len(shards), high / len(shards))
        factor_of = factor_of * jnp.repeat(jnp.exp(steps), shape[position] // shards_of).reshape((-1,) + (1,) * (len(shape) - 1 - position))
    return factor_of


def routed_block(stream_key, own, number, rows, amount, top, bound, skew):
    ranking = jax.random.permutation(stream_key, amount)
    heavy_load, common = portions_of(amount, rows * top, bound, skew, True), portions_of(amount, rows * top, bound, skew, False)
    places = jnp.arange(amount)

    def named(lengths, rotation):
        used = int((lengths > 0).sum())
        fixed = max(1, used // 4)
        shifted = fixed + (places - fixed + rotation * (used - fixed)) % max(1, amount - fixed)
        return jnp.zeros((amount,), jnp.int32).at[ranking[jnp.where(places < fixed, places, shifted)]].set(jnp.asarray(lengths, jnp.int32))

    lengths = jnp.where(number % 4 == 0, named(heavy_load, number // 4), named(common, number - number // 4 - 1))
    mixed = jax.random.permutation(jax.random.fold_in(own, 3), amount)
    donor, receiver = mixed[0:amount // 2 * 2:2], mixed[1:amount // 2 * 2:2]
    margin = jnp.minimum(lengths[donor] - 1, bound - lengths[receiver]) // 2
    margin = jnp.where((donor == ranking[0]) | (receiver == ranking[0]) | (lengths[receiver] == 0), 0, jnp.maximum(margin, 0))
    shifted = jax.random.randint(jax.random.fold_in(own, 4), (amount // 2,), 0, 1 << 20) % (margin + 1)
    lengths = lengths.at[donor].add(-shifted).at[receiver].add(shifted)
    members = jnp.searchsorted(jnp.cumsum(lengths), jnp.arange(rows * top), side="right").astype(jnp.int32)
    listing = members.reshape(top, rows).T
    listing = listing[jax.random.permutation(jax.random.fold_in(own, 1), rows)]
    rotation = jax.random.randint(jax.random.fold_in(own, 2), (rows, 1), 0, top)
    return jnp.take_along_axis(listing, (jnp.arange(top)[None, :] + rotation) % top, axis=1)


def portions_of(count, total, most, lean, full):
    loads = [(1 << 20) // math.isqrt(standing ** lean) + 1 for standing in range(1, count + 1)]
    largest = most if full else min(most, max(-(-total // count), total * loads[0] // sum(loads)))
    least = 1 if total - largest >= count - 1 else 0
    holding, surplus = [largest] + [least] * (count - 1), total - largest - least * (count - 1)
    while surplus > 0:
        movable = [i for i in range(1, count) if holding[i] < largest] or [i for i in range(1, count) if holding[i] < most]
        whole, left = sum([loads[i] for i in movable]), surplus
        for i in movable:
            extra = min(most - holding[i], max(1, left * loads[i] // whole), surplus)
            holding[i] = holding[i] + extra
            surplus = surplus - extra
    return np.array(holding)


def normal_values(stream_key, dims, scale, reach, split=(), kind=jnp.bfloat16):
    drawn = jax.random.normal(stream_key, dims, jnp.float32) * scale
    if len(split) > 0:
        drawn = block_levels(stream_key, dims, split, -0.22, 0.18) * drawn
    return jnp.clip(drawn, min=-reach, max=reach).astype(kind)


def setup_inputs(seed: int = 0) -> dict:
    streams_of = jax.random.split(jax.random.key(seed), 6)
    bricks = normal_values(streams_of[0], (BRICKS, 1536), 1.0, 6.0, ((0, 128),))
    brick_target_keys = jax.random.split(jax.random.fold_in(streams_of[1], 1), BRICKS // B_DEV)
    brick_target_turns = jax.random.permutation(jax.random.fold_in(streams_of[1], 3), BRICKS // B_DEV)
    brick_target = jax.vmap(lambda own, number: routed_block(jax.random.fold_in(streams_of[1], 2), own, number, B_DEV, DEVICES, 1, CAP, 2))(brick_target_keys, brick_target_turns).reshape((BRICKS, 1))
    brick_slot = plant(jax.random.randint(streams_of[2], (BRICKS,), 0, LB), jax.random.fold_in(streams_of[2], 1), 0, LB - 1).astype(jnp.int32)
    screen = jnp.clip(jnp.exp(math.log(2.0) - 3.6888794 * jax.random.uniform(streams_of[3], (NX, NY, NZ), jnp.float32) ** block_levels(streams_of[3], (NX, NY, NZ), ((0, 8), (1, 16)), -0.2, 0.2)), 0.05, 2.0)
    coarse_guess = draw_coarse_guess(jax.random.fold_in(streams_of[5], 71), 0)
    return dict(bricks=bricks, brick_target=brick_target, brick_slot=brick_slot, screen=screen, coarse_guess=coarse_guess)


def splat(bricks, brick_target, brick_slot):
    span_x = CX // 8
    span_y = CY // 8
    span_z = NZ // 8
    blocks_x = NX // 8
    blocks_y = NY // 8
    target = brick_target[:, 0]
    local_x = brick_slot // (span_y * span_z)
    local_y = (brick_slot // span_z) % span_y
    local_z = brick_slot % span_z
    block_x = (target // N_GY) * span_x + local_x
    block_y = (target % N_GY) * span_y + local_y
    flat_index = ((block_x * blocks_y + block_y) * span_z + local_z).astype(jnp.int32)
    blocks = jnp.zeros((blocks_x * blocks_y * span_z, 1536), jnp.float32)
    blocks = blocks.at[flat_index].add(bricks.astype(jnp.float32))
    field = blocks.reshape(blocks_x, blocks_y, span_z, 3, 8, 8, 8).transpose(3, 0, 4, 1, 5, 2, 6)
    return field.reshape(3, NX, NY, NZ)


def divergence(normals):
    along_x = jnp.pad(normals[0], ((1, 1), (0, 0), (0, 0)))
    along_y = jnp.pad(normals[1], ((0, 0), (1, 1), (0, 0)))
    along_z = jnp.pad(normals[2], ((0, 0), (0, 0), (1, 1)))
    total = along_x[2:] - along_x[:-2]
    total = total + (along_y[:, 2:] - along_y[:, :-2])
    total = total + (along_z[:, :, 2:] - along_z[:, :, :-2])
    return -0.5 * total


def operate(field, screen):
    padded = jnp.pad(field, 1)
    beside = padded[2:, 1:-1, 1:-1] + padded[:-2, 1:-1, 1:-1]
    beside = beside + padded[1:-1, 2:, 1:-1] + padded[1:-1, :-2, 1:-1]
    beside = beside + padded[1:-1, 1:-1, 2:] + padded[1:-1, 1:-1, :-2]
    return (6.0 + screen) * field - beside


def reference(bricks, brick_target, brick_slot, screen, coarse_guess):
    source = divergence(splat(bricks, brick_target, brick_slot))
    inverse = 1.0 / (6.0 + screen)
    solution = coarse_guess
    residual = source - operate(solution, screen)
    precond = residual * inverse
    direction = precond
    gamma = jnp.sum(residual * precond)
    for step in range(ITERS):
        image = operate(direction, screen)
        alpha = gamma / jnp.sum(direction * image)
        solution = solution + alpha * direction
        residual = residual - alpha * image
        if step + 1 < ITERS:
            precond = residual * inverse
            gamma_next = jnp.sum(residual * precond)
            direction = precond + (gamma_next / gamma) * direction
            gamma = gamma_next
    return solution, residual
```

```python
import jax
import jax.numpy as jnp
from jax import lax
from jax.sharding import Mesh
from jax.sharding import PartitionSpec as P

ITERS = 2
GX_GY = ("gx_0", "gx_1", "gy_0", "gy_1")
GX = ("gx_0", "gx_1")
GY = ("gy_0", "gy_1")


def extended(shard, sides, width):
    edges = {}
    for axis, dim in sides:
        count, length = (lax.axis_size(axis), shard.shape[dim])
        up = [(i, (i + 1) % count) for i in range(count - 1)]
        last = lax.slice_in_dim(shard, length - width, length, axis=dim)
        first = lax.slice_in_dim(shard, 0, width, axis=dim)
        edges[dim] = (
            lax.ppermute(last, axis, up),
            lax.ppermute(first, axis, [(b, a) for a, b in up]),
        )
    done = []
    for _, dim in sides:
        low, high = edges[dim]
        around = [(width, width) if d in done else (0, 0) for d in range(shard.ndim)]
        shard = jnp.concatenate([jnp.pad(low, around), shard, jnp.pad(high, around)], axis=dim)
        done.append(dim)
    return shard


def over_axes(shard, axes):
    for axis in axes:
        shard = lax.psum(shard, axis)
    return shard


def with_halo(block, sides, width):
    for axis, dim in sides:
        count = lax.axis_size(axis)
        forward = [(i, i + 1) for i in range(count - 1)]
        backward = [(target, source) for source, target in forward]
        low = lax.ppermute(
            lax.slice_in_dim(block, block.shape[dim] - width, None, axis=dim), axis, forward
        )
        high = lax.ppermute(lax.slice_in_dim(block, 0, width, axis=dim), axis, backward)
        block = jnp.concatenate([low, block, high], axis=dim)
    return block


def build_send(bricks, brick_target, brick_slot, peers, capacity):
    target = brick_target[:, 0]
    onehot = (target[:, None] == jnp.arange(peers, dtype=jnp.int32)[None, :]).astype(jnp.int32)
    earlier = jnp.cumsum(onehot, axis=0) - onehot
    order = jnp.sum(earlier * onehot, axis=1)
    place = target * capacity + order
    payload = jnp.zeros((peers * capacity, bricks.shape[1]), bricks.dtype).at[place].set(bricks)
    slots = jnp.zeros((peers * capacity,), jnp.int32).at[place].set(brick_slot)
    return (payload, slots)


def next_along_z(field):
    edge = jnp.zeros(field.shape[:-1] + (1,), field.dtype)
    return jnp.concatenate([field[..., 1:], edge], axis=-1)


def prior_along_z(field):
    edge = jnp.zeros(field.shape[:-1] + (1,), field.dtype)
    return jnp.concatenate([edge, field[..., :-1]], axis=-1)


def operate(field, screen):
    padded = extended(field, ((GX, 0), (GY, 1)), 1)
    beside = padded[2:, 1:-1] + padded[:-2, 1:-1]
    beside = beside + padded[1:-1, 2:] + padded[1:-1, :-2]
    beside = beside + next_along_z(field) + prior_along_z(field)
    return (6.0 + screen) * field - beside


def paired_total(first, second):
    both = lax.psum(jnp.stack([first, second]), GX_GY)
    return (both[0], both[1])


def component_grid(blocks, comp, span_x, span_y, span_z):
    part_blocks = blocks[:, comp, :].reshape(span_x, span_y, span_z, 8, 8, 8)
    grid = part_blocks.transpose(0, 3, 1, 4, 2, 5)
    return grid.reshape(span_x * 8, span_y * 8, span_z * 8)


def body(bricks, brick_target, brick_slot, screen, coarse_guess):
    peers = lax.axis_size(GX_GY)
    capacity = max(2, 3 * bricks.shape[0] // peers)
    payload, slots = build_send(bricks, brick_target, brick_slot, peers, capacity)
    arrived, landed = (
        lax.all_to_all(
            payload.reshape(peers, capacity, 1536), GX_GY, split_axis=0, concat_axis=0, tiled=True
        ),
        lax.all_to_all(
            slots.reshape(peers, capacity), GX_GY, split_axis=0, concat_axis=0, tiled=True
        ),
    )
    width_x, width_y, depth = screen.shape
    span_x = width_x // 8
    span_y = width_y // 8
    span_z = depth // 8
    blocks = jnp.zeros((span_x * span_y * span_z, 1536), jnp.float32)
    blocks = blocks.at[landed.reshape(-1)].add(arrived.reshape(-1, 1536).astype(jnp.float32))
    blocks = blocks.reshape(span_x * span_y * span_z, 3, 512)
    normal_x = component_grid(blocks, 0, span_x, span_y, span_z)
    normal_y = component_grid(blocks, 1, span_x, span_y, span_z)
    normal_z = component_grid(blocks, 2, span_x, span_y, span_z)
    along_x = with_halo(normal_x, ((GX, 0),), 1)
    along_y = with_halo(normal_y, ((GY, 1),), 1)
    total = along_x[2:] - along_x[:-2]
    total = total + (along_y[:, 2:] - along_y[:, :-2])
    total = total + (next_along_z(normal_z) - prior_along_z(normal_z))
    source = -0.5 * total
    inverse = 1.0 / (6.0 + screen)
    solution = coarse_guess
    residual = source - operate(solution, screen)
    precond = residual * inverse
    image = operate(precond, screen)
    gamma, delta = paired_total(jnp.sum(residual * precond), jnp.sum(image * precond))
    alpha = gamma / delta
    direction = precond
    along = image
    for step in range(ITERS):
        solution = solution + alpha * direction
        residual = residual - alpha * along
        if step + 1 < ITERS:
            precond = residual * inverse
            image = operate(precond, screen)
            gamma_next, delta = paired_total(jnp.sum(residual * precond), jnp.sum(image * precond))
            ratio = gamma_next / gamma
            alpha = gamma_next / (delta - ratio * gamma_next / alpha)
            direction = precond + ratio * direction
            along = image + ratio * along
            gamma = gamma_next
    return (solution, residual)


def solution(mesh):
    split = Mesh(mesh.devices.reshape(4, 2, 4, 4), ("gx_0", "gx_1", "gy_0", "gy_1"))
    placed = (P(GX_GY, None), P(GX_GY, None), P(GX_GY), P(GX, GY, None), P(GX, GY, None))
    return jax.shard_map(
        body,
        mesh=split,
        in_specs=placed,
        out_specs=(P(GX, GY, None), P(GX, GY, None)),
        check_vma=False,
    )
```

```python
import jax
import jax.numpy as jnp
from jax import lax
from jax.sharding import Mesh
from jax.sharding import PartitionSpec as P
from jax.experimental import pallas as pl
from jax.experimental.pallas import tpu as pltpu

ITERS = 2
GX_GY = ("gx_0", "gx_1", "gy_0", "gy_1")
GX = ("gx_0", "gx_1")
GY = ("gy_0", "gy_1")


def extended(shard, sides, width):
    edges = {}
    for axis, dim in sides:
        count, length = (lax.axis_size(axis), shard.shape[dim])
        up = [(i, (i + 1) % count) for i in range(count - 1)]
        last = lax.slice_in_dim(shard, length - width, length, axis=dim)
        first = lax.slice_in_dim(shard, 0, width, axis=dim)
        edges[dim] = (
            lax.ppermute(last, axis, up),
            lax.ppermute(first, axis, [(b, a) for a, b in up]),
        )
    done = []
    for _, dim in sides:
        low, high = edges[dim]
        around = [(width, width) if d in done else (0, 0) for d in range(shard.ndim)]
        shard = jnp.concatenate([jnp.pad(low, around), shard, jnp.pad(high, around)], axis=dim)
        done.append(dim)
    return shard


def over_axes(shard, axes):
    for axis in axes:
        shard = lax.psum(shard, axis)
    return shard


def with_halo(block, sides, width):
    for axis, dim in sides:
        count = lax.axis_size(axis)
        forward = [(i, i + 1) for i in range(count - 1)]
        backward = [(target, source) for source, target in forward]
        low = lax.ppermute(
            lax.slice_in_dim(block, block.shape[dim] - width, None, axis=dim), axis, forward
        )
        high = lax.ppermute(lax.slice_in_dim(block, 0, width, axis=dim), axis, backward)
        block = jnp.concatenate([low, block, high], axis=dim)
    return block


def build_send(bricks, brick_target, brick_slot, peers, capacity):
    target = brick_target[:, 0]
    onehot = (target[:, None] == jnp.arange(peers, dtype=jnp.int32)[None, :]).astype(jnp.int32)
    earlier = jnp.cumsum(onehot, axis=0) - onehot
    order = jnp.sum(earlier * onehot, axis=1)
    place = target * capacity + order
    payload = jnp.zeros((peers * capacity, bricks.shape[1]), bricks.dtype).at[place].set(bricks)
    slots = jnp.zeros((peers * capacity,), jnp.int32).at[place].set(brick_slot)
    return (payload, slots)


def next_along_z(field):
    edge = jnp.zeros(field.shape[:-1] + (1,), field.dtype)
    return jnp.concatenate([field[..., 1:], edge], axis=-1)


def prior_along_z(field):
    edge = jnp.zeros(field.shape[:-1] + (1,), field.dtype)
    return jnp.concatenate([edge, field[..., :-1]], axis=-1)


def operate(field, screen):
    padded = extended(field, ((GX, 0), (GY, 1)), 1)
    beside = padded[2:, 1:-1] + padded[:-2, 1:-1]
    beside = beside + padded[1:-1, 2:] + padded[1:-1, :-2]
    beside = beside + next_along_z(field) + prior_along_z(field)
    return (6.0 + screen) * field - beside


def paired_total(first, second):
    return (over_axes(first, GX_GY), over_axes(second, GX_GY))


def component_grid(blocks, comp, span_x, span_y, span_z):
    part_blocks = blocks[:, comp, :].reshape(span_x, span_y, span_z, 8, 8, 8)
    grid = part_blocks.transpose(0, 3, 1, 4, 2, 5)
    return grid.reshape(span_x * 8, span_y * 8, span_z * 8)


def relayout_kernel(blk_ref, out_ref):
    sub = lax.broadcasted_iota(jnp.int32, (8, 128), 0)
    lane = lax.broadcasted_iota(jnp.int32, (8, 128), 1)
    grp = (lane // 8) % 8
    low_half = lane < 64
    swaps = []
    for m in (4, 2, 1):
        first = ((sub & m) == 0) & ((grp & m) != 0)
        second = ((sub & m) != 0) & ((grp & m) == 0)
        swaps.append((m, first, second))

    def transpose_groups(x):
        for m, first, second in swaps:
            a = pltpu.roll(pltpu.roll(x, 8 - m, 0), 8 * m, 1)
            b = pltpu.roll(pltpu.roll(x, m, 0), 128 - 8 * m, 1)
            x = jnp.where(first, a, jnp.where(second, b, x))
        return x

    def step(i, carry):
        uh = i % 4
        c = (i // 4) % 3
        ly = (i // 12) % 8
        lx = i // 96
        row = pl.multiple_of((lx * 8 + ly) * 16, 16)
        col = pl.multiple_of((c * 4 + uh) * 128, 128)
        s0 = blk_ref[pl.ds(row, 8), pl.ds(col, 128)]
        s1 = blk_ref[pl.ds(row + 8, 8), pl.ds(col, 128)]
        u0 = jnp.where(low_half, s0, pltpu.roll(s1, 64, 1))
        u1 = jnp.where(low_half, pltpu.roll(s0, 64, 1), s1)
        y = pl.multiple_of(ly * 8, 8)
        out_ref[c, lx * 8 + uh * 2, pl.ds(y, 8), :] = transpose_groups(u0)
        out_ref[c, lx * 8 + uh * 2 + 1, pl.ds(y, 8), :] = transpose_groups(u1)
        return carry

    lax.fori_loop(0, 384, step, 0)


def to_grid(blocks, span_x, span_y, depth):
    return pl.pallas_call(
        relayout_kernel,
        out_shape=jax.ShapeDtypeStruct((3, span_x * 8, span_y * 8, depth), jnp.float32),
        in_specs=[pl.BlockSpec(memory_space=pltpu.VMEM)],
        out_specs=pl.BlockSpec(memory_space=pltpu.VMEM),
    )(blocks)


def body(bricks, brick_target, brick_slot, screen, coarse_guess):
    peers = lax.axis_size(GX_GY)
    capacity = max(2, 3 * bricks.shape[0] // peers)
    payload, slots = build_send(bricks, brick_target, brick_slot, peers, capacity)
    arrived, landed = (
        lax.all_to_all(
            payload.reshape(peers, capacity, 1536), GX_GY, split_axis=0, concat_axis=0, tiled=True
        ),
        lax.all_to_all(
            slots.reshape(peers, capacity), GX_GY, split_axis=0, concat_axis=0, tiled=True
        ),
    )
    width_x, width_y, depth = screen.shape
    span_x = width_x // 8
    span_y = width_y // 8
    span_z = depth // 8
    picks = landed.reshape(-1, 1) == jnp.arange(span_x * span_y * span_z, dtype=jnp.int32)[None, :]
    blocks = jnp.einsum(
        "ks,kj->sj",
        picks.astype(jnp.bfloat16),
        arrived.reshape(-1, 1536),
        preferred_element_type=jnp.float32,
    )
    normals = to_grid(blocks, span_x, span_y, depth)
    normal_x, normal_y, normal_z = normals[0], normals[1], normals[2]
    along_x = with_halo(normal_x, ((GX, 0),), 1)
    along_y = with_halo(normal_y, ((GY, 1),), 1)
    total = along_x[2:] - along_x[:-2]
    total = total + (along_y[:, 2:] - along_y[:, :-2])
    total = total + (next_along_z(normal_z) - prior_along_z(normal_z))
    source = -0.5 * total
    inverse = 1.0 / (6.0 + screen)
    solution = coarse_guess
    residual = source - operate(solution, screen)
    precond = residual * inverse
    image = operate(precond, screen)
    gamma, delta = paired_total(jnp.sum(residual * precond), jnp.sum(image * precond))
    alpha = gamma / delta
    direction = precond
    along = image
    for step in range(ITERS):
        solution = solution + alpha * direction
        residual = residual - alpha * along
        if step + 1 < ITERS:
            precond = residual * inverse
            image = operate(precond, screen)
            gamma_next, delta = paired_total(jnp.sum(residual * precond), jnp.sum(image * precond))
            ratio = gamma_next / gamma
            alpha = gamma_next / (delta - ratio * gamma_next / alpha)
            direction = precond + ratio * direction
            along = image + ratio * along
            gamma = gamma_next
    return (solution, residual)


def solution(mesh):
    split = Mesh(mesh.devices.reshape(4, 2, 4, 4), ("gx_0", "gx_1", "gy_0", "gy_1"))
    placed = (P(GX_GY, None), P(GX_GY, None), P(GX_GY), P(GX, GY, None), P(GX, GY, None))
    return jax.shard_map(
        body,
        mesh=split,
        in_specs=placed,
        out_specs=(P(GX, GY, None), P(GX, GY, None)),
        check_vma=False,
    )
```

```python
import jax
import jax.numpy as jnp
from jax import lax
from jax.sharding import Mesh
from jax.sharding import PartitionSpec as P
from jax.experimental import pallas as pl
from jax.experimental.pallas import tpu as pltpu

ITERS = 2
GX_GY = ("gx_0", "gx_1", "gy_0", "gy_1")
GX = ("gx_0", "gx_1")
GY = ("gy_0", "gy_1")


def extended(shard, sides, width):
    edges = {}
    for axis, dim in sides:
        count, length = (lax.axis_size(axis), shard.shape[dim])
        up = [(i, (i + 1) % count) for i in range(count - 1)]
        last = lax.slice_in_dim(shard, length - width, length, axis=dim)
        first = lax.slice_in_dim(shard, 0, width, axis=dim)
        edges[dim] = (
            lax.ppermute(last, axis, up),
            lax.ppermute(first, axis, [(b, a) for a, b in up]),
        )
    done = []
    for _, dim in sides:
        low, high = edges[dim]
        around = [(width, width) if d in done else (0, 0) for d in range(shard.ndim)]
        shard = jnp.concatenate([jnp.pad(low, around), shard, jnp.pad(high, around)], axis=dim)
        done.append(dim)
    return shard


def over_axes(shard, axes):
    for axis in axes:
        shard = lax.psum(shard, axis)
    return shard


def with_halo(block, sides, width):
    for axis, dim in sides:
        count = lax.axis_size(axis)
        forward = [(i, i + 1) for i in range(count - 1)]
        backward = [(target, source) for source, target in forward]
        low = lax.ppermute(
            lax.slice_in_dim(block, block.shape[dim] - width, None, axis=dim), axis, forward
        )
        high = lax.ppermute(lax.slice_in_dim(block, 0, width, axis=dim), axis, backward)
        block = jnp.concatenate([low, block, high], axis=dim)
    return block


def build_send(bricks, brick_target, brick_slot, peers, capacity):
    target = brick_target[:, 0]
    onehot = (target[:, None] == jnp.arange(peers, dtype=jnp.int32)[None, :]).astype(jnp.int32)
    earlier = jnp.cumsum(onehot, axis=0) - onehot
    order = jnp.sum(earlier * onehot, axis=1)
    place = target * capacity + order
    payload = jnp.zeros((peers * capacity, bricks.shape[1]), bricks.dtype).at[place].set(bricks)
    slots = jnp.zeros((peers * capacity,), jnp.int32).at[place].set(brick_slot)
    return (payload, slots)


def next_along_z(field):
    edge = jnp.zeros(field.shape[:-1] + (1,), field.dtype)
    return jnp.concatenate([field[..., 1:], edge], axis=-1)


def prior_along_z(field):
    edge = jnp.zeros(field.shape[:-1] + (1,), field.dtype)
    return jnp.concatenate([edge, field[..., :-1]], axis=-1)


def operate(field, screen):
    padded = extended(field, ((GX, 0), (GY, 1)), 1)
    beside = padded[2:, 1:-1] + padded[:-2, 1:-1]
    beside = beside + padded[1:-1, 2:] + padded[1:-1, :-2]
    beside = beside + next_along_z(field) + prior_along_z(field)
    return (6.0 + screen) * field - beside


def paired_total(first, second):
    return (over_axes(first, GX_GY), over_axes(second, GX_GY))


def component_grid(blocks, comp, span_x, span_y, span_z):
    part_blocks = blocks[:, comp, :].reshape(span_x, span_y, span_z, 8, 8, 8)
    grid = part_blocks.transpose(0, 3, 1, 4, 2, 5)
    return grid.reshape(span_x * 8, span_y * 8, span_z * 8)


def relayout_kernel(blk_ref, out_ref):
    sub = lax.broadcasted_iota(jnp.int32, (8, 128), 0)
    lane = lax.broadcasted_iota(jnp.int32, (8, 128), 1)
    grp = (lane // 8) % 8
    low_half = lane < 64
    swaps = []
    for m in (4, 2, 1):
        first = ((sub & m) == 0) & ((grp & m) != 0)
        second = ((sub & m) != 0) & ((grp & m) == 0)
        swaps.append((m, first, second))

    def transpose_groups(x):
        for m, first, second in swaps:
            a = pltpu.roll(pltpu.roll(x, 8 - m, 0), 8 * m, 1)
            b = pltpu.roll(pltpu.roll(x, m, 0), 128 - 8 * m, 1)
            x = jnp.where(first, a, jnp.where(second, b, x))
        return x

    def step(i, carry):
        ly = i % 8
        lx = i // 8
        row = pl.multiple_of(i * 16, 16)
        y = pl.multiple_of(ly * 8, 8)
        top = blk_ref[pl.ds(row, 8), :]
        bottom = blk_ref[pl.ds(row + 8, 8), :]
        for c in range(3):
            for uh in range(4):
                col = (c * 4 + uh) * 128
                s0 = top[:, col:col + 128]
                s1 = bottom[:, col:col + 128]
                u0 = jnp.where(low_half, s0, pltpu.roll(s1, 64, 1))
                u1 = jnp.where(low_half, pltpu.roll(s0, 64, 1), s1)
                out_ref[c, lx * 8 + uh * 2, pl.ds(y, 8), :] = transpose_groups(u0)
                out_ref[c, lx * 8 + uh * 2 + 1, pl.ds(y, 8), :] = transpose_groups(u1)
        return carry

    lax.fori_loop(0, 32, step, 0)


def to_grid(blocks, span_x, span_y, depth):
    return pl.pallas_call(
        relayout_kernel,
        out_shape=jax.ShapeDtypeStruct((3, span_x * 8, span_y * 8, depth), jnp.float32),
        in_specs=[pl.BlockSpec(memory_space=pltpu.VMEM)],
        out_specs=pl.BlockSpec(memory_space=pltpu.VMEM),
    )(blocks)


def body(bricks, brick_target, brick_slot, screen, coarse_guess):
    peers = lax.axis_size(GX_GY)
    capacity = max(2, 3 * bricks.shape[0] // peers)
    payload, slots = build_send(bricks, brick_target, brick_slot, peers, capacity)
    arrived, landed = (
        lax.all_to_all(
            payload.reshape(peers, capacity, 1536), GX_GY, split_axis=0, concat_axis=0, tiled=True
        ),
        lax.all_to_all(
            slots.reshape(peers, capacity), GX_GY, split_axis=0, concat_axis=0, tiled=True
        ),
    )
    width_x, width_y, depth = screen.shape
    span_x = width_x // 8
    span_y = width_y // 8
    span_z = depth // 8
    picks = landed.reshape(-1, 1) == jnp.arange(span_x * span_y * span_z, dtype=jnp.int32)[None, :]
    blocks = jnp.einsum(
        "ks,kj->sj",
        picks.astype(jnp.bfloat16),
        arrived.reshape(-1, 1536),
        preferred_element_type=jnp.float32,
    )
    normals = to_grid(blocks, span_x, span_y, depth)
    normal_x, normal_y, normal_z = normals[0], normals[1], normals[2]
    along_x = with_halo(normal_x, ((GX, 0),), 1)
    along_y = with_halo(normal_y, ((GY, 1),), 1)
    total = along_x[2:] - along_x[:-2]
    total = total + (along_y[:, 2:] - along_y[:, :-2])
    total = total + (next_along_z(normal_z) - prior_along_z(normal_z))
    source = -0.5 * total
    inverse = 1.0 / (6.0 + screen)
    solution = coarse_guess
    residual = source - operate(solution, screen)
    precond = residual * inverse
    image = operate(precond, screen)
    gamma, delta = paired_total(jnp.sum(residual * precond), jnp.sum(image * precond))
    alpha = gamma / delta
    direction = precond
    along = image
    for step in range(ITERS):
        solution = solution + alpha * direction
        residual = residual - alpha * along
        if step + 1 < ITERS:
            precond = residual * inverse
            image = operate(precond, screen)
            gamma_next, delta = paired_total(jnp.sum(residual * precond), jnp.sum(image * precond))
            ratio = gamma_next / gamma
            alpha = gamma_next / (delta - ratio * gamma_next / alpha)
            direction = precond + ratio * direction
            along = image + ratio * along
            gamma = gamma_next
    return (solution, residual)


def solution(mesh):
    split = Mesh(mesh.devices.reshape(4, 2, 4, 4), ("gx_0", "gx_1", "gy_0", "gy_1"))
    placed = (P(GX_GY, None), P(GX_GY, None), P(GX_GY), P(GX, GY, None), P(GX, GY, None))
    return jax.shard_map(
        body,
        mesh=split,
        in_specs=placed,
        out_specs=(P(GX, GY, None), P(GX, GY, None)),
        check_vma=False,
    )
```

```python
import jax
import jax.numpy as jnp
from jax import lax
from jax.sharding import Mesh
from jax.sharding import PartitionSpec as P
from jax.experimental import pallas as pl
from jax.experimental.pallas import tpu as pltpu

GX_GY = ("gx_0", "gx_1", "gy_0", "gy_1")
GX = ("gx_0", "gx_1")
GY = ("gy_0", "gy_1")


def extended(shard, sides, width):
    edges = {}
    for axis, dim in sides:
        count, length = (lax.axis_size(axis), shard.shape[dim])
        up = [(i, (i + 1) % count) for i in range(count - 1)]
        last = lax.slice_in_dim(shard, length - width, length, axis=dim)
        first = lax.slice_in_dim(shard, 0, width, axis=dim)
        edges[dim] = (
            lax.ppermute(last, axis, up),
            lax.ppermute(first, axis, [(b, a) for a, b in up]),
        )
    done = []
    for _, dim in sides:
        low, high = edges[dim]
        around = [(width, width) if d in done else (0, 0) for d in range(shard.ndim)]
        shard = jnp.concatenate([jnp.pad(low, around), shard, jnp.pad(high, around)], axis=dim)
        done.append(dim)
    return shard


def over_axes(shard, axes):
    for axis in axes:
        shard = lax.psum(shard, axis)
    return shard


def with_halo(block, sides, width):
    for axis, dim in sides:
        count = lax.axis_size(axis)
        forward = [(i, i + 1) for i in range(count - 1)]
        backward = [(target, source) for source, target in forward]
        low = lax.ppermute(
            lax.slice_in_dim(block, block.shape[dim] - width, None, axis=dim), axis, forward
        )
        high = lax.ppermute(lax.slice_in_dim(block, 0, width, axis=dim), axis, backward)
        block = jnp.concatenate([low, block, high], axis=dim)
    return block


def build_send(bricks, brick_target, brick_slot, peers, capacity):
    target = brick_target[:, 0]
    onehot = (target[:, None] == jnp.arange(peers, dtype=jnp.int32)[None, :]).astype(jnp.int32)
    earlier = jnp.cumsum(onehot, axis=0) - onehot
    order = jnp.sum(earlier * onehot, axis=1)
    place = target * capacity + order
    payload = jnp.zeros((peers * capacity, bricks.shape[1]), bricks.dtype).at[place].set(bricks)
    slots = jnp.zeros((peers * capacity,), jnp.int32).at[place].set(brick_slot)
    return (payload, slots)


def next_along_z(field):
    edge = jnp.zeros(field.shape[:-1] + (1,), field.dtype)
    return jnp.concatenate([field[..., 1:], edge], axis=-1)


def prior_along_z(field):
    edge = jnp.zeros(field.shape[:-1] + (1,), field.dtype)
    return jnp.concatenate([edge, field[..., :-1]], axis=-1)


def operate(field, screen):
    padded = extended(field, ((GX, 0), (GY, 1)), 1)
    beside = padded[2:, 1:-1] + padded[:-2, 1:-1]
    beside = beside + padded[1:-1, 2:] + padded[1:-1, :-2]
    beside = beside + next_along_z(field) + prior_along_z(field)
    return (6.0 + screen) * field - beside


def component_grid(blocks, comp, span_x, span_y, span_z):
    part_blocks = blocks[:, comp, :].reshape(span_x, span_y, span_z, 8, 8, 8)
    grid = part_blocks.transpose(0, 3, 1, 4, 2, 5)
    return grid.reshape(span_x * 8, span_y * 8, span_z * 8)


def relayout_kernel(blk_ref, out_ref):
    sub = lax.broadcasted_iota(jnp.int32, (8, 128), 0)
    lane = lax.broadcasted_iota(jnp.int32, (8, 128), 1)
    grp = (lane // 8) % 8
    low_half = lane < 64
    swaps = []
    for m in (4, 2, 1):
        first = ((sub & m) == 0) & ((grp & m) != 0)
        second = ((sub & m) != 0) & ((grp & m) == 0)
        swaps.append((m, first, second))

    def transpose_groups(x):
        for m, first, second in swaps:
            a = pltpu.roll(pltpu.roll(x, 8 - m, 0), 8 * m, 1)
            b = pltpu.roll(pltpu.roll(x, m, 0), 128 - 8 * m, 1)
            x = jnp.where(first, a, jnp.where(second, b, x))
        return x

    def step(i, carry):
        ly = i % 8
        lx = i // 8
        row = pl.multiple_of(i * 16, 16)
        y = pl.multiple_of(ly * 8, 8)
        top = blk_ref[pl.ds(row, 8), :]
        bottom = blk_ref[pl.ds(row + 8, 8), :]
        for c in range(3):
            for uh in range(4):
                col = (c * 4 + uh) * 128
                s0 = top[:, col:col + 128]
                s1 = bottom[:, col:col + 128]
                u0 = jnp.where(low_half, s0, pltpu.roll(s1, 64, 1))
                u1 = jnp.where(low_half, pltpu.roll(s0, 64, 1), s1)
                out_ref[c, lx * 8 + uh * 2, pl.ds(y, 8), :] = transpose_groups(u0)
                out_ref[c, lx * 8 + uh * 2 + 1, pl.ds(y, 8), :] = transpose_groups(u1)
        return carry

    lax.fori_loop(0, 32, step, 0)


def to_grid(blocks, span_x, span_y, depth):
    return pl.pallas_call(
        relayout_kernel,
        out_shape=jax.ShapeDtypeStruct((3, span_x * 8, span_y * 8, depth), jnp.float32),
        in_specs=[pl.BlockSpec(memory_space=pltpu.VMEM)],
        out_specs=pl.BlockSpec(memory_space=pltpu.VMEM),
    )(blocks)


def body(bricks, brick_target, brick_slot, screen, coarse_guess):
    peers = lax.axis_size(GX_GY)
    capacity = max(2, 3 * bricks.shape[0] // peers)
    payload, slots = build_send(bricks, brick_target, brick_slot, peers, capacity)
    arrived, landed = (
        lax.all_to_all(
            payload.reshape(peers, capacity, 1536), GX_GY, split_axis=0, concat_axis=0, tiled=True
        ),
        lax.all_to_all(
            slots.reshape(peers, capacity), GX_GY, split_axis=0, concat_axis=0, tiled=True
        ),
    )
    width_x, width_y, depth = screen.shape
    span_x = width_x // 8
    span_y = width_y // 8
    span_z = depth // 8
    picks = landed.reshape(-1, 1) == jnp.arange(span_x * span_y * span_z, dtype=jnp.int32)[None, :]
    blocks = jnp.einsum(
        "ks,kj->sj",
        picks.astype(jnp.bfloat16),
        arrived.reshape(-1, 1536),
        preferred_element_type=jnp.float32,
    )
    normals = to_grid(blocks, span_x, span_y, depth)
    normal_x, normal_y, normal_z = normals[0], normals[1], normals[2]
    along_x = with_halo(normal_x, ((GX, 0),), 1)
    along_y = with_halo(normal_y, ((GY, 1),), 1)
    total = along_x[2:] - along_x[:-2]
    total = total + (along_y[:, 2:] - along_y[:, :-2])
    total = total + (next_along_z(normal_z) - prior_along_z(normal_z))
    source = -0.5 * total
    inverse = 1.0 / (6.0 + screen)
    residual = source - operate(coarse_guess, screen)
    precond = residual * inverse
    image = operate(precond, screen)
    scaled = image * inverse
    scaled_image = operate(scaled, screen)
    sums = over_axes(
        jnp.stack(
            [
                jnp.sum(residual * precond),
                jnp.sum(precond * image),
                jnp.sum(image * scaled),
                jnp.sum(scaled * scaled_image),
            ]
        ),
        GX_GY,
    )
    gamma, delta, energy, curvature = sums[0], sums[1], sums[2], sums[3]
    alpha = gamma / delta
    gamma_next = alpha * alpha * energy - gamma
    ratio = gamma_next / gamma
    grow = 1.0 + ratio
    delta_next = grow * grow * delta - 2.0 * grow * alpha * energy + alpha * alpha * curvature
    alpha_next = gamma_next / delta_next
    solution = coarse_guess + alpha * precond
    residual = residual - alpha * image
    direction = residual * inverse + ratio * precond
    along = image - alpha * scaled_image + ratio * image
    solution = solution + alpha_next * direction
    residual = residual - alpha_next * along
    return (solution, residual)


def solution(mesh):
    split = Mesh(mesh.devices.reshape(4, 2, 4, 4), ("gx_0", "gx_1", "gy_0", "gy_1"))
    placed = (P(GX_GY, None), P(GX_GY, None), P(GX_GY), P(GX, GY, None), P(GX, GY, None))
    return jax.shard_map(
        body,
        mesh=split,
        in_specs=placed,
        out_specs=(P(GX, GY, None), P(GX, GY, None)),
        check_vma=False,
    )
```

```python
import jax
import jax.numpy as jnp
from jax import lax
from jax.sharding import Mesh
from jax.sharding import PartitionSpec as P
from jax.experimental import pallas as pl
from jax.experimental.pallas import tpu as pltpu

GX_GY = ("gx_0", "gx_1", "gy_0", "gy_1")
GX = ("gx_0", "gx_1")
GY = ("gy_0", "gy_1")


def extended(shard, sides, width):
    edges = {}
    for axis, dim in sides:
        count, length = (lax.axis_size(axis), shard.shape[dim])
        up = [(i, (i + 1) % count) for i in range(count - 1)]
        last = lax.slice_in_dim(shard, length - width, length, axis=dim)
        first = lax.slice_in_dim(shard, 0, width, axis=dim)
        edges[dim] = (
            lax.ppermute(last, axis, up),
            lax.ppermute(first, axis, [(b, a) for a, b in up]),
        )
    done = []
    for _, dim in sides:
        low, high = edges[dim]
        around = [(width, width) if d in done else (0, 0) for d in range(shard.ndim)]
        shard = jnp.concatenate([jnp.pad(low, around), shard, jnp.pad(high, around)], axis=dim)
        done.append(dim)
    return shard


def over_axes(shard, axes):
    for axis in axes:
        shard = lax.psum(shard, axis)
    return shard


def with_halo(block, sides, width):
    for axis, dim in sides:
        count = lax.axis_size(axis)
        forward = [(i, i + 1) for i in range(count - 1)]
        backward = [(target, source) for source, target in forward]
        low = lax.ppermute(
            lax.slice_in_dim(block, block.shape[dim] - width, None, axis=dim), axis, forward
        )
        high = lax.ppermute(lax.slice_in_dim(block, 0, width, axis=dim), axis, backward)
        block = jnp.concatenate([low, block, high], axis=dim)
    return block


def build_send(bricks, brick_target, brick_slot, peers, capacity):
    target = brick_target[:, 0]
    onehot = (target[:, None] == jnp.arange(peers, dtype=jnp.int32)[None, :]).astype(jnp.int32)
    earlier = jnp.cumsum(onehot, axis=0) - onehot
    order = jnp.sum(earlier * onehot, axis=1)
    place = target * capacity + order
    high = (brick_slot // 32).astype(jnp.bfloat16)
    low = (brick_slot % 32).astype(jnp.bfloat16)
    tag = jnp.zeros((bricks.shape[0], 128), jnp.bfloat16).at[:, 0].set(high).at[:, 1].set(low)
    rows = jnp.concatenate([bricks, tag], axis=1)
    chosen = place[None, :] == jnp.arange(peers * capacity, dtype=jnp.int32)[:, None]
    payload = jnp.einsum(
        "pk,kj->pj", chosen.astype(jnp.bfloat16), rows, preferred_element_type=jnp.float32
    )
    return payload.astype(jnp.bfloat16)


def next_along_z(field):
    edge = jnp.zeros(field.shape[:-1] + (1,), field.dtype)
    return jnp.concatenate([field[..., 1:], edge], axis=-1)


def prior_along_z(field):
    edge = jnp.zeros(field.shape[:-1] + (1,), field.dtype)
    return jnp.concatenate([edge, field[..., :-1]], axis=-1)


def operate(field, screen):
    padded = extended(field, ((GX, 0), (GY, 1)), 1)
    beside = padded[2:, 1:-1] + padded[:-2, 1:-1]
    beside = beside + padded[1:-1, 2:] + padded[1:-1, :-2]
    beside = beside + next_along_z(field) + prior_along_z(field)
    return (6.0 + screen) * field - beside


def component_grid(blocks, comp, span_x, span_y, span_z):
    part_blocks = blocks[:, comp, :].reshape(span_x, span_y, span_z, 8, 8, 8)
    grid = part_blocks.transpose(0, 3, 1, 4, 2, 5)
    return grid.reshape(span_x * 8, span_y * 8, span_z * 8)


def relayout_kernel(blk_ref, out_ref):
    sub = lax.broadcasted_iota(jnp.int32, (8, 128), 0)
    lane = lax.broadcasted_iota(jnp.int32, (8, 128), 1)
    grp = (lane // 8) % 8
    low_half = lane < 64
    swaps = []
    for m in (4, 2, 1):
        first = ((sub & m) == 0) & ((grp & m) != 0)
        second = ((sub & m) != 0) & ((grp & m) == 0)
        swaps.append((m, first, second))

    def transpose_groups(x):
        for m, first, second in swaps:
            a = pltpu.roll(pltpu.roll(x, 8 - m, 0), 8 * m, 1)
            b = pltpu.roll(pltpu.roll(x, m, 0), 128 - 8 * m, 1)
            x = jnp.where(first, a, jnp.where(second, b, x))
        return x

    def step(i, carry):
        ly = i % 8
        lx = i // 8
        row = pl.multiple_of(i * 16, 16)
        y = pl.multiple_of(ly * 8, 8)
        top = blk_ref[pl.ds(row, 8), :]
        bottom = blk_ref[pl.ds(row + 8, 8), :]
        for c in range(3):
            for uh in range(4):
                col = (c * 4 + uh) * 128
                s0 = top[:, col:col + 128]
                s1 = bottom[:, col:col + 128]
                u0 = jnp.where(low_half, s0, pltpu.roll(s1, 64, 1))
                u1 = jnp.where(low_half, pltpu.roll(s0, 64, 1), s1)
                out_ref[c, lx * 8 + uh * 2, pl.ds(y, 8), :] = transpose_groups(u0)
                out_ref[c, lx * 8 + uh * 2 + 1, pl.ds(y, 8), :] = transpose_groups(u1)
        return carry

    lax.fori_loop(0, 32, step, 0)


def to_grid(blocks, span_x, span_y, depth):
    return pl.pallas_call(
        relayout_kernel,
        out_shape=jax.ShapeDtypeStruct((3, span_x * 8, span_y * 8, depth), jnp.float32),
        in_specs=[pl.BlockSpec(memory_space=pltpu.VMEM)],
        out_specs=pl.BlockSpec(memory_space=pltpu.VMEM),
    )(blocks)


def body(bricks, brick_target, brick_slot, screen, coarse_guess):
    peers = lax.axis_size(GX_GY)
    capacity = max(2, 3 * bricks.shape[0] // peers)
    payload = build_send(bricks, brick_target, brick_slot, peers, capacity)
    arrived = lax.all_to_all(
        payload.reshape(peers, capacity, payload.shape[1]), GX_GY, split_axis=0, concat_axis=0, tiled=True
    ).reshape(peers * capacity, payload.shape[1])
    tag = arrived[:, 1536:1538].astype(jnp.int32)
    landed = tag[:, 0] * 32 + tag[:, 1]
    width_x, width_y, depth = screen.shape
    span_x = width_x // 8
    span_y = width_y // 8
    span_z = depth // 8
    picks = landed.reshape(-1, 1) == jnp.arange(span_x * span_y * span_z, dtype=jnp.int32)[None, :]
    blocks = jnp.einsum(
        "ks,kj->sj",
        picks.astype(jnp.bfloat16),
        arrived[:, :1536],
        preferred_element_type=jnp.float32,
    )
    normals = to_grid(blocks, span_x, span_y, depth)
    normal_x, normal_y, normal_z = normals[0], normals[1], normals[2]
    along_x = with_halo(normal_x, ((GX, 0),), 1)
    along_y = with_halo(normal_y, ((GY, 1),), 1)
    total = along_x[2:] - along_x[:-2]
    total = total + (along_y[:, 2:] - along_y[:, :-2])
    total = total + (next_along_z(normal_z) - prior_along_z(normal_z))
    source = -0.5 * total
    inverse = 1.0 / (6.0 + screen)
    residual = source - operate(coarse_guess, screen)
    precond = residual * inverse
    image = operate(precond, screen)
    scaled = image * inverse
    scaled_image = operate(scaled, screen)
    sums = over_axes(
        jnp.stack(
            [
                jnp.sum(residual * precond),
                jnp.sum(precond * image),
                jnp.sum(image * scaled),
                jnp.sum(scaled * scaled_image),
            ]
        ),
        GX_GY,
    )
    gamma, delta, energy, curvature = sums[0], sums[1], sums[2], sums[3]
    alpha = gamma / delta
    gamma_next = alpha * alpha * energy - gamma
    ratio = gamma_next / gamma
    grow = 1.0 + ratio
    delta_next = grow * grow * delta - 2.0 * grow * alpha * energy + alpha * alpha * curvature
    alpha_next = gamma_next / delta_next
    solution = coarse_guess + alpha * precond
    residual = residual - alpha * image
    direction = residual * inverse + ratio * precond
    along = image - alpha * scaled_image + ratio * image
    solution = solution + alpha_next * direction
    residual = residual - alpha_next * along
    return (solution, residual)


def solution(mesh):
    split = Mesh(mesh.devices.reshape(4, 2, 4, 4), ("gx_0", "gx_1", "gy_0", "gy_1"))
    placed = (P(GX_GY, None), P(GX_GY, None), P(GX_GY), P(GX, GY, None), P(GX, GY, None))
    return jax.shard_map(
        body,
        mesh=split,
        in_specs=placed,
        out_specs=(P(GX, GY, None), P(GX, GY, None)),
        check_vma=False,
    )
```

```python
import jax
import jax.numpy as jnp
from jax import lax
from jax.sharding import Mesh
from jax.sharding import PartitionSpec as P
from jax.experimental import pallas as pl
from jax.experimental.pallas import tpu as pltpu

GX_GY = ("gx_0", "gx_1", "gy_0", "gy_1")
GX = ("gx_0", "gx_1")
GY = ("gy_0", "gy_1")


def extended(shard, sides, width):
    edges = {}
    for axis, dim in sides:
        count, length = (lax.axis_size(axis), shard.shape[dim])
        up = [(i, (i + 1) % count) for i in range(count - 1)]
        last = lax.slice_in_dim(shard, length - width, length, axis=dim)
        first = lax.slice_in_dim(shard, 0, width, axis=dim)
        edges[dim] = (
            lax.ppermute(last, axis, up),
            lax.ppermute(first, axis, [(b, a) for a, b in up]),
        )
    done = []
    for _, dim in sides:
        low, high = edges[dim]
        around = [(width, width) if d in done else (0, 0) for d in range(shard.ndim)]
        shard = jnp.concatenate([jnp.pad(low, around), shard, jnp.pad(high, around)], axis=dim)
        done.append(dim)
    return shard


def over_axes(shard, axes):
    for axis in axes:
        shard = lax.psum(shard, axis)
    return shard


def with_halo(block, sides, width):
    for axis, dim in sides:
        count = lax.axis_size(axis)
        forward = [(i, i + 1) for i in range(count - 1)]
        backward = [(target, source) for source, target in forward]
        low = lax.ppermute(
            lax.slice_in_dim(block, block.shape[dim] - width, None, axis=dim), axis, forward
        )
        high = lax.ppermute(lax.slice_in_dim(block, 0, width, axis=dim), axis, backward)
        block = jnp.concatenate([low, block, high], axis=dim)
    return block


def build_send(bricks, brick_target, brick_slot, peers, capacity):
    target = brick_target[:, 0]
    onehot = (target[:, None] == jnp.arange(peers, dtype=jnp.int32)[None, :]).astype(jnp.int32)
    earlier = jnp.cumsum(onehot, axis=0) - onehot
    order = jnp.sum(earlier * onehot, axis=1)
    place = target * capacity + order
    high = (brick_slot // 32).astype(jnp.bfloat16)
    low = (brick_slot % 32).astype(jnp.bfloat16)
    tag = jnp.zeros((bricks.shape[0], 128), jnp.bfloat16).at[:, 0].set(high).at[:, 1].set(low)
    rows = jnp.concatenate([bricks, tag], axis=1)
    chosen = place[None, :] == jnp.arange(peers * capacity, dtype=jnp.int32)[:, None]
    payload = jnp.einsum(
        "pk,kj->pj", chosen.astype(jnp.bfloat16), rows, preferred_element_type=jnp.float32
    )
    return payload.astype(jnp.bfloat16)


def next_along_z(field):
    edge = jnp.zeros(field.shape[:-1] + (1,), field.dtype)
    return jnp.concatenate([field[..., 1:], edge], axis=-1)


def prior_along_z(field):
    edge = jnp.zeros(field.shape[:-1] + (1,), field.dtype)
    return jnp.concatenate([edge, field[..., :-1]], axis=-1)


def operate(field, screen):
    padded = extended(field, ((GX, 0), (GY, 1)), 1)
    beside = padded[2:, 1:-1] + padded[:-2, 1:-1]
    beside = beside + padded[1:-1, 2:] + padded[1:-1, :-2]
    beside = beside + next_along_z(field) + prior_along_z(field)
    return (6.0 + screen) * field - beside


def component_grid(blocks, comp, span_x, span_y, span_z):
    part_blocks = blocks[:, comp, :].reshape(span_x, span_y, span_z, 8, 8, 8)
    grid = part_blocks.transpose(0, 3, 1, 4, 2, 5)
    return grid.reshape(span_x * 8, span_y * 8, span_z * 8)


def relayout_kernel(blk_ref, out_ref):
    sub = lax.broadcasted_iota(jnp.int32, (8, 128), 0)
    lane = lax.broadcasted_iota(jnp.int32, (8, 128), 1)
    grp = (lane // 8) % 8
    low_half = lane < 64
    swaps = []
    for m in (4, 2, 1):
        first = ((sub & m) == 0) & ((grp & m) != 0)
        second = ((sub & m) != 0) & ((grp & m) == 0)
        swaps.append((m, first, second))

    def transpose_groups(x):
        for m, first, second in swaps:
            a = pltpu.roll(pltpu.roll(x, 8 - m, 0), 8 * m, 1)
            b = pltpu.roll(pltpu.roll(x, m, 0), 128 - 8 * m, 1)
            x = jnp.where(first, a, jnp.where(second, b, x))
        return x

    def step(i, carry):
        ly = i % 8
        lx = i // 8
        row = pl.multiple_of(i * 16, 16)
        y = pl.multiple_of(ly * 8, 8)
        top = blk_ref[pl.ds(row, 8), :]
        bottom = blk_ref[pl.ds(row + 8, 8), :]
        for c in range(3):
            for uh in range(4):
                col = (c * 4 + uh) * 128
                s0 = top[:, col:col + 128]
                s1 = bottom[:, col:col + 128]
                u0 = jnp.where(low_half, s0, pltpu.roll(s1, 64, 1))
                u1 = jnp.where(low_half, pltpu.roll(s0, 64, 1), s1)
                out_ref[c, lx * 8 + uh * 2, pl.ds(y, 8), :] = transpose_groups(u0)
                out_ref[c, lx * 8 + uh * 2 + 1, pl.ds(y, 8), :] = transpose_groups(u1)
        return carry

    lax.fori_loop(0, 32, step, 0)


def to_grid(blocks, span_x, span_y, depth):
    return pl.pallas_call(
        relayout_kernel,
        out_shape=jax.ShapeDtypeStruct((3, span_x * 8, span_y * 8, depth), jnp.float32),
        in_specs=[pl.BlockSpec(memory_space=pltpu.VMEM)],
        out_specs=pl.BlockSpec(memory_space=pltpu.VMEM),
    )(blocks)


def body(bricks, brick_target, brick_slot, screen, coarse_guess):
    peers = lax.axis_size(GX_GY)
    capacity = max(2, 3 * bricks.shape[0] // peers)
    payload = build_send(bricks, brick_target, brick_slot, peers, capacity)
    arrived = lax.all_to_all(
        payload.reshape(peers, capacity, payload.shape[1]), GX_GY, split_axis=0, concat_axis=0, tiled=True
    ).reshape(peers * capacity, payload.shape[1])
    tag = arrived[:, 1536:1538].astype(jnp.int32)
    landed = tag[:, 0] * 32 + tag[:, 1]
    width_x, width_y, depth = screen.shape
    span_x = width_x // 8
    span_y = width_y // 8
    span_z = depth // 8
    picks = landed.reshape(-1, 1) == jnp.arange(span_x * span_y * span_z, dtype=jnp.int32)[None, :]
    blocks = jnp.einsum(
        "ks,kj->sj",
        picks.astype(jnp.bfloat16),
        arrived[:, :1536],
        preferred_element_type=jnp.float32,
    )
    normals = to_grid(blocks, span_x, span_y, depth)
    normal_x, normal_y, normal_z = normals[0], normals[1], normals[2]
    along_x = with_halo(normal_x, ((GX, 0),), 1)
    along_y = with_halo(normal_y, ((GY, 1),), 1)
    total = along_x[2:] - along_x[:-2]
    total = total + (along_y[:, 2:] - along_y[:, :-2])
    total = total + (next_along_z(normal_z) - prior_along_z(normal_z))
    source = -0.5 * total
    inverse = 1.0 / (6.0 + screen)
    residual = source - operate(coarse_guess, screen)
    precond = residual * inverse
    image = operate(precond, screen)
    scaled = image * inverse
    scaled_image = operate(scaled, screen)
    sums = over_axes(
        jnp.stack(
            [
                jnp.sum(residual * precond),
                jnp.sum(precond * image),
                jnp.sum(image * scaled),
                jnp.sum(scaled * scaled_image),
            ]
        ),
        (GX, GY),
    )
    gamma, delta, energy, curvature = sums[0], sums[1], sums[2], sums[3]
    alpha = gamma / delta
    gamma_next = alpha * alpha * energy - gamma
    ratio = gamma_next / gamma
    grow = 1.0 + ratio
    delta_next = grow * grow * delta - 2.0 * grow * alpha * energy + alpha * alpha * curvature
    alpha_next = gamma_next / delta_next
    solution = coarse_guess + alpha * precond
    residual = residual - alpha * image
    direction = residual * inverse + ratio * precond
    along = image - alpha * scaled_image + ratio * image
    solution = solution + alpha_next * direction
    residual = residual - alpha_next * along
    return (solution, residual)


def solution(mesh):
    split = Mesh(mesh.devices.reshape(4, 2, 4, 4), ("gx_0", "gx_1", "gy_0", "gy_1"))
    placed = (P(GX_GY, None), P(GX_GY, None), P(GX_GY), P(GX, GY, None), P(GX, GY, None))
    return jax.shard_map(
        body,
        mesh=split,
        in_specs=placed,
        out_specs=(P(GX, GY, None), P(GX, GY, None)),
        check_vma=False,
    )
```

```python
import jax
import jax.numpy as jnp
from jax import lax
from jax.sharding import Mesh
from jax.sharding import PartitionSpec as P
from jax.experimental import pallas as pl
from jax.experimental.pallas import tpu as pltpu

GX = ("y_hi", "y_lo", "core")
GY = ("x_hi", "x_lo", "z_hi", "z_lo")
GX_GY = GX + GY
PAIRS = ("core", "y_lo", "y_hi", "z_lo", "z_hi", "x_lo", "x_hi")


def extended(shard, sides, width):
    edges = {}
    for axis, dim in sides:
        count, length = (lax.axis_size(axis), shard.shape[dim])
        up = [(i, (i + 1) % count) for i in range(count - 1)]
        last = lax.slice_in_dim(shard, length - width, length, axis=dim)
        first = lax.slice_in_dim(shard, 0, width, axis=dim)
        edges[dim] = (
            lax.ppermute(last, axis, up),
            lax.ppermute(first, axis, [(b, a) for a, b in up]),
        )
    done = []
    for _, dim in sides:
        low, high = edges[dim]
        around = [(width, width) if d in done else (0, 0) for d in range(shard.ndim)]
        shard = jnp.concatenate([jnp.pad(low, around), shard, jnp.pad(high, around)], axis=dim)
        done.append(dim)
    return shard


def over_axes(shard, axes):
    for axis in axes:
        shard = lax.psum(shard, axis)
    return shard


def with_halo(block, sides, width):
    for axis, dim in sides:
        count = lax.axis_size(axis)
        forward = [(i, i + 1) for i in range(count - 1)]
        backward = [(target, source) for source, target in forward]
        low = lax.ppermute(
            lax.slice_in_dim(block, block.shape[dim] - width, None, axis=dim), axis, forward
        )
        high = lax.ppermute(lax.slice_in_dim(block, 0, width, axis=dim), axis, backward)
        block = jnp.concatenate([low, block, high], axis=dim)
    return block


def build_send(bricks, brick_target, brick_slot, peers, capacity):
    target = brick_target[:, 0]
    onehot = (target[:, None] == jnp.arange(peers, dtype=jnp.int32)[None, :]).astype(jnp.int32)
    earlier = jnp.cumsum(onehot, axis=0) - onehot
    order = jnp.sum(earlier * onehot, axis=1)
    place = target * capacity + order
    high = (brick_slot // 32).astype(jnp.bfloat16)
    low = (brick_slot % 32).astype(jnp.bfloat16)
    tag = jnp.zeros((bricks.shape[0], 128), jnp.bfloat16).at[:, 0].set(high).at[:, 1].set(low)
    rows = jnp.concatenate([bricks, tag], axis=1)
    chosen = place[None, :] == jnp.arange(peers * capacity, dtype=jnp.int32)[:, None]
    payload = jnp.einsum(
        "pk,kj->pj", chosen.astype(jnp.bfloat16), rows, preferred_element_type=jnp.float32
    )
    return payload.astype(jnp.bfloat16)


def next_along_z(field):
    edge = jnp.zeros(field.shape[:-1] + (1,), field.dtype)
    return jnp.concatenate([field[..., 1:], edge], axis=-1)


def prior_along_z(field):
    edge = jnp.zeros(field.shape[:-1] + (1,), field.dtype)
    return jnp.concatenate([edge, field[..., :-1]], axis=-1)


def operate(field, screen):
    padded = extended(field, ((GX, 0), (GY, 1)), 1)
    beside = padded[2:, 1:-1] + padded[:-2, 1:-1]
    beside = beside + padded[1:-1, 2:] + padded[1:-1, :-2]
    beside = beside + next_along_z(field) + prior_along_z(field)
    return (6.0 + screen) * field - beside


def component_grid(blocks, comp, span_x, span_y, span_z):
    part_blocks = blocks[:, comp, :].reshape(span_x, span_y, span_z, 8, 8, 8)
    grid = part_blocks.transpose(0, 3, 1, 4, 2, 5)
    return grid.reshape(span_x * 8, span_y * 8, span_z * 8)


def relayout_kernel(blk_ref, out_ref):
    sub = lax.broadcasted_iota(jnp.int32, (8, 128), 0)
    lane = lax.broadcasted_iota(jnp.int32, (8, 128), 1)
    grp = (lane // 8) % 8
    low_half = lane < 64
    swaps = []
    for m in (4, 2, 1):
        first = ((sub & m) == 0) & ((grp & m) != 0)
        second = ((sub & m) != 0) & ((grp & m) == 0)
        swaps.append((m, first, second))

    def transpose_groups(x):
        for m, first, second in swaps:
            a = pltpu.roll(pltpu.roll(x, 8 - m, 0), 8 * m, 1)
            b = pltpu.roll(pltpu.roll(x, m, 0), 128 - 8 * m, 1)
            x = jnp.where(first, a, jnp.where(second, b, x))
        return x

    def step(i, carry):
        ly = i % 8
        lx = i // 8
        row = pl.multiple_of(i * 16, 16)
        y = pl.multiple_of(ly * 8, 8)
        top = blk_ref[pl.ds(row, 8), :]
        bottom = blk_ref[pl.ds(row + 8, 8), :]
        for c in range(3):
            for uh in range(4):
                col = (c * 4 + uh) * 128
                s0 = top[:, col:col + 128]
                s1 = bottom[:, col:col + 128]
                u0 = jnp.where(low_half, s0, pltpu.roll(s1, 64, 1))
                u1 = jnp.where(low_half, pltpu.roll(s0, 64, 1), s1)
                out_ref[c, lx * 8 + uh * 2, pl.ds(y, 8), :] = transpose_groups(u0)
                out_ref[c, lx * 8 + uh * 2 + 1, pl.ds(y, 8), :] = transpose_groups(u1)
        return carry

    lax.fori_loop(0, 32, step, 0)


def to_grid(blocks, span_x, span_y, depth):
    return pl.pallas_call(
        relayout_kernel,
        out_shape=jax.ShapeDtypeStruct((3, span_x * 8, span_y * 8, depth), jnp.float32),
        in_specs=[pl.BlockSpec(memory_space=pltpu.VMEM)],
        out_specs=pl.BlockSpec(memory_space=pltpu.VMEM),
    )(blocks)


def body(bricks, brick_target, brick_slot, screen, coarse_guess):
    peers = lax.axis_size(GX_GY)
    capacity = max(2, 3 * bricks.shape[0] // peers)
    payload = build_send(bricks, brick_target, brick_slot, peers, capacity)
    arrived = lax.all_to_all(
        payload.reshape(peers, capacity, payload.shape[1]), GX_GY, split_axis=0, concat_axis=0, tiled=True
    ).reshape(peers * capacity, payload.shape[1])
    tag = arrived[:, 1536:1538].astype(jnp.int32)
    landed = tag[:, 0] * 32 + tag[:, 1]
    width_x, width_y, depth = screen.shape
    span_x = width_x // 8
    span_y = width_y // 8
    span_z = depth // 8
    picks = landed.reshape(-1, 1) == jnp.arange(span_x * span_y * span_z, dtype=jnp.int32)[None, :]
    blocks = jnp.einsum(
        "ks,kj->sj",
        picks.astype(jnp.bfloat16),
        arrived[:, :1536],
        preferred_element_type=jnp.float32,
    )
    normals = to_grid(blocks, span_x, span_y, depth)
    normal_x, normal_y, normal_z = normals[0], normals[1], normals[2]
    along_x = with_halo(normal_x, ((GX, 0),), 1)
    along_y = with_halo(normal_y, ((GY, 1),), 1)
    total = along_x[2:] - along_x[:-2]
    total = total + (along_y[:, 2:] - along_y[:, :-2])
    total = total + (next_along_z(normal_z) - prior_along_z(normal_z))
    source = -0.5 * total
    inverse = 1.0 / (6.0 + screen)
    residual = source - operate(coarse_guess, screen)
    precond = residual * inverse
    image = operate(precond, screen)
    scaled = image * inverse
    scaled_image = operate(scaled, screen)
    sums = over_axes(
        jnp.stack(
            [
                jnp.sum(residual * precond),
                jnp.sum(precond * image),
                jnp.sum(image * scaled),
                jnp.sum(scaled * scaled_image),
            ]
        ),
        PAIRS,
    )
    gamma, delta, energy, curvature = sums[0], sums[1], sums[2], sums[3]
    alpha = gamma / delta
    gamma_next = alpha * alpha * energy - gamma
    ratio = gamma_next / gamma
    grow = 1.0 + ratio
    delta_next = grow * grow * delta - 2.0 * grow * alpha * energy + alpha * alpha * curvature
    alpha_next = gamma_next / delta_next
    solution = coarse_guess + alpha * precond
    residual = residual - alpha * image
    direction = residual * inverse + ratio * precond
    along = image - alpha * scaled_image + ratio * image
    solution = solution + alpha_next * direction
    residual = residual - alpha_next * along
    return (solution, residual)


def solution(mesh):
    split = Mesh(mesh.devices.reshape((2,) * 7), GX_GY)
    placed = (P(GX_GY, None), P(GX_GY, None), P(GX_GY), P(GX, GY, None), P(GX, GY, None))
    return jax.shard_map(
        body,
        mesh=split,
        in_specs=placed,
        out_specs=(P(GX, GY, None), P(GX, GY, None)),
        check_vma=False,
    )
```

```python
import jax
import jax.numpy as jnp
from jax import lax
from jax.sharding import Mesh
from jax.sharding import PartitionSpec as P
from jax.experimental import pallas as pl
from jax.experimental.pallas import tpu as pltpu

GX_GY = ("gx_0", "gx_1", "gy_0", "gy_1")
GX = ("gx_0", "gx_1")
GY = ("gy_0", "gy_1")


def shifted(piece, axis, pairs, dim):
    if dim == 1:
        flat = piece.reshape(piece.shape[0], piece.shape[2])
        return lax.ppermute(flat, axis, pairs).reshape(piece.shape)
    return lax.ppermute(piece, axis, pairs)


def extended(shard, sides, width):
    edges = {}
    for axis, dim in sides:
        count, length = (lax.axis_size(axis), shard.shape[dim])
        up = [(i, (i + 1) % count) for i in range(count - 1)]
        last = lax.slice_in_dim(shard, length - width, length, axis=dim)
        first = lax.slice_in_dim(shard, 0, width, axis=dim)
        edges[dim] = (
            shifted(last, axis, up, dim),
            shifted(first, axis, [(b, a) for a, b in up], dim),
        )
    done = []
    for _, dim in sides:
        low, high = edges[dim]
        around = [(width, width) if d in done else (0, 0) for d in range(shard.ndim)]
        shard = jnp.concatenate([jnp.pad(low, around), shard, jnp.pad(high, around)], axis=dim)
        done.append(dim)
    return shard


def over_axes(shard, axes):
    for axis in axes:
        shard = lax.psum(shard, axis)
    return shard


def with_halo(block, sides, width):
    for axis, dim in sides:
        count = lax.axis_size(axis)
        forward = [(i, i + 1) for i in range(count - 1)]
        backward = [(target, source) for source, target in forward]
        low = shifted(
            lax.slice_in_dim(block, block.shape[dim] - width, None, axis=dim), axis, forward, dim
        )
        high = shifted(lax.slice_in_dim(block, 0, width, axis=dim), axis, backward, dim)
        block = jnp.concatenate([low, block, high], axis=dim)
    return block


def build_send(bricks, brick_target, brick_slot, peers, capacity):
    target = brick_target[:, 0]
    onehot = (target[:, None] == jnp.arange(peers, dtype=jnp.int32)[None, :]).astype(jnp.int32)
    earlier = jnp.cumsum(onehot, axis=0) - onehot
    order = jnp.sum(earlier * onehot, axis=1)
    place = target * capacity + order
    high = (brick_slot // 32).astype(jnp.bfloat16)
    low = (brick_slot % 32).astype(jnp.bfloat16)
    tag = jnp.zeros((bricks.shape[0], 128), jnp.bfloat16).at[:, 0].set(high).at[:, 1].set(low)
    rows = jnp.concatenate([bricks, tag], axis=1)
    chosen = place[None, :] == jnp.arange(peers * capacity, dtype=jnp.int32)[:, None]
    payload = jnp.einsum(
        "pk,kj->pj", chosen.astype(jnp.bfloat16), rows, preferred_element_type=jnp.float32
    )
    return payload.astype(jnp.bfloat16)


def next_along_z(field):
    edge = jnp.zeros(field.shape[:-1] + (1,), field.dtype)
    return jnp.concatenate([field[..., 1:], edge], axis=-1)


def prior_along_z(field):
    edge = jnp.zeros(field.shape[:-1] + (1,), field.dtype)
    return jnp.concatenate([edge, field[..., :-1]], axis=-1)


def operate(field, screen):
    padded = extended(field, ((GX, 0), (GY, 1)), 1)
    beside = padded[2:, 1:-1] + padded[:-2, 1:-1]
    beside = beside + padded[1:-1, 2:] + padded[1:-1, :-2]
    beside = beside + next_along_z(field) + prior_along_z(field)
    return (6.0 + screen) * field - beside


def component_grid(blocks, comp, span_x, span_y, span_z):
    part_blocks = blocks[:, comp, :].reshape(span_x, span_y, span_z, 8, 8, 8)
    grid = part_blocks.transpose(0, 3, 1, 4, 2, 5)
    return grid.reshape(span_x * 8, span_y * 8, span_z * 8)


def relayout_kernel(blk_ref, out_ref):
    sub = lax.broadcasted_iota(jnp.int32, (8, 128), 0)
    lane = lax.broadcasted_iota(jnp.int32, (8, 128), 1)
    grp = (lane // 8) % 8
    low_half = lane < 64
    swaps = []
    for m in (4, 2, 1):
        first = ((sub & m) == 0) & ((grp & m) != 0)
        second = ((sub & m) != 0) & ((grp & m) == 0)
        swaps.append((m, first, second))

    def transpose_groups(x):
        for m, first, second in swaps:
            a = pltpu.roll(pltpu.roll(x, 8 - m, 0), 8 * m, 1)
            b = pltpu.roll(pltpu.roll(x, m, 0), 128 - 8 * m, 1)
            x = jnp.where(first, a, jnp.where(second, b, x))
        return x

    def step(i, carry):
        ly = i % 8
        lx = i // 8
        row = pl.multiple_of(i * 16, 16)
        y = pl.multiple_of(ly * 8, 8)
        top = blk_ref[pl.ds(row, 8), :]
        bottom = blk_ref[pl.ds(row + 8, 8), :]
        for c in range(3):
            for uh in range(4):
                col = (c * 4 + uh) * 128
                s0 = top[:, col:col + 128]
                s1 = bottom[:, col:col + 128]
                u0 = jnp.where(low_half, s0, pltpu.roll(s1, 64, 1))
                u1 = jnp.where(low_half, pltpu.roll(s0, 64, 1), s1)
                out_ref[c, lx * 8 + uh * 2, pl.ds(y, 8), :] = transpose_groups(u0)
                out_ref[c, lx * 8 + uh * 2 + 1, pl.ds(y, 8), :] = transpose_groups(u1)
        return carry

    lax.fori_loop(0, 32, step, 0)


def to_grid(blocks, span_x, span_y, depth):
    return pl.pallas_call(
        relayout_kernel,
        out_shape=jax.ShapeDtypeStruct((3, span_x * 8, span_y * 8, depth), jnp.float32),
        in_specs=[pl.BlockSpec(memory_space=pltpu.VMEM)],
        out_specs=pl.BlockSpec(memory_space=pltpu.VMEM),
    )(blocks)


def body(bricks, brick_target, brick_slot, screen, coarse_guess):
    peers = lax.axis_size(GX_GY)
    capacity = max(2, 3 * bricks.shape[0] // peers)
    payload = build_send(bricks, brick_target, brick_slot, peers, capacity)
    arrived = lax.all_to_all(
        payload.reshape(peers, capacity, payload.shape[1]), GX_GY, split_axis=0, concat_axis=0, tiled=True
    ).reshape(peers * capacity, payload.shape[1])
    tag = arrived[:, 1536:1538].astype(jnp.int32)
    landed = tag[:, 0] * 32 + tag[:, 1]
    width_x, width_y, depth = screen.shape
    span_x = width_x // 8
    span_y = width_y // 8
    span_z = depth // 8
    picks = landed.reshape(-1, 1) == jnp.arange(span_x * span_y * span_z, dtype=jnp.int32)[None, :]
    blocks = jnp.einsum(
        "ks,kj->sj",
        picks.astype(jnp.bfloat16),
        arrived[:, :1536],
        preferred_element_type=jnp.float32,
    )
    normals = to_grid(blocks, span_x, span_y, depth)
    normal_x, normal_y, normal_z = normals[0], normals[1], normals[2]
    along_x = with_halo(normal_x, ((GX, 0),), 1)
    along_y = with_halo(normal_y, ((GY, 1),), 1)
    total = along_x[2:] - along_x[:-2]
    total = total + (along_y[:, 2:] - along_y[:, :-2])
    total = total + (next_along_z(normal_z) - prior_along_z(normal_z))
    source = -0.5 * total
    inverse = 1.0 / (6.0 + screen)
    residual = source - operate(coarse_guess, screen)
    precond = residual * inverse
    image = operate(precond, screen)
    scaled = image * inverse
    scaled_image = operate(scaled, screen)
    sums = over_axes(
        jnp.stack(
            [
                jnp.sum(residual * precond),
                jnp.sum(precond * image),
                jnp.sum(image * scaled),
                jnp.sum(scaled * scaled_image),
            ]
        ),
        GX_GY,
    )
    gamma, delta, energy, curvature = sums[0], sums[1], sums[2], sums[3]
    alpha = gamma / delta
    gamma_next = alpha * alpha * energy - gamma
    ratio = gamma_next / gamma
    grow = 1.0 + ratio
    delta_next = grow * grow * delta - 2.0 * grow * alpha * energy + alpha * alpha * curvature
    alpha_next = gamma_next / delta_next
    solution = coarse_guess + alpha * precond
    residual = residual - alpha * image
    direction = residual * inverse + ratio * precond
    along = image - alpha * scaled_image + ratio * image
    solution = solution + alpha_next * direction
    residual = residual - alpha_next * along
    return (solution, residual)


def solution(mesh):
    split = Mesh(mesh.devices.reshape(4, 2, 4, 4), ("gx_0", "gx_1", "gy_0", "gy_1"))
    placed = (P(GX_GY, None), P(GX_GY, None), P(GX_GY), P(GX, GY, None), P(GX, GY, None))
    return jax.shard_map(
        body,
        mesh=split,
        in_specs=placed,
        out_specs=(P(GX, GY, None), P(GX, GY, None)),
        check_vma=False,
    )
```

```python
import jax
import jax.numpy as jnp
from jax import lax
from jax.sharding import Mesh
from jax.sharding import PartitionSpec as P
from jax.experimental import pallas as pl
from jax.experimental.pallas import tpu as pltpu

GX_GY = ("gx_0", "gx_1", "gy_0", "gy_1")
GX = ("gx_0", "gx_1")
GY = ("gy_0", "gy_1")


def shifted(piece, axis, pairs, dim):
    if dim == 1:
        flat = piece.reshape(piece.shape[0], piece.shape[2])
        return lax.ppermute(flat, axis, pairs).reshape(piece.shape)
    return lax.ppermute(piece, axis, pairs)


def extended(shard, sides, width):
    edges = {}
    for axis, dim in sides:
        count, length = (lax.axis_size(axis), shard.shape[dim])
        up = [(i, (i + 1) % count) for i in range(count - 1)]
        last = lax.slice_in_dim(shard, length - width, length, axis=dim)
        first = lax.slice_in_dim(shard, 0, width, axis=dim)
        edges[dim] = (
            shifted(last, axis, up, dim),
            shifted(first, axis, [(b, a) for a, b in up], dim),
        )
    done = []
    for _, dim in sides:
        low, high = edges[dim]
        around = [(width, width) if d in done else (0, 0) for d in range(shard.ndim)]
        shard = jnp.concatenate([jnp.pad(low, around), shard, jnp.pad(high, around)], axis=dim)
        done.append(dim)
    return shard


def over_axes(shard, axes):
    for axis in axes:
        shard = lax.psum(shard, axis)
    return shard


def with_halo(block, sides, width):
    for axis, dim in sides:
        count = lax.axis_size(axis)
        forward = [(i, i + 1) for i in range(count - 1)]
        backward = [(target, source) for source, target in forward]
        low = shifted(
            lax.slice_in_dim(block, block.shape[dim] - width, None, axis=dim), axis, forward, dim
        )
        high = shifted(lax.slice_in_dim(block, 0, width, axis=dim), axis, backward, dim)
        block = jnp.concatenate([low, block, high], axis=dim)
    return block


def build_send(bricks, brick_target, brick_slot, peers, capacity):
    target = brick_target[:, 0]
    onehot = (target[:, None] == jnp.arange(peers, dtype=jnp.int32)[None, :]).astype(jnp.int32)
    earlier = jnp.cumsum(onehot, axis=0) - onehot
    order = jnp.sum(earlier * onehot, axis=1)
    place = target * capacity + order
    high = (brick_slot // 32).astype(jnp.bfloat16)
    low = (brick_slot % 32).astype(jnp.bfloat16)
    tag = jnp.zeros((bricks.shape[0], 128), jnp.bfloat16).at[:, 0].set(high).at[:, 1].set(low)
    rows = jnp.concatenate([bricks, tag], axis=1)
    chosen = place[None, :] == jnp.arange(peers * capacity, dtype=jnp.int32)[:, None]
    payload = jnp.einsum(
        "pk,kj->pj", chosen.astype(jnp.bfloat16), rows, preferred_element_type=jnp.float32
    )
    return payload.astype(jnp.bfloat16)


def next_along_z(field):
    edge = jnp.zeros(field.shape[:-1] + (1,), field.dtype)
    return jnp.concatenate([field[..., 1:], edge], axis=-1)


def prior_along_z(field):
    edge = jnp.zeros(field.shape[:-1] + (1,), field.dtype)
    return jnp.concatenate([edge, field[..., :-1]], axis=-1)


def operate(field, screen):
    padded = extended(field, ((GX, 0), (GY, 1)), 1)
    beside = padded[2:, 1:-1] + padded[:-2, 1:-1]
    beside = beside + padded[1:-1, 2:] + padded[1:-1, :-2]
    beside = beside + next_along_z(field) + prior_along_z(field)
    return (6.0 + screen) * field - beside


def component_grid(blocks, comp, span_x, span_y, span_z):
    part_blocks = blocks[:, comp, :].reshape(span_x, span_y, span_z, 8, 8, 8)
    grid = part_blocks.transpose(0, 3, 1, 4, 2, 5)
    return grid.reshape(span_x * 8, span_y * 8, span_z * 8)


def relayout_kernel(blk_ref, out_ref):
    sub = lax.broadcasted_iota(jnp.int32, (8, 128), 0)
    lane = lax.broadcasted_iota(jnp.int32, (8, 128), 1)
    grp = (lane // 8) % 8
    low_half = lane < 64
    swaps = []
    for m in (4, 2, 1):
        first = ((sub & m) == 0) & ((grp & m) != 0)
        second = ((sub & m) != 0) & ((grp & m) == 0)
        swaps.append((m, first, second))

    def transpose_groups(x):
        for m, first, second in swaps:
            a = pltpu.roll(pltpu.roll(x, 8 - m, 0), 8 * m, 1)
            b = pltpu.roll(pltpu.roll(x, m, 0), 128 - 8 * m, 1)
            x = jnp.where(first, a, jnp.where(second, b, x))
        return x

    def step(i, carry):
        ly = i % 8
        lx = i // 8
        row = pl.multiple_of(i * 16, 16)
        y = pl.multiple_of(ly * 8, 8)
        top = blk_ref[pl.ds(row, 8), :]
        bottom = blk_ref[pl.ds(row + 8, 8), :]
        for c in range(3):
            for uh in range(4):
                col = (c * 4 + uh) * 128
                s0 = top[:, col:col + 128]
                s1 = bottom[:, col:col + 128]
                u0 = jnp.where(low_half, s0, pltpu.roll(s1, 64, 1))
                u1 = jnp.where(low_half, pltpu.roll(s0, 64, 1), s1)
                out_ref[c, lx * 8 + uh * 2, pl.ds(y, 8), :] = transpose_groups(u0)
                out_ref[c, lx * 8 + uh * 2 + 1, pl.ds(y, 8), :] = transpose_groups(u1)
        return carry

    lax.fori_loop(0, 32, step, 0)


def to_grid(blocks, span_x, span_y, depth):
    return pl.pallas_call(
        relayout_kernel,
        out_shape=jax.ShapeDtypeStruct((3, span_x * 8, span_y * 8, depth), jnp.float32),
        in_specs=[pl.BlockSpec(memory_space=pltpu.VMEM)],
        out_specs=pl.BlockSpec(memory_space=pltpu.VMEM),
    )(blocks)


def body(bricks, brick_target, brick_slot, screen, coarse_guess):
    peers = lax.axis_size(GX_GY)
    capacity = max(2, 3 * bricks.shape[0] // peers)
    payload = build_send(bricks, brick_target, brick_slot, peers, capacity)
    row = payload.shape[1]
    arrived = lax.all_to_all(
        payload.reshape(peers, capacity * row), GX_GY, split_axis=0, concat_axis=0, tiled=True
    )
    width_x, width_y, depth = screen.shape
    span_x = width_x // 8
    span_y = width_y // 8
    span_z = depth // 8
    cells = jnp.arange(span_x * span_y * span_z, dtype=jnp.int32)[None, :]
    blocks = None
    for slot in range(capacity):
        part = arrived[:, slot * row:(slot + 1) * row]
        tag = part[:, 1536:1538].astype(jnp.int32)
        landed = tag[:, 0] * 32 + tag[:, 1]
        picks = (landed[:, None] == cells).astype(jnp.bfloat16)
        term = jnp.einsum(
            "ks,kj->sj", picks, part[:, :1536], preferred_element_type=jnp.float32
        )
        blocks = term if blocks is None else blocks + term
    normals = to_grid(blocks, span_x, span_y, depth)
    normal_x, normal_y, normal_z = normals[0], normals[1], normals[2]
    along_x = with_halo(normal_x, ((GX, 0),), 1)
    along_y = with_halo(normal_y, ((GY, 1),), 1)
    total = along_x[2:] - along_x[:-2]
    total = total + (along_y[:, 2:] - along_y[:, :-2])
    total = total + (next_along_z(normal_z) - prior_along_z(normal_z))
    source = -0.5 * total
    inverse = 1.0 / (6.0 + screen)
    residual = source - operate(coarse_guess, screen)
    precond = residual * inverse
    image = operate(precond, screen)
    scaled = image * inverse
    scaled_image = operate(scaled, screen)
    sums = over_axes(
        jnp.stack(
            [
                jnp.sum(residual * precond),
                jnp.sum(precond * image),
                jnp.sum(image * scaled),
                jnp.sum(scaled * scaled_image),
            ]
        ),
        GX_GY,
    )
    gamma, delta, energy, curvature = sums[0], sums[1], sums[2], sums[3]
    alpha = gamma / delta
    gamma_next = alpha * alpha * energy - gamma
    ratio = gamma_next / gamma
    grow = 1.0 + ratio
    delta_next = grow * grow * delta - 2.0 * grow * alpha * energy + alpha * alpha * curvature
    alpha_next = gamma_next / delta_next
    solution = coarse_guess + alpha * precond
    residual = residual - alpha * image
    direction = residual * inverse + ratio * precond
    along = image - alpha * scaled_image + ratio * image
    solution = solution + alpha_next * direction
    residual = residual - alpha_next * along
    return (solution, residual)


def solution(mesh):
    split = Mesh(mesh.devices.reshape(4, 2, 4, 4), ("gx_0", "gx_1", "gy_0", "gy_1"))
    placed = (P(GX_GY, None), P(GX_GY, None), P(GX_GY), P(GX, GY, None), P(GX, GY, None))
    return jax.shard_map(
        body,
        mesh=split,
        in_specs=placed,
        out_specs=(P(GX, GY, None), P(GX, GY, None)),
        check_vma=False,
    )
```

```python
import jax
import jax.numpy as jnp
from jax import lax
from jax.sharding import Mesh
from jax.sharding import PartitionSpec as P
from jax.experimental import pallas as pl
from jax.experimental.pallas import tpu as pltpu

GX_GY = ("gx_0", "gx_1", "gy_0", "gy_1")
GX = ("gx_0", "gx_1")
GY = ("gy_0", "gy_1")


def shifted(piece, axis, pairs, dim):
    if dim == 1:
        flat = piece.reshape(piece.shape[0], piece.shape[2])
        return lax.ppermute(flat, axis, pairs).reshape(piece.shape)
    return lax.ppermute(piece, axis, pairs)


def extended(shard, sides, width):
    edges = {}
    for axis, dim in sides:
        count, length = (lax.axis_size(axis), shard.shape[dim])
        up = [(i, (i + 1) % count) for i in range(count - 1)]
        last = lax.slice_in_dim(shard, length - width, length, axis=dim)
        first = lax.slice_in_dim(shard, 0, width, axis=dim)
        edges[dim] = (
            shifted(last, axis, up, dim),
            shifted(first, axis, [(b, a) for a, b in up], dim),
        )
    done = []
    for _, dim in sides:
        low, high = edges[dim]
        around = [(width, width) if d in done else (0, 0) for d in range(shard.ndim)]
        shard = jnp.concatenate([jnp.pad(low, around), shard, jnp.pad(high, around)], axis=dim)
        done.append(dim)
    return shard


def over_axes(shard, axes):
    for axis in axes:
        shard = lax.psum(shard, axis)
    return shard


def with_halo(block, sides, width):
    for axis, dim in sides:
        count = lax.axis_size(axis)
        forward = [(i, i + 1) for i in range(count - 1)]
        backward = [(target, source) for source, target in forward]
        low = shifted(
            lax.slice_in_dim(block, block.shape[dim] - width, None, axis=dim), axis, forward, dim
        )
        high = shifted(lax.slice_in_dim(block, 0, width, axis=dim), axis, backward, dim)
        block = jnp.concatenate([low, block, high], axis=dim)
    return block


def build_send(bricks, brick_target, brick_slot, peers, capacity):
    target = brick_target[:, 0]
    onehot = (target[:, None] == jnp.arange(peers, dtype=jnp.int32)[None, :]).astype(jnp.int32)
    earlier = jnp.cumsum(onehot, axis=0) - onehot
    order = jnp.sum(earlier * onehot, axis=1)
    place = target * capacity + order
    high = (brick_slot // 32).astype(jnp.bfloat16)
    low = (brick_slot % 32).astype(jnp.bfloat16)
    tag = jnp.zeros((bricks.shape[0], 128), jnp.bfloat16).at[:, 0].set(high).at[:, 1].set(low)
    rows = jnp.concatenate([bricks, tag], axis=1)
    chosen = place[None, None, :] == (
        jnp.arange(peers, dtype=jnp.int32)[:, None, None] * capacity
        + jnp.arange(capacity, dtype=jnp.int32)[None, :, None]
    )
    payload = jnp.einsum(
        "pck,kj->pcj", chosen.astype(jnp.bfloat16), rows, preferred_element_type=jnp.float32
    )
    return payload.astype(jnp.bfloat16)


def next_along_z(field):
    edge = jnp.zeros(field.shape[:-1] + (1,), field.dtype)
    return jnp.concatenate([field[..., 1:], edge], axis=-1)


def prior_along_z(field):
    edge = jnp.zeros(field.shape[:-1] + (1,), field.dtype)
    return jnp.concatenate([edge, field[..., :-1]], axis=-1)


def operate(field, screen):
    padded = extended(field, ((GX, 0), (GY, 1)), 1)
    beside = padded[2:, 1:-1] + padded[:-2, 1:-1]
    beside = beside + padded[1:-1, 2:] + padded[1:-1, :-2]
    beside = beside + next_along_z(field) + prior_along_z(field)
    return (6.0 + screen) * field - beside


def component_grid(blocks, comp, span_x, span_y, span_z):
    part_blocks = blocks[:, comp, :].reshape(span_x, span_y, span_z, 8, 8, 8)
    grid = part_blocks.transpose(0, 3, 1, 4, 2, 5)
    return grid.reshape(span_x * 8, span_y * 8, span_z * 8)


def relayout_kernel(blk_ref, out_ref):
    sub = lax.broadcasted_iota(jnp.int32, (8, 128), 0)
    lane = lax.broadcasted_iota(jnp.int32, (8, 128), 1)
    grp = (lane // 8) % 8
    low_half = lane < 64
    swaps = []
    for m in (4, 2, 1):
        first = ((sub & m) == 0) & ((grp & m) != 0)
        second = ((sub & m) != 0) & ((grp & m) == 0)
        swaps.append((m, first, second))

    def transpose_groups(x):
        for m, first, second in swaps:
            a = pltpu.roll(pltpu.roll(x, 8 - m, 0), 8 * m, 1)
            b = pltpu.roll(pltpu.roll(x, m, 0), 128 - 8 * m, 1)
            x = jnp.where(first, a, jnp.where(second, b, x))
        return x

    def step(i, carry):
        ly = i % 8
        lx = i // 8
        row = pl.multiple_of(i * 16, 16)
        y = pl.multiple_of(ly * 8, 8)
        top = blk_ref[pl.ds(row, 8), :]
        bottom = blk_ref[pl.ds(row + 8, 8), :]
        for c in range(3):
            for uh in range(4):
                col = (c * 4 + uh) * 128
                s0 = top[:, col:col + 128]
                s1 = bottom[:, col:col + 128]
                u0 = jnp.where(low_half, s0, pltpu.roll(s1, 64, 1))
                u1 = jnp.where(low_half, pltpu.roll(s0, 64, 1), s1)
                out_ref[c, lx * 8 + uh * 2, pl.ds(y, 8), :] = transpose_groups(u0)
                out_ref[c, lx * 8 + uh * 2 + 1, pl.ds(y, 8), :] = transpose_groups(u1)
        return carry

    lax.fori_loop(0, 32, step, 0)


def to_grid(blocks, span_x, span_y, depth):
    return pl.pallas_call(
        relayout_kernel,
        out_shape=jax.ShapeDtypeStruct((3, span_x * 8, span_y * 8, depth), jnp.float32),
        in_specs=[pl.BlockSpec(memory_space=pltpu.VMEM)],
        out_specs=pl.BlockSpec(memory_space=pltpu.VMEM),
    )(blocks)


def body(bricks, brick_target, brick_slot, screen, coarse_guess):
    peers = lax.axis_size(GX_GY)
    capacity = max(2, 3 * bricks.shape[0] // peers)
    payload = build_send(bricks, brick_target, brick_slot, peers, capacity)
    arrived = lax.all_to_all(payload, GX_GY, split_axis=0, concat_axis=0, tiled=True)
    tag = arrived[:, :, 1536:1538].astype(jnp.int32)
    landed = tag[:, :, 0] * 32 + tag[:, :, 1]
    width_x, width_y, depth = screen.shape
    span_x = width_x // 8
    span_y = width_y // 8
    span_z = depth // 8
    picks = landed[:, :, None] == jnp.arange(span_x * span_y * span_z, dtype=jnp.int32)[None, None, :]
    blocks = jnp.einsum(
        "pcs,pcj->sj",
        picks.astype(jnp.bfloat16),
        arrived[:, :, :1536],
        preferred_element_type=jnp.float32,
    )
    normals = to_grid(blocks, span_x, span_y, depth)
    normal_x, normal_y, normal_z = normals[0], normals[1], normals[2]
    along_x = with_halo(normal_x, ((GX, 0),), 1)
    along_y = with_halo(normal_y, ((GY, 1),), 1)
    total = along_x[2:] - along_x[:-2]
    total = total + (along_y[:, 2:] - along_y[:, :-2])
    total = total + (next_along_z(normal_z) - prior_along_z(normal_z))
    source = -0.5 * total
    inverse = 1.0 / (6.0 + screen)
    residual = source - operate(coarse_guess, screen)
    precond = residual * inverse
    image = operate(precond, screen)
    scaled = image * inverse
    scaled_image = operate(scaled, screen)
    sums = over_axes(
        jnp.stack(
            [
                jnp.sum(residual * precond),
                jnp.sum(precond * image),
                jnp.sum(image * scaled),
                jnp.sum(scaled * scaled_image),
            ]
        ),
        GX_GY,
    )
    gamma, delta, energy, curvature = sums[0], sums[1], sums[2], sums[3]
    alpha = gamma / delta
    gamma_next = alpha * alpha * energy - gamma
    ratio = gamma_next / gamma
    grow = 1.0 + ratio
    delta_next = grow * grow * delta - 2.0 * grow * alpha * energy + alpha * alpha * curvature
    alpha_next = gamma_next / delta_next
    solution = coarse_guess + alpha * precond
    residual = residual - alpha * image
    direction = residual * inverse + ratio * precond
    along = image - alpha * scaled_image + ratio * image
    solution = solution + alpha_next * direction
    residual = residual - alpha_next * along
    return (solution, residual)


def solution(mesh):
    split = Mesh(mesh.devices.reshape(4, 2, 4, 4), ("gx_0", "gx_1", "gy_0", "gy_1"))
    placed = (P(GX_GY, None), P(GX_GY, None), P(GX_GY), P(GX, GY, None), P(GX, GY, None))
    return jax.shard_map(
        body,
        mesh=split,
        in_specs=placed,
        out_specs=(P(GX, GY, None), P(GX, GY, None)),
        check_vma=False,
    )
```

```python
import jax
import jax.numpy as jnp
from jax import lax
from jax.sharding import Mesh
from jax.sharding import PartitionSpec as P
from jax.experimental import pallas as pl
from jax.experimental.pallas import tpu as pltpu

GX = ("y", "core")
GY = ("x_hi", "x_lo", "z")
GX_GY = GX + GY
ORDER = ("y", "core", "z", "x_lo", "x_hi")


def shifted(piece, axis, pairs, dim):
    if dim == 1:
        flat = piece.reshape(piece.shape[0], piece.shape[2])
        return lax.ppermute(flat, axis, pairs).reshape(piece.shape)
    return lax.ppermute(piece, axis, pairs)


def extended(shard, sides, width):
    edges = {}
    for axis, dim in sides:
        count, length = (lax.axis_size(axis), shard.shape[dim])
        up = [(i, (i + 1) % count) for i in range(count - 1)]
        last = lax.slice_in_dim(shard, length - width, length, axis=dim)
        first = lax.slice_in_dim(shard, 0, width, axis=dim)
        edges[dim] = (
            shifted(last, axis, up, dim),
            shifted(first, axis, [(b, a) for a, b in up], dim),
        )
    done = []
    for _, dim in sides:
        low, high = edges[dim]
        around = [(width, width) if d in done else (0, 0) for d in range(shard.ndim)]
        shard = jnp.concatenate([jnp.pad(low, around), shard, jnp.pad(high, around)], axis=dim)
        done.append(dim)
    return shard


def over_axes(shard, axes):
    for axis in axes:
        shard = lax.psum(shard, axis)
    return shard


def with_halo(block, sides, width):
    for axis, dim in sides:
        count = lax.axis_size(axis)
        forward = [(i, i + 1) for i in range(count - 1)]
        backward = [(target, source) for source, target in forward]
        low = shifted(
            lax.slice_in_dim(block, block.shape[dim] - width, None, axis=dim), axis, forward, dim
        )
        high = shifted(lax.slice_in_dim(block, 0, width, axis=dim), axis, backward, dim)
        block = jnp.concatenate([low, block, high], axis=dim)
    return block


def build_send(bricks, brick_target, brick_slot, peers, capacity):
    target = brick_target[:, 0]
    onehot = (target[:, None] == jnp.arange(peers, dtype=jnp.int32)[None, :]).astype(jnp.int32)
    earlier = jnp.cumsum(onehot, axis=0) - onehot
    order = jnp.sum(earlier * onehot, axis=1)
    place = target * capacity + order
    high = (brick_slot // 32).astype(jnp.bfloat16)
    low = (brick_slot % 32).astype(jnp.bfloat16)
    tag = jnp.zeros((bricks.shape[0], 128), jnp.bfloat16).at[:, 0].set(high).at[:, 1].set(low)
    rows = jnp.concatenate([bricks, tag], axis=1)
    chosen = place[None, None, :] == (
        jnp.arange(peers, dtype=jnp.int32)[:, None, None] * capacity
        + jnp.arange(capacity, dtype=jnp.int32)[None, :, None]
    )
    payload = jnp.einsum(
        "pck,kj->pcj", chosen.astype(jnp.bfloat16), rows, preferred_element_type=jnp.float32
    )
    return payload.astype(jnp.bfloat16)


def next_along_z(field):
    edge = jnp.zeros(field.shape[:-1] + (1,), field.dtype)
    return jnp.concatenate([field[..., 1:], edge], axis=-1)


def prior_along_z(field):
    edge = jnp.zeros(field.shape[:-1] + (1,), field.dtype)
    return jnp.concatenate([edge, field[..., :-1]], axis=-1)


def operate(field, screen):
    padded = extended(field, ((GX, 0), (GY, 1)), 1)
    beside = padded[2:, 1:-1] + padded[:-2, 1:-1]
    beside = beside + padded[1:-1, 2:] + padded[1:-1, :-2]
    beside = beside + next_along_z(field) + prior_along_z(field)
    return (6.0 + screen) * field - beside


def component_grid(blocks, comp, span_x, span_y, span_z):
    part_blocks = blocks[:, comp, :].reshape(span_x, span_y, span_z, 8, 8, 8)
    grid = part_blocks.transpose(0, 3, 1, 4, 2, 5)
    return grid.reshape(span_x * 8, span_y * 8, span_z * 8)


def relayout_kernel(blk_ref, out_ref):
    sub = lax.broadcasted_iota(jnp.int32, (8, 128), 0)
    lane = lax.broadcasted_iota(jnp.int32, (8, 128), 1)
    grp = (lane // 8) % 8
    low_half = lane < 64
    swaps = []
    for m in (4, 2, 1):
        first = ((sub & m) == 0) & ((grp & m) != 0)
        second = ((sub & m) != 0) & ((grp & m) == 0)
        swaps.append((m, first, second))

    def transpose_groups(x):
        for m, first, second in swaps:
            a = pltpu.roll(pltpu.roll(x, 8 - m, 0), 8 * m, 1)
            b = pltpu.roll(pltpu.roll(x, m, 0), 128 - 8 * m, 1)
            x = jnp.where(first, a, jnp.where(second, b, x))
        return x

    def step(i, carry):
        ly = i % 8
        lx = i // 8
        row = pl.multiple_of(i * 16, 16)
        y = pl.multiple_of(ly * 8, 8)
        top = blk_ref[pl.ds(row, 8), :]
        bottom = blk_ref[pl.ds(row + 8, 8), :]
        for c in range(3):
            for uh in range(4):
                col = (c * 4 + uh) * 128
                s0 = top[:, col:col + 128]
                s1 = bottom[:, col:col + 128]
                u0 = jnp.where(low_half, s0, pltpu.roll(s1, 64, 1))
                u1 = jnp.where(low_half, pltpu.roll(s0, 64, 1), s1)
                out_ref[c, lx * 8 + uh * 2, pl.ds(y, 8), :] = transpose_groups(u0)
                out_ref[c, lx * 8 + uh * 2 + 1, pl.ds(y, 8), :] = transpose_groups(u1)
        return carry

    lax.fori_loop(0, 32, step, 0)


def to_grid(blocks, span_x, span_y, depth):
    return pl.pallas_call(
        relayout_kernel,
        out_shape=jax.ShapeDtypeStruct((3, span_x * 8, span_y * 8, depth), jnp.float32),
        in_specs=[pl.BlockSpec(memory_space=pltpu.VMEM)],
        out_specs=pl.BlockSpec(memory_space=pltpu.VMEM),
    )(blocks)


def body(bricks, brick_target, brick_slot, screen, coarse_guess):
    peers = lax.axis_size(GX_GY)
    capacity = max(2, 3 * bricks.shape[0] // peers)
    payload = build_send(bricks, brick_target, brick_slot, peers, capacity)
    arrived = lax.all_to_all(payload, GX_GY, split_axis=0, concat_axis=0, tiled=True)
    tag = arrived[:, :, 1536:1538].astype(jnp.int32)
    landed = tag[:, :, 0] * 32 + tag[:, :, 1]
    width_x, width_y, depth = screen.shape
    span_x = width_x // 8
    span_y = width_y // 8
    span_z = depth // 8
    picks = landed[:, :, None] == jnp.arange(span_x * span_y * span_z, dtype=jnp.int32)[None, None, :]
    blocks = jnp.einsum(
        "pcs,pcj->sj",
        picks.astype(jnp.bfloat16),
        arrived,
        preferred_element_type=jnp.float32,
    )
    normals = to_grid(blocks, span_x, span_y, depth)
    normal_x, normal_y, normal_z = normals[0], normals[1], normals[2]
    along_x = with_halo(normal_x, ((GX, 0),), 1)
    along_y = with_halo(normal_y, ((GY, 1),), 1)
    total = along_x[2:] - along_x[:-2]
    total = total + (along_y[:, 2:] - along_y[:, :-2])
    total = total + (next_along_z(normal_z) - prior_along_z(normal_z))
    source = -0.5 * total
    inverse = 1.0 / (6.0 + screen)
    residual = source - operate(coarse_guess, screen)
    precond = residual * inverse
    image = operate(precond, screen)
    scaled = image * inverse
    scaled_image = operate(scaled, screen)
    sums = over_axes(
        jnp.stack(
            [
                jnp.sum(residual * precond),
                jnp.sum(precond * image),
                jnp.sum(image * scaled),
                jnp.sum(scaled * scaled_image),
            ]
        ),
        ORDER,
    )
    gamma, delta, energy, curvature = sums[0], sums[1], sums[2], sums[3]
    alpha = gamma / delta
    gamma_next = alpha * alpha * energy - gamma
    ratio = gamma_next / gamma
    grow = 1.0 + ratio
    delta_next = grow * grow * delta - 2.0 * grow * alpha * energy + alpha * alpha * curvature
    alpha_next = gamma_next / delta_next
    solution = coarse_guess + alpha * precond
    residual = residual - alpha * image
    direction = residual * inverse + ratio * precond
    along = image - alpha * scaled_image + ratio * image
    solution = solution + alpha_next * direction
    residual = residual - alpha_next * along
    return (solution, residual)


def solution(mesh):
    split = Mesh(mesh.devices.reshape(4, 2, 2, 2, 4), GX_GY)
    placed = (P(GX_GY, None), P(GX_GY, None), P(GX_GY), P(GX, GY, None), P(GX, GY, None))
    return jax.shard_map(
        body,
        mesh=split,
        in_specs=placed,
        out_specs=(P(GX, GY, None), P(GX, GY, None)),
        check_vma=False,
    )
```

```python
import functools

import jax
import jax.numpy as jnp
from jax import lax
from jax.sharding import Mesh
from jax.sharding import PartitionSpec as P
from jax.experimental import pallas as pl
from jax.experimental.pallas import tpu as pltpu

GX_GY = ("gx_0", "gx_1", "gy_0", "gy_1")
GX = ("gx_0", "gx_1")
GY = ("gy_0", "gy_1")


def shifted(piece, axis, pairs, dim):
    if dim == 1:
        flat = piece.reshape(piece.shape[0], piece.shape[2])
        return lax.ppermute(flat, axis, pairs).reshape(piece.shape)
    return lax.ppermute(piece, axis, pairs)


def extended(shard, sides, width):
    edges = {}
    for axis, dim in sides:
        count, length = (lax.axis_size(axis), shard.shape[dim])
        up = [(i, (i + 1) % count) for i in range(count - 1)]
        last = lax.slice_in_dim(shard, length - width, length, axis=dim)
        first = lax.slice_in_dim(shard, 0, width, axis=dim)
        edges[dim] = (
            shifted(last, axis, up, dim),
            shifted(first, axis, [(b, a) for a, b in up], dim),
        )
    done = []
    for _, dim in sides:
        low, high = edges[dim]
        around = [(width, width) if d in done else (0, 0) for d in range(shard.ndim)]
        shard = jnp.concatenate([jnp.pad(low, around), shard, jnp.pad(high, around)], axis=dim)
        done.append(dim)
    return shard


def over_axes(shard, axes):
    for axis in axes:
        shard = lax.psum(shard, axis)
    return shard


def with_halo(block, sides, width):
    for axis, dim in sides:
        count = lax.axis_size(axis)
        forward = [(i, i + 1) for i in range(count - 1)]
        backward = [(target, source) for source, target in forward]
        low = shifted(
            lax.slice_in_dim(block, block.shape[dim] - width, None, axis=dim), axis, forward, dim
        )
        high = shifted(lax.slice_in_dim(block, 0, width, axis=dim), axis, backward, dim)
        block = jnp.concatenate([low, block, high], axis=dim)
    return block


def build_send(bricks, brick_target, brick_slot, peers, capacity):
    target = brick_target[:, 0]
    onehot = (target[:, None] == jnp.arange(peers, dtype=jnp.int32)[None, :]).astype(jnp.int32)
    earlier = jnp.cumsum(onehot, axis=0) - onehot
    order = jnp.sum(earlier * onehot, axis=1)
    place = target * capacity + order
    high = (brick_slot // 32).astype(jnp.bfloat16)
    low = (brick_slot % 32).astype(jnp.bfloat16)
    tag = jnp.zeros((bricks.shape[0], 128), jnp.bfloat16).at[:, 0].set(high).at[:, 1].set(low)
    rows = jnp.concatenate([bricks, tag], axis=1)
    chosen = place[None, None, :] == (
        jnp.arange(peers, dtype=jnp.int32)[:, None, None] * capacity
        + jnp.arange(capacity, dtype=jnp.int32)[None, :, None]
    )
    payload = jnp.einsum(
        "pck,kj->pcj", chosen.astype(jnp.bfloat16), rows, preferred_element_type=jnp.float32
    )
    return payload.astype(jnp.bfloat16)


def next_along_z(field):
    edge = jnp.zeros(field.shape[:-1] + (1,), field.dtype)
    return jnp.concatenate([field[..., 1:], edge], axis=-1)


def prior_along_z(field):
    edge = jnp.zeros(field.shape[:-1] + (1,), field.dtype)
    return jnp.concatenate([edge, field[..., :-1]], axis=-1)


def operate(field, screen):
    padded = extended(field, ((GX, 0), (GY, 1)), 1)
    beside = padded[2:, 1:-1] + padded[:-2, 1:-1]
    beside = beside + padded[1:-1, 2:] + padded[1:-1, :-2]
    beside = beside + next_along_z(field) + prior_along_z(field)
    return (6.0 + screen) * field - beside


def component_grid(blocks, comp, span_x, span_y, span_z):
    part_blocks = blocks[:, comp, :].reshape(span_x, span_y, span_z, 8, 8, 8)
    grid = part_blocks.transpose(0, 3, 1, 4, 2, 5)
    return grid.reshape(span_x * 8, span_y * 8, span_z * 8)


def relayout_kernel(comp, blk_ref, out_ref):
    sub = lax.broadcasted_iota(jnp.int32, (8, 128), 0)
    lane = lax.broadcasted_iota(jnp.int32, (8, 128), 1)
    grp = (lane // 8) % 8
    low_half = lane < 64
    swaps = []
    for m in (4, 2, 1):
        first = ((sub & m) == 0) & ((grp & m) != 0)
        second = ((sub & m) != 0) & ((grp & m) == 0)
        swaps.append((m, first, second))

    def transpose_groups(x):
        for m, first, second in swaps:
            a = pltpu.roll(pltpu.roll(x, 8 - m, 0), 8 * m, 1)
            b = pltpu.roll(pltpu.roll(x, m, 0), 128 - 8 * m, 1)
            x = jnp.where(first, a, jnp.where(second, b, x))
        return x

    def step(i, carry):
        ly = i % 8
        lx = i // 8
        row = pl.multiple_of(i * 16, 16)
        y = pl.multiple_of(ly * 8, 8)
        top = blk_ref[pl.ds(row, 8), :]
        bottom = blk_ref[pl.ds(row + 8, 8), :]
        for uh in range(4):
            col = (comp * 4 + uh) * 128
            s0 = top[:, col:col + 128]
            s1 = bottom[:, col:col + 128]
            u0 = jnp.where(low_half, s0, pltpu.roll(s1, 64, 1))
            u1 = jnp.where(low_half, pltpu.roll(s0, 64, 1), s1)
            out_ref[lx * 8 + uh * 2, pl.ds(y, 8), :] = transpose_groups(u0)
            out_ref[lx * 8 + uh * 2 + 1, pl.ds(y, 8), :] = transpose_groups(u1)
        return carry

    lax.fori_loop(0, 32, step, 0)


def to_grid(blocks, comp, span_x, span_y, depth):
    cells = span_x * span_y * 8 * depth
    return pl.pallas_call(
        functools.partial(relayout_kernel, comp),
        out_shape=jax.ShapeDtypeStruct((span_x * 8, span_y * 8, depth), jnp.float32),
        in_specs=[pl.BlockSpec(memory_space=pltpu.VMEM)],
        out_specs=pl.BlockSpec(memory_space=pltpu.VMEM),
        cost_estimate=pl.CostEstimate(flops=20 * cells, bytes_accessed=8 * cells, transcendentals=0),
    )(blocks)


def body(bricks, brick_target, brick_slot, screen, coarse_guess):
    peers = lax.axis_size(GX_GY)
    capacity = max(2, 3 * bricks.shape[0] // peers)
    payload = build_send(bricks, brick_target, brick_slot, peers, capacity)
    arrived = lax.all_to_all(payload, GX_GY, split_axis=0, concat_axis=0, tiled=True)
    tag = arrived[:, :, 1536:1538].astype(jnp.int32)
    landed = tag[:, :, 0] * 32 + tag[:, :, 1]
    width_x, width_y, depth = screen.shape
    span_x = width_x // 8
    span_y = width_y // 8
    span_z = depth // 8
    picks = landed[:, :, None] == jnp.arange(span_x * span_y * span_z, dtype=jnp.int32)[None, None, :]
    blocks = jnp.einsum(
        "pcs,pcj->sj",
        picks.astype(jnp.bfloat16),
        arrived[:, :, :1536],
        preferred_element_type=jnp.float32,
    )
    normal_x = to_grid(blocks, 0, span_x, span_y, depth)
    normal_y = to_grid(blocks, 1, span_x, span_y, depth)
    normal_z = to_grid(blocks, 2, span_x, span_y, depth)
    along_x = with_halo(normal_x, ((GX, 0),), 1)
    along_y = with_halo(normal_y, ((GY, 1),), 1)
    total = along_x[2:] - along_x[:-2]
    total = total + (along_y[:, 2:] - along_y[:, :-2])
    total = total + (next_along_z(normal_z) - prior_along_z(normal_z))
    source = -0.5 * total
    inverse = 1.0 / (6.0 + screen)
    residual = source - operate(coarse_guess, screen)
    precond = residual * inverse
    image = operate(precond, screen)
    scaled = image * inverse
    scaled_image = operate(scaled, screen)
    sums = over_axes(
        jnp.stack(
            [
                jnp.sum(residual * precond),
                jnp.sum(precond * image),
                jnp.sum(image * scaled),
                jnp.sum(scaled * scaled_image),
            ]
        ),
        GX_GY,
    )
    gamma, delta, energy, curvature = sums[0], sums[1], sums[2], sums[3]
    alpha = gamma / delta
    gamma_next = alpha * alpha * energy - gamma
    ratio = gamma_next / gamma
    grow = 1.0 + ratio
    delta_next = grow * grow * delta - 2.0 * grow * alpha * energy + alpha * alpha * curvature
    alpha_next = gamma_next / delta_next
    solution = coarse_guess + alpha * precond
    residual = residual - alpha * image
    direction = residual * inverse + ratio * precond
    along = image - alpha * scaled_image + ratio * image
    solution = solution + alpha_next * direction
    residual = residual - alpha_next * along
    return (solution, residual)


def solution(mesh):
    split = Mesh(mesh.devices.reshape(4, 2, 4, 4), ("gx_0", "gx_1", "gy_0", "gy_1"))
    placed = (P(GX_GY, None), P(GX_GY, None), P(GX_GY), P(GX, GY, None), P(GX, GY, None))
    return jax.shard_map(
        body,
        mesh=split,
        in_specs=placed,
        out_specs=(P(GX, GY, None), P(GX, GY, None)),
        check_vma=False,
    )
```

```python
import jax
import jax.numpy as jnp
from jax import lax
from jax.sharding import Mesh
from jax.sharding import PartitionSpec as P
from jax.experimental import pallas as pl
from jax.experimental.pallas import tpu as pltpu

GX_GY = ("gx_0", "gx_1", "gy_0", "gy_1")
GX = ("gx_0", "gx_1")
GY = ("gy_0", "gy_1")


def shifted(piece, axis, pairs, dim):
    if dim == 1:
        flat = piece.reshape(piece.shape[0], piece.shape[2])
        return lax.ppermute(flat, axis, pairs).reshape(piece.shape)
    return lax.ppermute(piece, axis, pairs)


def extended(shard, sides, width):
    edges = {}
    for axis, dim in sides:
        count, length = (lax.axis_size(axis), shard.shape[dim])
        up = [(i, (i + 1) % count) for i in range(count - 1)]
        last = lax.slice_in_dim(shard, length - width, length, axis=dim)
        first = lax.slice_in_dim(shard, 0, width, axis=dim)
        edges[dim] = (
            shifted(last, axis, up, dim),
            shifted(first, axis, [(b, a) for a, b in up], dim),
        )
    done = []
    for _, dim in sides:
        low, high = edges[dim]
        around = [(width, width) if d in done else (0, 0) for d in range(shard.ndim)]
        shard = jnp.concatenate([jnp.pad(low, around), shard, jnp.pad(high, around)], axis=dim)
        done.append(dim)
    return shard


def over_axes(shard, axes):
    for axis in axes:
        shard = lax.psum(shard, axis)
    return shard


def with_halo(block, sides, width):
    for axis, dim in sides:
        count = lax.axis_size(axis)
        forward = [(i, i + 1) for i in range(count - 1)]
        backward = [(target, source) for source, target in forward]
        low = shifted(
            lax.slice_in_dim(block, block.shape[dim] - width, None, axis=dim), axis, forward, dim
        )
        high = shifted(lax.slice_in_dim(block, 0, width, axis=dim), axis, backward, dim)
        block = jnp.concatenate([low, block, high], axis=dim)
    return block


def build_send(bricks, brick_target, brick_slot, peers, capacity):
    target = brick_target[:, 0]
    onehot = (target[:, None] == jnp.arange(peers, dtype=jnp.int32)[None, :]).astype(jnp.int32)
    earlier = jnp.cumsum(onehot, axis=0) - onehot
    order = jnp.sum(earlier * onehot, axis=1)
    place = target * capacity + order
    high = (brick_slot // 32).astype(jnp.bfloat16)
    low = (brick_slot % 32).astype(jnp.bfloat16)
    tag = jnp.zeros((bricks.shape[0], 128), jnp.bfloat16).at[:, 0].set(high).at[:, 1].set(low)
    rows = jnp.concatenate([bricks, tag], axis=1)
    chosen = place[None, None, :] == (
        jnp.arange(peers, dtype=jnp.int32)[:, None, None] * capacity
        + jnp.arange(capacity, dtype=jnp.int32)[None, :, None]
    )
    payload = jnp.einsum(
        "pck,kj->pcj", chosen.astype(jnp.bfloat16), rows, preferred_element_type=jnp.float32
    )
    return payload.astype(jnp.bfloat16)


def next_along_z(field):
    edge = jnp.zeros(field.shape[:-1] + (1,), field.dtype)
    return jnp.concatenate([field[..., 1:], edge], axis=-1)


def prior_along_z(field):
    edge = jnp.zeros(field.shape[:-1] + (1,), field.dtype)
    return jnp.concatenate([edge, field[..., :-1]], axis=-1)


def operate(field, screen):
    padded = extended(field, ((GX, 0), (GY, 1)), 1)
    beside = padded[2:, 1:-1] + padded[:-2, 1:-1]
    beside = beside + padded[1:-1, 2:] + padded[1:-1, :-2]
    beside = beside + next_along_z(field) + prior_along_z(field)
    return (6.0 + screen) * field - beside


def component_grid(blocks, comp, span_x, span_y, span_z):
    part_blocks = blocks[:, comp, :].reshape(span_x, span_y, span_z, 8, 8, 8)
    grid = part_blocks.transpose(0, 3, 1, 4, 2, 5)
    return grid.reshape(span_x * 8, span_y * 8, span_z * 8)


def relayout_kernel(blk_ref, out_ref):
    sub = lax.broadcasted_iota(jnp.int32, (8, 128), 0)
    lane = lax.broadcasted_iota(jnp.int32, (8, 128), 1)
    grp = (lane // 8) % 8
    low_half = lane < 64
    swaps = []
    for m in (4, 2, 1):
        first = ((sub & m) == 0) & ((grp & m) != 0)
        second = ((sub & m) != 0) & ((grp & m) == 0)
        swaps.append((m, first, second))

    def transpose_groups(x):
        for m, first, second in swaps:
            a = pltpu.roll(pltpu.roll(x, 8 - m, 0), 8 * m, 1)
            b = pltpu.roll(pltpu.roll(x, m, 0), 128 - 8 * m, 1)
            x = jnp.where(first, a, jnp.where(second, b, x))
        return x

    top = blk_ref[0:8, :]
    bottom = blk_ref[8:16, :]
    for c in range(3):
        for uh in range(4):
            col = (c * 4 + uh) * 128
            s0 = top[:, col:col + 128]
            s1 = bottom[:, col:col + 128]
            u0 = jnp.where(low_half, s0, pltpu.roll(s1, 64, 1))
            u1 = jnp.where(low_half, pltpu.roll(s0, 64, 1), s1)
            out_ref[c, uh * 2] = transpose_groups(u0)
            out_ref[c, uh * 2 + 1] = transpose_groups(u1)


def to_grid(blocks, span_x, span_y, depth):
    cells = 3 * span_x * span_y * 64 * depth
    return pl.pallas_call(
        relayout_kernel,
        out_shape=jax.ShapeDtypeStruct((3, span_x * 8, span_y * 8, depth), jnp.float32),
        grid=(span_x, span_y),
        in_specs=[pl.BlockSpec((16, blocks.shape[1]), lambda i, j: (i * span_y + j, 0))],
        out_specs=pl.BlockSpec((3, 8, 8, depth), lambda i, j: (0, i, j, 0)),
        cost_estimate=pl.CostEstimate(flops=20 * cells, bytes_accessed=8 * cells, transcendentals=0),
    )(blocks)


def body(bricks, brick_target, brick_slot, screen, coarse_guess):
    peers = lax.axis_size(GX_GY)
    capacity = max(2, 3 * bricks.shape[0] // peers)
    payload = build_send(bricks, brick_target, brick_slot, peers, capacity)
    arrived = lax.all_to_all(payload, GX_GY, split_axis=0, concat_axis=0, tiled=True)
    tag = arrived[:, :, 1536:1538].astype(jnp.int32)
    landed = tag[:, :, 0] * 32 + tag[:, :, 1]
    width_x, width_y, depth = screen.shape
    span_x = width_x // 8
    span_y = width_y // 8
    span_z = depth // 8
    picks = landed[:, :, None] == jnp.arange(span_x * span_y * span_z, dtype=jnp.int32)[None, None, :]
    blocks = jnp.einsum(
        "pcs,pcj->sj",
        picks.astype(jnp.bfloat16),
        arrived[:, :, :1536],
        preferred_element_type=jnp.float32,
    )
    normals = to_grid(blocks, span_x, span_y, depth)
    normal_x, normal_y, normal_z = normals[0], normals[1], normals[2]
    along_x = with_halo(normal_x, ((GX, 0),), 1)
    along_y = with_halo(normal_y, ((GY, 1),), 1)
    total = along_x[2:] - along_x[:-2]
    total = total + (along_y[:, 2:] - along_y[:, :-2])
    total = total + (next_along_z(normal_z) - prior_along_z(normal_z))
    source = -0.5 * total
    inverse = 1.0 / (6.0 + screen)
    residual = source - operate(coarse_guess, screen)
    precond = residual * inverse
    image = operate(precond, screen)
    scaled = image * inverse
    scaled_image = operate(scaled, screen)
    sums = over_axes(
        jnp.stack(
            [
                jnp.sum(residual * precond),
                jnp.sum(precond * image),
                jnp.sum(image * scaled),
                jnp.sum(scaled * scaled_image),
            ]
        ),
        GX_GY,
    )
    gamma, delta, energy, curvature = sums[0], sums[1], sums[2], sums[3]
    alpha = gamma / delta
    gamma_next = alpha * alpha * energy - gamma
    ratio = gamma_next / gamma
    grow = 1.0 + ratio
    delta_next = grow * grow * delta - 2.0 * grow * alpha * energy + alpha * alpha * curvature
    alpha_next = gamma_next / delta_next
    solution = coarse_guess + alpha * precond
    residual = residual - alpha * image
    direction = residual * inverse + ratio * precond
    along = image - alpha * scaled_image + ratio * image
    solution = solution + alpha_next * direction
    residual = residual - alpha_next * along
    return (solution, residual)


def solution(mesh):
    split = Mesh(mesh.devices.reshape(4, 2, 4, 4), ("gx_0", "gx_1", "gy_0", "gy_1"))
    placed = (P(GX_GY, None), P(GX_GY, None), P(GX_GY), P(GX, GY, None), P(GX, GY, None))
    return jax.shard_map(
        body,
        mesh=split,
        in_specs=placed,
        out_specs=(P(GX, GY, None), P(GX, GY, None)),
        check_vma=False,
    )
```

```python
import jax
import jax.numpy as jnp
from jax import lax
from jax.sharding import Mesh
from jax.sharding import PartitionSpec as P
from jax.experimental import pallas as pl
from jax.experimental.pallas import tpu as pltpu

GX_GY = ("gx_0", "gx_1", "gy_0", "gy_1")
GX = ("gx_0", "gx_1")
GY = ("gy_0", "gy_1")


def shifted(piece, axis, pairs, dim):
    if dim == 1:
        flat = piece.reshape(piece.shape[0], piece.shape[2])
        return lax.ppermute(flat, axis, pairs).reshape(piece.shape)
    return lax.ppermute(piece, axis, pairs)


def extended(shard, sides, width):
    edges = {}
    for axis, dim in sides:
        count, length = (lax.axis_size(axis), shard.shape[dim])
        up = [(i, (i + 1) % count) for i in range(count - 1)]
        last = lax.slice_in_dim(shard, length - width, length, axis=dim)
        first = lax.slice_in_dim(shard, 0, width, axis=dim)
        edges[dim] = (
            shifted(last, axis, up, dim),
            shifted(first, axis, [(b, a) for a, b in up], dim),
        )
    done = []
    for _, dim in sides:
        low, high = edges[dim]
        around = [(width, width) if d in done else (0, 0) for d in range(shard.ndim)]
        shard = jnp.concatenate([jnp.pad(low, around), shard, jnp.pad(high, around)], axis=dim)
        done.append(dim)
    return shard


def over_axes(shard, axes):
    for axis in axes:
        shard = lax.psum(shard, axis)
    return shard


def with_halo(block, sides, width):
    for axis, dim in sides:
        count = lax.axis_size(axis)
        forward = [(i, i + 1) for i in range(count - 1)]
        backward = [(target, source) for source, target in forward]
        low = shifted(
            lax.slice_in_dim(block, block.shape[dim] - width, None, axis=dim), axis, forward, dim
        )
        high = shifted(lax.slice_in_dim(block, 0, width, axis=dim), axis, backward, dim)
        block = jnp.concatenate([low, block, high], axis=dim)
    return block


def build_send(bricks, brick_target, brick_slot, peers, capacity):
    target = brick_target[:, 0]
    onehot = (target[:, None] == jnp.arange(peers, dtype=jnp.int32)[None, :]).astype(jnp.int32)
    earlier = jnp.cumsum(onehot, axis=0) - onehot
    order = jnp.sum(earlier * onehot, axis=1)
    place = target * capacity + order
    high = (brick_slot // 32).astype(jnp.bfloat16)
    low = (brick_slot % 32).astype(jnp.bfloat16)
    tag = jnp.zeros((bricks.shape[0], 128), jnp.bfloat16).at[:, 0].set(high).at[:, 1].set(low)
    rows = jnp.concatenate([bricks, tag], axis=1)
    chosen = place[None, None, :] == (
        jnp.arange(peers, dtype=jnp.int32)[:, None, None] * capacity
        + jnp.arange(capacity, dtype=jnp.int32)[None, :, None]
    )
    payload = jnp.einsum(
        "pck,kj->pcj", chosen.astype(jnp.bfloat16), rows, preferred_element_type=jnp.float32
    )
    return payload.astype(jnp.bfloat16)


def next_along_z(field):
    edge = jnp.zeros(field.shape[:-1] + (1,), field.dtype)
    return jnp.concatenate([field[..., 1:], edge], axis=-1)


def prior_along_z(field):
    edge = jnp.zeros(field.shape[:-1] + (1,), field.dtype)
    return jnp.concatenate([edge, field[..., :-1]], axis=-1)


def operate(field, screen):
    padded = extended(field, ((GX, 0), (GY, 1)), 1)
    beside = padded[2:, 1:-1] + padded[:-2, 1:-1]
    beside = beside + padded[1:-1, 2:] + padded[1:-1, :-2]
    beside = beside + next_along_z(field) + prior_along_z(field)
    return (6.0 + screen) * field - beside


def component_grid(blocks, comp, span_x, span_y, span_z):
    part_blocks = blocks[:, comp, :].reshape(span_x, span_y, span_z, 8, 8, 8)
    grid = part_blocks.transpose(0, 3, 1, 4, 2, 5)
    return grid.reshape(span_x * 8, span_y * 8, span_z * 8)


def relayout_kernel(blk_ref, out_ref):
    sub = lax.broadcasted_iota(jnp.int32, (8, 128), 0)
    lane = lax.broadcasted_iota(jnp.int32, (8, 128), 1)
    grp = (lane // 8) % 8
    low_half = lane < 64
    swaps = []
    for m in (4, 2, 1):
        first = ((sub & m) == 0) & ((grp & m) != 0)
        second = ((sub & m) != 0) & ((grp & m) == 0)
        swaps.append((m, first, second))

    def transpose_groups(x):
        for m, first, second in swaps:
            a = pltpu.roll(pltpu.roll(x, 8 - m, 0), 8 * m, 1)
            b = pltpu.roll(pltpu.roll(x, m, 0), 128 - 8 * m, 1)
            x = jnp.where(first, a, jnp.where(second, b, x))
        return x

    def step(ly, carry):
        row = pl.multiple_of(ly * 16, 16)
        y = pl.multiple_of(ly * 8, 8)
        top = blk_ref[pl.ds(row, 8), :]
        bottom = blk_ref[pl.ds(row + 8, 8), :]
        for c in range(3):
            for uh in range(4):
                col = (c * 4 + uh) * 128
                s0 = top[:, col:col + 128]
                s1 = bottom[:, col:col + 128]
                u0 = jnp.where(low_half, s0, pltpu.roll(s1, 64, 1))
                u1 = jnp.where(low_half, pltpu.roll(s0, 64, 1), s1)
                out_ref[c, uh * 2, pl.ds(y, 8), :] = transpose_groups(u0)
                out_ref[c, uh * 2 + 1, pl.ds(y, 8), :] = transpose_groups(u1)
        return carry

    lax.fori_loop(0, 8, step, 0)


def to_grid(blocks, span_x, span_y, depth):
    cells = 3 * span_x * span_y * 64 * depth
    return pl.pallas_call(
        relayout_kernel,
        out_shape=jax.ShapeDtypeStruct((3, span_x * 8, span_y * 8, depth), jnp.float32),
        grid=(span_x,),
        in_specs=[pl.BlockSpec((span_y * 16, blocks.shape[1]), lambda i: (i, 0))],
        out_specs=pl.BlockSpec((3, 8, span_y * 8, depth), lambda i: (0, i, 0, 0)),
        cost_estimate=pl.CostEstimate(flops=20 * cells, bytes_accessed=8 * cells, transcendentals=0),
    )(blocks)


def body(bricks, brick_target, brick_slot, screen, coarse_guess):
    peers = lax.axis_size(GX_GY)
    capacity = max(2, 3 * bricks.shape[0] // peers)
    payload = build_send(bricks, brick_target, brick_slot, peers, capacity)
    arrived = lax.all_to_all(payload, GX_GY, split_axis=0, concat_axis=0, tiled=True)
    tag = arrived[:, :, 1536:1538].astype(jnp.int32)
    landed = tag[:, :, 0] * 32 + tag[:, :, 1]
    width_x, width_y, depth = screen.shape
    span_x = width_x // 8
    span_y = width_y // 8
    span_z = depth // 8
    picks = landed[:, :, None] == jnp.arange(span_x * span_y * span_z, dtype=jnp.int32)[None, None, :]
    blocks = jnp.einsum(
        "pcs,pcj->sj",
        picks.astype(jnp.bfloat16),
        arrived[:, :, :1536],
        preferred_element_type=jnp.float32,
    )
    normals = to_grid(blocks, span_x, span_y, depth)
    normal_x, normal_y, normal_z = normals[0], normals[1], normals[2]
    along_x = with_halo(normal_x, ((GX, 0),), 1)
    along_y = with_halo(normal_y, ((GY, 1),), 1)
    total = along_x[2:] - along_x[:-2]
    total = total + (along_y[:, 2:] - along_y[:, :-2])
    total = total + (next_along_z(normal_z) - prior_along_z(normal_z))
    source = -0.5 * total
    inverse = 1.0 / (6.0 + screen)
    residual = source - operate(coarse_guess, screen)
    precond = residual * inverse
    image = operate(precond, screen)
    scaled = image * inverse
    scaled_image = operate(scaled, screen)
    sums = over_axes(
        jnp.stack(
            [
                jnp.sum(residual * precond),
                jnp.sum(precond * image),
                jnp.sum(image * scaled),
                jnp.sum(scaled * scaled_image),
            ]
        ),
        GX_GY,
    )
    gamma, delta, energy, curvature = sums[0], sums[1], sums[2], sums[3]
    alpha = gamma / delta
    gamma_next = alpha * alpha * energy - gamma
    ratio = gamma_next / gamma
    grow = 1.0 + ratio
    delta_next = grow * grow * delta - 2.0 * grow * alpha * energy + alpha * alpha * curvature
    alpha_next = gamma_next / delta_next
    solution = coarse_guess + alpha * precond
    residual = residual - alpha * image
    direction = residual * inverse + ratio * precond
    along = image - alpha * scaled_image + ratio * image
    solution = solution + alpha_next * direction
    residual = residual - alpha_next * along
    return (solution, residual)


def solution(mesh):
    split = Mesh(mesh.devices.reshape(4, 2, 4, 4), ("gx_0", "gx_1", "gy_0", "gy_1"))
    placed = (P(GX_GY, None), P(GX_GY, None), P(GX_GY), P(GX, GY, None), P(GX, GY, None))
    return jax.shard_map(
        body,
        mesh=split,
        in_specs=placed,
        out_specs=(P(GX, GY, None), P(GX, GY, None)),
        check_vma=False,
    )
```

```python
import jax
import jax.numpy as jnp
from jax import lax
from jax.sharding import Mesh
from jax.sharding import PartitionSpec as P
from jax.experimental import pallas as pl
from jax.experimental.pallas import tpu as pltpu

GX_GY = ("gx_0", "gx_1", "gy_0", "gy_1")
GX = ("gx_0", "gx_1")
GY = ("gy_0", "gy_1")


def shifted(piece, axis, pairs, dim):
    if dim == 1:
        flat = piece.reshape(piece.shape[0], piece.shape[2])
        return lax.ppermute(flat, axis, pairs).reshape(piece.shape)
    return lax.ppermute(piece, axis, pairs)


def extended(shard, sides, width):
    edges = {}
    for axis, dim in sides:
        count, length = (lax.axis_size(axis), shard.shape[dim])
        up = [(i, (i + 1) % count) for i in range(count - 1)]
        last = lax.slice_in_dim(shard, length - width, length, axis=dim)
        first = lax.slice_in_dim(shard, 0, width, axis=dim)
        edges[dim] = (
            shifted(last, axis, up, dim),
            shifted(first, axis, [(b, a) for a, b in up], dim),
        )
    done = []
    for _, dim in sides:
        low, high = edges[dim]
        around = [(width, width) if d in done else (0, 0) for d in range(shard.ndim)]
        shard = jnp.concatenate([jnp.pad(low, around), shard, jnp.pad(high, around)], axis=dim)
        done.append(dim)
    return shard


def over_axes(shard, axes):
    for axis in axes:
        shard = lax.psum(shard, axis)
    return shard


def with_halo(block, sides, width):
    for axis, dim in sides:
        count = lax.axis_size(axis)
        forward = [(i, i + 1) for i in range(count - 1)]
        backward = [(target, source) for source, target in forward]
        low = shifted(
            lax.slice_in_dim(block, block.shape[dim] - width, None, axis=dim), axis, forward, dim
        )
        high = shifted(lax.slice_in_dim(block, 0, width, axis=dim), axis, backward, dim)
        block = jnp.concatenate([low, block, high], axis=dim)
    return block


def build_send(bricks, brick_target, brick_slot, peers, capacity):
    target = brick_target[:, 0]
    onehot = (target[:, None] == jnp.arange(peers, dtype=jnp.int32)[None, :]).astype(jnp.int32)
    earlier = jnp.cumsum(onehot, axis=0) - onehot
    order = jnp.sum(earlier * onehot, axis=1)
    place = target * capacity + order
    high = (brick_slot // 32).astype(jnp.bfloat16)
    low = (brick_slot % 32).astype(jnp.bfloat16)
    tag = jnp.zeros((bricks.shape[0], 128), jnp.bfloat16).at[:, 0].set(high).at[:, 1].set(low)
    rows = jnp.concatenate([bricks, tag], axis=1)
    chosen = place[None, None, :] == (
        jnp.arange(peers, dtype=jnp.int32)[:, None, None] * capacity
        + jnp.arange(capacity, dtype=jnp.int32)[None, :, None]
    )
    payload = jnp.einsum(
        "pck,kj->pcj", chosen.astype(jnp.bfloat16), rows, preferred_element_type=jnp.float32
    )
    return payload.astype(jnp.bfloat16)


def next_along_z(field):
    edge = jnp.zeros(field.shape[:-1] + (1,), field.dtype)
    return jnp.concatenate([field[..., 1:], edge], axis=-1)


def prior_along_z(field):
    edge = jnp.zeros(field.shape[:-1] + (1,), field.dtype)
    return jnp.concatenate([edge, field[..., :-1]], axis=-1)


def operate(field, screen):
    padded = extended(field, ((GX, 0), (GY, 1)), 1)
    beside = padded[2:, 1:-1] + padded[:-2, 1:-1]
    beside = beside + padded[1:-1, 2:] + padded[1:-1, :-2]
    beside = beside + next_along_z(field) + prior_along_z(field)
    return (6.0 + screen) * field - beside


def component_grid(blocks, comp, span_x, span_y, span_z):
    part_blocks = blocks[:, comp, :].reshape(span_x, span_y, span_z, 8, 8, 8)
    grid = part_blocks.transpose(0, 3, 1, 4, 2, 5)
    return grid.reshape(span_x * 8, span_y * 8, span_z * 8)


def relayout_kernel(blk_ref, out_ref):
    sub = lax.broadcasted_iota(jnp.int32, (8, 128), 0)
    lane = lax.broadcasted_iota(jnp.int32, (8, 128), 1)
    grp = (lane // 8) % 8
    low_half = lane < 64
    swaps = []
    for m in (4, 2, 1):
        first = ((sub & m) == 0) & ((grp & m) != 0)
        second = ((sub & m) != 0) & ((grp & m) == 0)
        swaps.append((m, first, second))

    def transpose_groups(x):
        for m, first, second in swaps:
            a = pltpu.roll(pltpu.roll(x, 8 - m, 0), 8 * m, 1)
            b = pltpu.roll(pltpu.roll(x, m, 0), 128 - 8 * m, 1)
            x = jnp.where(first, a, jnp.where(second, b, x))
        return x

    def step(ly, carry):
        row = pl.multiple_of(ly * 16, 16)
        y = pl.multiple_of(ly * 8, 8)
        top = blk_ref[pl.ds(row, 8), :]
        bottom = blk_ref[pl.ds(row + 8, 8), :]
        for c in range(3):
            for uh in range(4):
                col = (c * 4 + uh) * 128
                s0 = top[:, col:col + 128]
                s1 = bottom[:, col:col + 128]
                u0 = jnp.where(low_half, s0, pltpu.roll(s1, 64, 1))
                u1 = jnp.where(low_half, pltpu.roll(s0, 64, 1), s1)
                out_ref[c, uh * 2, pl.ds(y, 8), :] = transpose_groups(u0)
                out_ref[c, uh * 2 + 1, pl.ds(y, 8), :] = transpose_groups(u1)
        return carry

    lax.fori_loop(0, 8, step, 0)


def to_grid(blocks, span_x, span_y, depth):
    cells = 3 * span_x * span_y * 64 * depth
    return pl.pallas_call(
        relayout_kernel,
        out_shape=jax.ShapeDtypeStruct((3, span_x * 8, span_y * 8, depth), jnp.float32),
        grid=(span_x,),
        in_specs=[pl.BlockSpec((span_y * 16, blocks.shape[1]), lambda i: (i, 0))],
        out_specs=pl.BlockSpec((3, 8, span_y * 8, depth), lambda i: (0, i, 0, 0)),
        cost_estimate=pl.CostEstimate(flops=20 * cells, bytes_accessed=8 * cells, transcendentals=0),
    )(blocks)


def body(bricks, brick_target, brick_slot, screen, coarse_guess):
    peers = lax.axis_size(GX_GY)
    capacity = max(2, 3 * bricks.shape[0] // peers)
    payload = build_send(bricks, brick_target, brick_slot, peers, capacity)
    arrived = lax.all_to_all(payload, GX_GY, split_axis=0, concat_axis=0, tiled=True)
    tag = arrived[:, :, 1536:1538].astype(jnp.int32)
    landed = tag[:, :, 0] * 32 + tag[:, :, 1]
    width_x, width_y, depth = screen.shape
    span_x = width_x // 8
    span_y = width_y // 8
    span_z = depth // 8
    picks = landed[:, :, None] == jnp.arange(span_x * span_y * span_z, dtype=jnp.int32)[None, None, :]
    blocks = jnp.einsum(
        "pcs,pcj->sj",
        picks.astype(jnp.bfloat16),
        arrived[:, :, :1536],
        preferred_element_type=jnp.float32,
    )
    normals = to_grid(blocks, span_x, span_y, depth)
    normal_x, normal_y, normal_z = normals[0], normals[1], normals[2]
    along_x = with_halo(normal_x, ((GX, 0),), 1)
    along_y = with_halo(normal_y, ((GY, 1),), 1)
    total = along_x[2:] - along_x[:-2]
    total = total + (along_y[:, 2:] - along_y[:, :-2])
    total = total + (next_along_z(normal_z) - prior_along_z(normal_z))
    source = -0.5 * total
    inverse = 1.0 / (6.0 + screen)
    residual = source - operate(coarse_guess, screen)
    precond = residual * inverse
    image = operate(precond, screen)
    scaled = image * inverse
    scaled_image = operate(scaled, screen)
    gamma, delta, energy, curvature = over_axes(
        (
            jnp.sum(residual * precond),
            jnp.sum(precond * image),
            jnp.sum(image * scaled),
            jnp.sum(scaled * scaled_image),
        ),
        GX_GY,
    )
    alpha = gamma / delta
    gamma_next = alpha * alpha * energy - gamma
    ratio = gamma_next / gamma
    grow = 1.0 + ratio
    delta_next = grow * grow * delta - 2.0 * grow * alpha * energy + alpha * alpha * curvature
    alpha_next = gamma_next / delta_next
    solution = coarse_guess + alpha * precond
    residual = residual - alpha * image
    direction = residual * inverse + ratio * precond
    along = image - alpha * scaled_image + ratio * image
    solution = solution + alpha_next * direction
    residual = residual - alpha_next * along
    return (solution, residual)


def solution(mesh):
    split = Mesh(mesh.devices.reshape(4, 2, 4, 4), ("gx_0", "gx_1", "gy_0", "gy_1"))
    placed = (P(GX_GY, None), P(GX_GY, None), P(GX_GY), P(GX, GY, None), P(GX, GY, None))
    return jax.shard_map(
        body,
        mesh=split,
        in_specs=placed,
        out_specs=(P(GX, GY, None), P(GX, GY, None)),
        check_vma=False,
    )
```

```python
import jax
import jax.numpy as jnp
from jax import lax
from jax.sharding import Mesh
from jax.sharding import PartitionSpec as P
from jax.experimental import pallas as pl
from jax.experimental.pallas import tpu as pltpu

GX_GY = ("gx_0", "gx_1", "gy_0", "gy_1")
GX = ("gx_0", "gx_1")
GY = ("gy_0", "gy_1")


def shifted(piece, axis, pairs, dim):
    if dim == 1:
        flat = piece.reshape(piece.shape[0], piece.shape[2])
        return lax.ppermute(flat, axis, pairs).reshape(piece.shape)
    return lax.ppermute(piece, axis, pairs)


def extended(shard, sides, width):
    edges = {}
    for axis, dim in sides:
        count, length = (lax.axis_size(axis), shard.shape[dim])
        up = [(i, (i + 1) % count) for i in range(count - 1)]
        last = lax.slice_in_dim(shard, length - width, length, axis=dim)
        first = lax.slice_in_dim(shard, 0, width, axis=dim)
        edges[dim] = (
            shifted(last, axis, up, dim),
            shifted(first, axis, [(b, a) for a, b in up], dim),
        )
    done = []
    for _, dim in sides:
        low, high = edges[dim]
        around = [(width, width) if d in done else (0, 0) for d in range(shard.ndim)]
        shard = jnp.concatenate([jnp.pad(low, around), shard, jnp.pad(high, around)], axis=dim)
        done.append(dim)
    return shard


def over_axes(shard, axes):
    for axis in axes:
        shard = lax.psum(shard, axis)
    return shard


def with_halo(block, sides, width):
    for axis, dim in sides:
        count = lax.axis_size(axis)
        forward = [(i, i + 1) for i in range(count - 1)]
        backward = [(target, source) for source, target in forward]
        low = shifted(
            lax.slice_in_dim(block, block.shape[dim] - width, None, axis=dim), axis, forward, dim
        )
        high = shifted(lax.slice_in_dim(block, 0, width, axis=dim), axis, backward, dim)
        block = jnp.concatenate([low, block, high], axis=dim)
    return block


def build_send(bricks, brick_target, brick_slot, peers, capacity):
    target = brick_target[:, 0]
    onehot = (target[:, None] == jnp.arange(peers, dtype=jnp.int32)[None, :]).astype(jnp.int32)
    earlier = jnp.cumsum(onehot, axis=0) - onehot
    order = jnp.sum(earlier * onehot, axis=1)
    place = target * capacity + order
    high = (brick_slot // 32).astype(jnp.bfloat16)
    low = (brick_slot % 32).astype(jnp.bfloat16)
    tag = jnp.zeros((bricks.shape[0], 128), jnp.bfloat16).at[:, 0].set(high).at[:, 1].set(low)
    rows = jnp.concatenate([bricks, tag], axis=1)
    chosen = place[None, None, :] == (
        jnp.arange(peers, dtype=jnp.int32)[:, None, None] * capacity
        + jnp.arange(capacity, dtype=jnp.int32)[None, :, None]
    )
    payload = jnp.einsum(
        "pck,kj->pcj", chosen.astype(jnp.bfloat16), rows, preferred_element_type=jnp.float32
    )
    return payload.astype(jnp.bfloat16)


def next_along_z(field):
    edge = jnp.zeros(field.shape[:-1] + (1,), field.dtype)
    return jnp.concatenate([field[..., 1:], edge], axis=-1)


def prior_along_z(field):
    edge = jnp.zeros(field.shape[:-1] + (1,), field.dtype)
    return jnp.concatenate([edge, field[..., :-1]], axis=-1)


def operate(field, screen):
    padded = extended(field, ((GX, 0), (GY, 1)), 1)
    beside = padded[2:, 1:-1] + padded[:-2, 1:-1]
    beside = beside + padded[1:-1, 2:] + padded[1:-1, :-2]
    beside = beside + next_along_z(field) + prior_along_z(field)
    return (6.0 + screen) * field - beside


def component_grid(blocks, comp, span_x, span_y, span_z):
    part_blocks = blocks[:, comp, :].reshape(span_x, span_y, span_z, 8, 8, 8)
    grid = part_blocks.transpose(0, 3, 1, 4, 2, 5)
    return grid.reshape(span_x * 8, span_y * 8, span_z * 8)


def relayout_kernel(blk_ref, out_ref):
    sub = lax.broadcasted_iota(jnp.int32, (8, 128), 0)
    lane = lax.broadcasted_iota(jnp.int32, (8, 128), 1)
    grp = (lane // 8) % 8
    low_half = lane < 64
    swaps = []
    for m in (4, 2, 1):
        first = ((sub & m) == 0) & ((grp & m) != 0)
        second = ((sub & m) != 0) & ((grp & m) == 0)
        swaps.append((m, first, second))

    def transpose_groups(x):
        for m, first, second in swaps:
            down = pltpu.roll(x, 8 - m, 0)
            up = down if m == 4 else pltpu.roll(x, m, 0)
            a = pltpu.roll(down, 8 * m, 1)
            b = pltpu.roll(up, 128 - 8 * m, 1)
            x = jnp.where(first, a, jnp.where(second, b, x))
        return x

    def step(ly, carry):
        row = pl.multiple_of(ly * 16, 16)
        y = pl.multiple_of(ly * 8, 8)
        top = blk_ref[pl.ds(row, 8), :]
        bottom = blk_ref[pl.ds(row + 8, 8), :]
        for c in range(3):
            for uh in range(4):
                col = (c * 4 + uh) * 128
                s0 = top[:, col:col + 128]
                s1 = bottom[:, col:col + 128]
                u0 = jnp.where(low_half, s0, pltpu.roll(s1, 64, 1))
                u1 = jnp.where(low_half, pltpu.roll(s0, 64, 1), s1)
                out_ref[c, uh * 2, pl.ds(y, 8), :] = transpose_groups(u0)
                out_ref[c, uh * 2 + 1, pl.ds(y, 8), :] = transpose_groups(u1)
        return carry

    lax.fori_loop(0, 8, step, 0)


def to_grid(blocks, span_x, span_y, depth):
    cells = 3 * span_x * span_y * 64 * depth
    return pl.pallas_call(
        relayout_kernel,
        out_shape=jax.ShapeDtypeStruct((3, span_x * 8, span_y * 8, depth), jnp.float32),
        grid=(span_x,),
        in_specs=[pl.BlockSpec((span_y * 16, blocks.shape[1]), lambda i: (i, 0))],
        out_specs=pl.BlockSpec((3, 8, span_y * 8, depth), lambda i: (0, i, 0, 0)),
        cost_estimate=pl.CostEstimate(flops=20 * cells, bytes_accessed=8 * cells, transcendentals=0),
    )(blocks)


def body(bricks, brick_target, brick_slot, screen, coarse_guess):
    peers = lax.axis_size(GX_GY)
    capacity = max(2, 3 * bricks.shape[0] // peers)
    payload = build_send(bricks, brick_target, brick_slot, peers, capacity)
    arrived = lax.all_to_all(payload, GX_GY, split_axis=0, concat_axis=0, tiled=True)
    tag = arrived[:, :, 1536:1538].astype(jnp.int32)
    landed = tag[:, :, 0] * 32 + tag[:, :, 1]
    width_x, width_y, depth = screen.shape
    span_x = width_x // 8
    span_y = width_y // 8
    span_z = depth // 8
    picks = landed[:, :, None] == jnp.arange(span_x * span_y * span_z, dtype=jnp.int32)[None, None, :]
    blocks = jnp.einsum(
        "pcs,pcj->sj",
        picks.astype(jnp.bfloat16),
        arrived[:, :, :1536],
        preferred_element_type=jnp.float32,
    )
    normals = to_grid(blocks, span_x, span_y, depth)
    normal_x, normal_y, normal_z = normals[0], normals[1], normals[2]
    along_x = with_halo(normal_x, ((GX, 0),), 1)
    along_y = with_halo(normal_y, ((GY, 1),), 1)
    total = along_x[2:] - along_x[:-2]
    total = total + (along_y[:, 2:] - along_y[:, :-2])
    total = total + (next_along_z(normal_z) - prior_along_z(normal_z))
    source = -0.5 * total
    inverse = 1.0 / (6.0 + screen)
    residual = source - operate(coarse_guess, screen)
    precond = residual * inverse
    image = operate(precond, screen)
    scaled = image * inverse
    scaled_image = operate(scaled, screen)
    sums = over_axes(
        jnp.stack(
            [
                jnp.sum(residual * precond),
                jnp.sum(precond * image),
                jnp.sum(image * scaled),
                jnp.sum(scaled * scaled_image),
            ]
        ),
        GX_GY,
    )
    gamma, delta, energy, curvature = sums[0], sums[1], sums[2], sums[3]
    alpha = gamma / delta
    gamma_next = alpha * alpha * energy - gamma
    ratio = gamma_next / gamma
    grow = 1.0 + ratio
    delta_next = grow * grow * delta - 2.0 * grow * alpha * energy + alpha * alpha * curvature
    alpha_next = gamma_next / delta_next
    solution = coarse_guess + alpha * precond
    residual = residual - alpha * image
    direction = residual * inverse + ratio * precond
    along = image - alpha * scaled_image + ratio * image
    solution = solution + alpha_next * direction
    residual = residual - alpha_next * along
    return (solution, residual)


def solution(mesh):
    split = Mesh(mesh.devices.reshape(4, 2, 4, 4), ("gx_0", "gx_1", "gy_0", "gy_1"))
    placed = (P(GX_GY, None), P(GX_GY, None), P(GX_GY), P(GX, GY, None), P(GX, GY, None))
    return jax.shard_map(
        body,
        mesh=split,
        in_specs=placed,
        out_specs=(P(GX, GY, None), P(GX, GY, None)),
        check_vma=False,
    )
```

```python
import jax
import jax.numpy as jnp
from jax import lax
from jax.sharding import Mesh
from jax.sharding import PartitionSpec as P
from jax.experimental import pallas as pl
from jax.experimental.pallas import tpu as pltpu

GX_GY = ("gx_0", "gx_1", "gy_0", "gy_1")
GX = ("gx_0", "gx_1")
GY = ("gy_0", "gy_1")


def shifted(piece, axis, pairs, dim):
    if dim == 1:
        flat = piece.reshape(piece.shape[0], piece.shape[2])
        return lax.ppermute(flat, axis, pairs).reshape(piece.shape)
    return lax.ppermute(piece, axis, pairs)


def extended(shard, sides, width):
    edges = {}
    for axis, dim in sides:
        count, length = (lax.axis_size(axis), shard.shape[dim])
        up = [(i, (i + 1) % count) for i in range(count - 1)]
        last = lax.slice_in_dim(shard, length - width, length, axis=dim)
        first = lax.slice_in_dim(shard, 0, width, axis=dim)
        edges[dim] = (
            shifted(last, axis, up, dim),
            shifted(first, axis, [(b, a) for a, b in up], dim),
        )
    done = []
    for _, dim in sides:
        low, high = edges[dim]
        around = [(width, width) if d in done else (0, 0) for d in range(shard.ndim)]
        shard = jnp.concatenate([jnp.pad(low, around), shard, jnp.pad(high, around)], axis=dim)
        done.append(dim)
    return shard


def over_axes(shard, axes):
    for axis in axes:
        shard = lax.psum(shard, axis)
    return shard


def with_halo(block, sides, width):
    for axis, dim in sides:
        count = lax.axis_size(axis)
        forward = [(i, i + 1) for i in range(count - 1)]
        backward = [(target, source) for source, target in forward]
        low = shifted(
            lax.slice_in_dim(block, block.shape[dim] - width, None, axis=dim), axis, forward, dim
        )
        high = shifted(lax.slice_in_dim(block, 0, width, axis=dim), axis, backward, dim)
        block = jnp.concatenate([low, block, high], axis=dim)
    return block


def build_send(bricks, brick_target, brick_slot, peers, capacity):
    target = brick_target[:, 0]
    onehot = (target[:, None] == jnp.arange(peers, dtype=jnp.int32)[None, :]).astype(jnp.int32)
    earlier = jnp.cumsum(onehot, axis=0) - onehot
    order = jnp.sum(earlier * onehot, axis=1)
    place = target * capacity + order
    high = (brick_slot // 32).astype(jnp.bfloat16)
    low = (brick_slot % 32).astype(jnp.bfloat16)
    tag = jnp.zeros((bricks.shape[0], 128), jnp.bfloat16).at[:, 0].set(high).at[:, 1].set(low)
    rows = jnp.concatenate([bricks, tag], axis=1)
    chosen = place[None, None, :] == (
        jnp.arange(peers, dtype=jnp.int32)[:, None, None] * capacity
        + jnp.arange(capacity, dtype=jnp.int32)[None, :, None]
    )
    payload = jnp.einsum(
        "pck,kj->pcj", chosen.astype(jnp.bfloat16), rows, preferred_element_type=jnp.float32
    )
    return payload.astype(jnp.bfloat16)


def next_along_z(field):
    edge = jnp.zeros(field.shape[:-1] + (1,), field.dtype)
    return jnp.concatenate([field[..., 1:], edge], axis=-1)


def prior_along_z(field):
    edge = jnp.zeros(field.shape[:-1] + (1,), field.dtype)
    return jnp.concatenate([edge, field[..., :-1]], axis=-1)


def operate(field, screen):
    padded = extended(field, ((GX, 0), (GY, 1)), 1)
    beside = padded[2:, 1:-1] + padded[:-2, 1:-1]
    beside = beside + padded[1:-1, 2:] + padded[1:-1, :-2]
    beside = beside + next_along_z(field) + prior_along_z(field)
    return (6.0 + screen) * field - beside


def component_grid(blocks, comp, span_x, span_y, span_z):
    part_blocks = blocks[:, comp, :].reshape(span_x, span_y, span_z, 8, 8, 8)
    grid = part_blocks.transpose(0, 3, 1, 4, 2, 5)
    return grid.reshape(span_x * 8, span_y * 8, span_z * 8)


def relayout_kernel(blk_ref, out_ref):
    sub = lax.broadcasted_iota(jnp.int32, (8, 128), 0)
    lane = lax.broadcasted_iota(jnp.int32, (8, 128), 1)
    grp = (lane // 8) % 8
    low_half = lane < 64
    swaps = []
    for m in (4, 2, 1):
        first = ((sub & m) == 0) & ((grp & m) != 0)
        second = ((sub & m) != 0) & ((grp & m) == 0)
        swaps.append((m, first, second))

    def transpose_groups(x):
        for m, first, second in swaps:
            down = pltpu.roll(x, 8 - m, 0)
            up = down if m == 4 else pltpu.roll(x, m, 0)
            a = pltpu.roll(down, 8 * m, 1)
            b = pltpu.roll(up, 128 - 8 * m, 1)
            x = jnp.where(first, a, jnp.where(second, b, x))
        return x

    def step(i, carry):
        ly = i // 3
        c = i % 3
        row = pl.multiple_of(ly * 16, 16)
        y = pl.multiple_of(ly * 8, 8)
        col = pl.multiple_of(c * 512, 512)
        top = blk_ref[pl.ds(row, 8), pl.ds(col, 512)]
        bottom = blk_ref[pl.ds(row + 8, 8), pl.ds(col, 512)]
        for uh in range(4):
            s0 = top[:, uh * 128:(uh + 1) * 128]
            s1 = bottom[:, uh * 128:(uh + 1) * 128]
            u0 = jnp.where(low_half, s0, pltpu.roll(s1, 64, 1))
            u1 = jnp.where(low_half, pltpu.roll(s0, 64, 1), s1)
            out_ref[c, uh * 2, pl.ds(y, 8), :] = transpose_groups(u0)
            out_ref[c, uh * 2 + 1, pl.ds(y, 8), :] = transpose_groups(u1)
        return carry

    lax.fori_loop(0, 24, step, 0)


def to_grid(blocks, span_x, span_y, depth):
    cells = 3 * span_x * span_y * 64 * depth
    return pl.pallas_call(
        relayout_kernel,
        out_shape=jax.ShapeDtypeStruct((3, span_x * 8, span_y * 8, depth), jnp.float32),
        grid=(span_x,),
        in_specs=[pl.BlockSpec((span_y * 16, blocks.shape[1]), lambda i: (i, 0))],
        out_specs=pl.BlockSpec((3, 8, span_y * 8, depth), lambda i: (0, i, 0, 0)),
        cost_estimate=pl.CostEstimate(flops=20 * cells, bytes_accessed=8 * cells, transcendentals=0),
    )(blocks)


def body(bricks, brick_target, brick_slot, screen, coarse_guess):
    peers = lax.axis_size(GX_GY)
    capacity = max(2, 3 * bricks.shape[0] // peers)
    payload = build_send(bricks, brick_target, brick_slot, peers, capacity)
    arrived = lax.all_to_all(payload, GX_GY, split_axis=0, concat_axis=0, tiled=True)
    tag = arrived[:, :, 1536:1538].astype(jnp.int32)
    landed = tag[:, :, 0] * 32 + tag[:, :, 1]
    width_x, width_y, depth = screen.shape
    span_x = width_x // 8
    span_y = width_y // 8
    span_z = depth // 8
    picks = landed[:, :, None] == jnp.arange(span_x * span_y * span_z, dtype=jnp.int32)[None, None, :]
    blocks = jnp.einsum(
        "pcs,pcj->sj",
        picks.astype(jnp.bfloat16),
        arrived[:, :, :1536],
        preferred_element_type=jnp.float32,
    )
    normals = to_grid(blocks, span_x, span_y, depth)
    normal_x, normal_y, normal_z = normals[0], normals[1], normals[2]
    along_x = with_halo(normal_x, ((GX, 0),), 1)
    along_y = with_halo(normal_y, ((GY, 1),), 1)
    total = along_x[2:] - along_x[:-2]
    total = total + (along_y[:, 2:] - along_y[:, :-2])
    total = total + (next_along_z(normal_z) - prior_along_z(normal_z))
    source = -0.5 * total
    inverse = 1.0 / (6.0 + screen)
    residual = source - operate(coarse_guess, screen)
    precond = residual * inverse
    image = operate(precond, screen)
    scaled = image * inverse
    scaled_image = operate(scaled, screen)
    sums = over_axes(
        jnp.stack(
            [
                jnp.sum(residual * precond),
                jnp.sum(precond * image),
                jnp.sum(image * scaled),
                jnp.sum(scaled * scaled_image),
            ]
        ),
        GX_GY,
    )
    gamma, delta, energy, curvature = sums[0], sums[1], sums[2], sums[3]
    alpha = gamma / delta
    gamma_next = alpha * alpha * energy - gamma
    ratio = gamma_next / gamma
    grow = 1.0 + ratio
    delta_next = grow * grow * delta - 2.0 * grow * alpha * energy + alpha * alpha * curvature
    alpha_next = gamma_next / delta_next
    solution = coarse_guess + alpha * precond
    residual = residual - alpha * image
    direction = residual * inverse + ratio * precond
    along = image - alpha * scaled_image + ratio * image
    solution = solution + alpha_next * direction
    residual = residual - alpha_next * along
    return (solution, residual)


def solution(mesh):
    split = Mesh(mesh.devices.reshape(4, 2, 4, 4), ("gx_0", "gx_1", "gy_0", "gy_1"))
    placed = (P(GX_GY, None), P(GX_GY, None), P(GX_GY), P(GX, GY, None), P(GX, GY, None))
    return jax.shard_map(
        body,
        mesh=split,
        in_specs=placed,
        out_specs=(P(GX, GY, None), P(GX, GY, None)),
        check_vma=False,
    )
```

```python
import jax
import jax.numpy as jnp
from jax import lax
from jax.sharding import Mesh
from jax.sharding import PartitionSpec as P
from jax.experimental import pallas as pl
from jax.experimental.pallas import tpu as pltpu

GX_GY = ("gx_0", "gx_1", "gy_0", "gy_1")
GX = ("gx_0", "gx_1")
GY = ("gy_0", "gy_1")


def shifted(piece, axis, pairs, dim):
    if dim == 1:
        flat = piece.reshape(piece.shape[0], piece.shape[2])
        return lax.ppermute(flat, axis, pairs).reshape(piece.shape)
    return lax.ppermute(piece, axis, pairs)


def extended(shard, sides, width):
    edges = {}
    for axis, dim in sides:
        count, length = (lax.axis_size(axis), shard.shape[dim])
        up = [(i, (i + 1) % count) for i in range(count - 1)]
        last = lax.slice_in_dim(shard, length - width, length, axis=dim)
        first = lax.slice_in_dim(shard, 0, width, axis=dim)
        edges[dim] = (
            shifted(last, axis, up, dim),
            shifted(first, axis, [(b, a) for a, b in up], dim),
        )
    done = []
    for _, dim in sides:
        low, high = edges[dim]
        around = [(width, width) if d in done else (0, 0) for d in range(shard.ndim)]
        shard = jnp.concatenate([jnp.pad(low, around), shard, jnp.pad(high, around)], axis=dim)
        done.append(dim)
    return shard


def over_axes(shard, axes):
    for axis in axes:
        shard = lax.psum(shard, axis)
    return shard


def with_halo(block, sides, width):
    for axis, dim in sides:
        count = lax.axis_size(axis)
        forward = [(i, i + 1) for i in range(count - 1)]
        backward = [(target, source) for source, target in forward]
        low = shifted(
            lax.slice_in_dim(block, block.shape[dim] - width, None, axis=dim), axis, forward, dim
        )
        high = shifted(lax.slice_in_dim(block, 0, width, axis=dim), axis, backward, dim)
        block = jnp.concatenate([low, block, high], axis=dim)
    return block


def build_send(bricks, brick_target, brick_slot, peers, capacity):
    target = brick_target[:, 0]
    onehot = (target[:, None] == jnp.arange(peers, dtype=jnp.int32)[None, :]).astype(jnp.int32)
    earlier = jnp.cumsum(onehot, axis=0) - onehot
    order = jnp.sum(earlier * onehot, axis=1)
    place = target * capacity + order
    high = (brick_slot // 32).astype(jnp.bfloat16)
    low = (brick_slot % 32).astype(jnp.bfloat16)
    tag = jnp.zeros((bricks.shape[0], 128), jnp.bfloat16).at[:, 0].set(high).at[:, 1].set(low)
    rows = jnp.concatenate([bricks, tag], axis=1)
    chosen = place[None, None, :] == (
        jnp.arange(peers, dtype=jnp.int32)[:, None, None] * capacity
        + jnp.arange(capacity, dtype=jnp.int32)[None, :, None]
    )
    payload = jnp.einsum(
        "pck,kj->pcj", chosen.astype(jnp.bfloat16), rows, preferred_element_type=jnp.float32
    )
    return payload.astype(jnp.bfloat16)


def next_along_z(field):
    edge = jnp.zeros(field.shape[:-1] + (1,), field.dtype)
    return jnp.concatenate([field[..., 1:], edge], axis=-1)


def prior_along_z(field):
    edge = jnp.zeros(field.shape[:-1] + (1,), field.dtype)
    return jnp.concatenate([edge, field[..., :-1]], axis=-1)


def operate(field, screen):
    padded = extended(field, ((GX, 0), (GY, 1)), 1)
    beside = padded[2:, 1:-1] + padded[:-2, 1:-1]
    beside = beside + padded[1:-1, 2:] + padded[1:-1, :-2]
    beside = beside + next_along_z(field) + prior_along_z(field)
    return (6.0 + screen) * field - beside


def component_grid(blocks, comp, span_x, span_y, span_z):
    part_blocks = blocks[:, comp, :].reshape(span_x, span_y, span_z, 8, 8, 8)
    grid = part_blocks.transpose(0, 3, 1, 4, 2, 5)
    return grid.reshape(span_x * 8, span_y * 8, span_z * 8)


def relayout_kernel(blk_ref, out_ref):
    sub = lax.broadcasted_iota(jnp.int32, (8, 128), 0)
    lane = lax.broadcasted_iota(jnp.int32, (8, 128), 1)
    grp = (lane // 8) % 8
    low_half = lane < 64
    swaps = []
    for m in (4, 2, 1):
        first = ((sub & m) == 0) & ((grp & m) != 0)
        second = ((sub & m) != 0) & ((grp & m) == 0)
        swaps.append((m, first, second))

    def transpose_groups(x):
        for m, first, second in swaps:
            down = pltpu.roll(x, 8 - m, 0)
            up = down if m == 4 else pltpu.roll(x, m, 0)
            a = pltpu.roll(down, 8 * m, 1)
            b = pltpu.roll(up, 128 - 8 * m, 1)
            x = jnp.where(first, a, jnp.where(second, b, x))
        return x

    def step(ly, carry):
        row = pl.multiple_of(ly * 16, 16)
        y = pl.multiple_of(ly * 8, 8)
        top = blk_ref[pl.ds(row, 8), :]
        bottom = blk_ref[pl.ds(row + 8, 8), :]
        for c in range(3):
            for uh in range(4):
                col = (c * 4 + uh) * 128
                s0 = top[:, col:col + 128]
                s1 = bottom[:, col:col + 128]
                u0 = jnp.where(low_half, s0, pltpu.roll(s1, 64, 1))
                u1 = jnp.where(low_half, pltpu.roll(s0, 64, 1), s1)
                out_ref[c, uh * 2, pl.ds(y, 8), :] = transpose_groups(u0)
                out_ref[c, uh * 2 + 1, pl.ds(y, 8), :] = transpose_groups(u1)
        return carry

    lax.fori_loop(0, 8, step, 0, unroll=2)


def to_grid(blocks, span_x, span_y, depth):
    cells = 3 * span_x * span_y * 64 * depth
    return pl.pallas_call(
        relayout_kernel,
        out_shape=jax.ShapeDtypeStruct((3, span_x * 8, span_y * 8, depth), jnp.float32),
        grid=(span_x,),
        in_specs=[pl.BlockSpec((span_y * 16, blocks.shape[1]), lambda i: (i, 0))],
        out_specs=pl.BlockSpec((3, 8, span_y * 8, depth), lambda i: (0, i, 0, 0)),
        cost_estimate=pl.CostEstimate(flops=20 * cells, bytes_accessed=8 * cells, transcendentals=0),
    )(blocks)


def body(bricks, brick_target, brick_slot, screen, coarse_guess):
    peers = lax.axis_size(GX_GY)
    capacity = max(2, 3 * bricks.shape[0] // peers)
    payload = build_send(bricks, brick_target, brick_slot, peers, capacity)
    arrived = lax.all_to_all(payload, GX_GY, split_axis=0, concat_axis=0, tiled=True)
    tag = arrived[:, :, 1536:1538].astype(jnp.int32)
    landed = tag[:, :, 0] * 32 + tag[:, :, 1]
    width_x, width_y, depth = screen.shape
    span_x = width_x // 8
    span_y = width_y // 8
    span_z = depth // 8
    picks = landed[:, :, None] == jnp.arange(span_x * span_y * span_z, dtype=jnp.int32)[None, None, :]
    blocks = jnp.einsum(
        "pcs,pcj->sj",
        picks.astype(jnp.bfloat16),
        arrived[:, :, :1536],
        preferred_element_type=jnp.float32,
    )
    normals = to_grid(blocks, span_x, span_y, depth)
    normal_x, normal_y, normal_z = normals[0], normals[1], normals[2]
    along_x = with_halo(normal_x, ((GX, 0),), 1)
    along_y = with_halo(normal_y, ((GY, 1),), 1)
    total = along_x[2:] - along_x[:-2]
    total = total + (along_y[:, 2:] - along_y[:, :-2])
    total = total + (next_along_z(normal_z) - prior_along_z(normal_z))
    source = -0.5 * total
    inverse = 1.0 / (6.0 + screen)
    residual = source - operate(coarse_guess, screen)
    precond = residual * inverse
    image = operate(precond, screen)
    scaled = image * inverse
    scaled_image = operate(scaled, screen)
    sums = over_axes(
        jnp.stack(
            [
                jnp.sum(residual * precond),
                jnp.sum(precond * image),
                jnp.sum(image * scaled),
                jnp.sum(scaled * scaled_image),
            ]
        ),
        GX_GY,
    )
    gamma, delta, energy, curvature = sums[0], sums[1], sums[2], sums[3]
    alpha = gamma / delta
    gamma_next = alpha * alpha * energy - gamma
    ratio = gamma_next / gamma
    grow = 1.0 + ratio
    delta_next = grow * grow * delta - 2.0 * grow * alpha * energy + alpha * alpha * curvature
    alpha_next = gamma_next / delta_next
    solution = coarse_guess + alpha * precond
    residual = residual - alpha * image
    direction = residual * inverse + ratio * precond
    along = image - alpha * scaled_image + ratio * image
    solution = solution + alpha_next * direction
    residual = residual - alpha_next * along
    return (solution, residual)


def solution(mesh):
    split = Mesh(mesh.devices.reshape(4, 2, 4, 4), ("gx_0", "gx_1", "gy_0", "gy_1"))
    placed = (P(GX_GY, None), P(GX_GY, None), P(GX_GY), P(GX, GY, None), P(GX, GY, None))
    return jax.shard_map(
        body,
        mesh=split,
        in_specs=placed,
        out_specs=(P(GX, GY, None), P(GX, GY, None)),
        check_vma=False,
    )
```

```python
import jax
import jax.numpy as jnp
from jax import lax
from jax.sharding import Mesh
from jax.sharding import PartitionSpec as P
from jax.experimental import pallas as pl
from jax.experimental.pallas import tpu as pltpu

GX_GY = ("gx_0", "gx_1", "gy_0", "gy_1")
GX = ("gx_0", "gx_1")
GY = ("gy_0", "gy_1")


def shifted(piece, axis, pairs, dim):
    if dim == 1:
        flat = piece.reshape(piece.shape[0], piece.shape[2])
        return lax.ppermute(flat, axis, pairs).reshape(piece.shape)
    return lax.ppermute(piece, axis, pairs)


def extended(shard, sides, width):
    edges = {}
    for axis, dim in sides:
        count, length = (lax.axis_size(axis), shard.shape[dim])
        up = [(i, (i + 1) % count) for i in range(count - 1)]
        last = lax.slice_in_dim(shard, length - width, length, axis=dim)
        first = lax.slice_in_dim(shard, 0, width, axis=dim)
        edges[dim] = (
            shifted(last, axis, up, dim),
            shifted(first, axis, [(b, a) for a, b in up], dim),
        )
    done = []
    for _, dim in sides:
        low, high = edges[dim]
        around = [(width, width) if d in done else (0, 0) for d in range(shard.ndim)]
        shard = jnp.concatenate([jnp.pad(low, around), shard, jnp.pad(high, around)], axis=dim)
        done.append(dim)
    return shard


def over_axes(shard, axes):
    for axis in axes:
        shard = lax.psum(shard, axis)
    return shard


def with_halo(block, sides, width):
    for axis, dim in sides:
        count = lax.axis_size(axis)
        forward = [(i, i + 1) for i in range(count - 1)]
        backward = [(target, source) for source, target in forward]
        low = shifted(
            lax.slice_in_dim(block, block.shape[dim] - width, None, axis=dim), axis, forward, dim
        )
        high = shifted(lax.slice_in_dim(block, 0, width, axis=dim), axis, backward, dim)
        block = jnp.concatenate([low, block, high], axis=dim)
    return block


def build_send(bricks, brick_target, brick_slot, peers, capacity):
    target = brick_target[:, 0]
    onehot = (target[:, None] == jnp.arange(peers, dtype=jnp.int32)[None, :]).astype(jnp.int32)
    earlier = jnp.cumsum(onehot, axis=0) - onehot
    order = jnp.sum(earlier * onehot, axis=1)
    place = target * capacity + order
    high = lax.shift_right_logical(brick_slot, 5).astype(jnp.bfloat16)
    low = (brick_slot & 31).astype(jnp.bfloat16)
    tag = jnp.zeros((bricks.shape[0], 128), jnp.bfloat16).at[:, 0].set(high).at[:, 1].set(low)
    rows = jnp.concatenate([bricks, tag], axis=1)
    chosen = place[None, None, :] == (
        jnp.arange(peers, dtype=jnp.int32)[:, None, None] * capacity
        + jnp.arange(capacity, dtype=jnp.int32)[None, :, None]
    )
    payload = jnp.einsum(
        "pck,kj->pcj", chosen.astype(jnp.bfloat16), rows, preferred_element_type=jnp.float32
    )
    return payload.astype(jnp.bfloat16)


def next_along_z(field):
    edge = jnp.zeros(field.shape[:-1] + (1,), field.dtype)
    return jnp.concatenate([field[..., 1:], edge], axis=-1)


def prior_along_z(field):
    edge = jnp.zeros(field.shape[:-1] + (1,), field.dtype)
    return jnp.concatenate([edge, field[..., :-1]], axis=-1)


def operate(field, screen):
    padded = extended(field, ((GX, 0), (GY, 1)), 1)
    beside = padded[2:, 1:-1] + padded[:-2, 1:-1]
    beside = beside + padded[1:-1, 2:] + padded[1:-1, :-2]
    beside = beside + next_along_z(field) + prior_along_z(field)
    return (6.0 + screen) * field - beside


def component_grid(blocks, comp, span_x, span_y, span_z):
    part_blocks = blocks[:, comp, :].reshape(span_x, span_y, span_z, 8, 8, 8)
    grid = part_blocks.transpose(0, 3, 1, 4, 2, 5)
    return grid.reshape(span_x * 8, span_y * 8, span_z * 8)


def relayout_kernel(blk_ref, out_ref):
    sub = lax.broadcasted_iota(jnp.int32, (8, 128), 0)
    lane = lax.broadcasted_iota(jnp.int32, (8, 128), 1)
    grp = (lane // 8) % 8
    low_half = lane < 64
    swaps = []
    for m in (4, 2, 1):
        first = ((sub & m) == 0) & ((grp & m) != 0)
        second = ((sub & m) != 0) & ((grp & m) == 0)
        swaps.append((m, first, second))

    def transpose_groups(x):
        for m, first, second in swaps:
            a = pltpu.roll(pltpu.roll(x, 8 - m, 0), 8 * m, 1)
            b = pltpu.roll(pltpu.roll(x, m, 0), 128 - 8 * m, 1)
            x = jnp.where(first, a, jnp.where(second, b, x))
        return x

    def step(ly, carry):
        row = pl.multiple_of(ly * 16, 16)
        y = pl.multiple_of(ly * 8, 8)
        top = blk_ref[pl.ds(row, 8), :]
        bottom = blk_ref[pl.ds(row + 8, 8), :]
        for c in range(3):
            for uh in range(4):
                col = (c * 4 + uh) * 128
                s0 = top[:, col:col + 128]
                s1 = bottom[:, col:col + 128]
                u0 = jnp.where(low_half, s0, pltpu.roll(s1, 64, 1))
                u1 = jnp.where(low_half, pltpu.roll(s0, 64, 1), s1)
                out_ref[c, uh * 2, pl.ds(y, 8), :] = transpose_groups(u0)
                out_ref[c, uh * 2 + 1, pl.ds(y, 8), :] = transpose_groups(u1)
        return carry

    lax.fori_loop(0, 8, step, 0)


def to_grid(blocks, span_x, span_y, depth):
    cells = 3 * span_x * span_y * 64 * depth
    return pl.pallas_call(
        relayout_kernel,
        out_shape=jax.ShapeDtypeStruct((3, span_x * 8, span_y * 8, depth), jnp.float32),
        grid=(span_x,),
        in_specs=[pl.BlockSpec((span_y * 16, blocks.shape[1]), lambda i: (i, 0))],
        out_specs=pl.BlockSpec((3, 8, span_y * 8, depth), lambda i: (0, i, 0, 0)),
        cost_estimate=pl.CostEstimate(flops=20 * cells, bytes_accessed=8 * cells, transcendentals=0),
    )(blocks)


def body(bricks, brick_target, brick_slot, screen, coarse_guess):
    peers = lax.axis_size(GX_GY)
    capacity = max(2, 3 * bricks.shape[0] // peers)
    payload = build_send(bricks, brick_target, brick_slot, peers, capacity)
    arrived = lax.all_to_all(payload, GX_GY, split_axis=0, concat_axis=0, tiled=True)
    tag = arrived[:, :, 1536:1538].astype(jnp.int32)
    landed = tag[:, :, 0] * 32 + tag[:, :, 1]
    width_x, width_y, depth = screen.shape
    span_x = width_x // 8
    span_y = width_y // 8
    span_z = depth // 8
    picks = landed[:, :, None] == jnp.arange(span_x * span_y * span_z, dtype=jnp.int32)[None, None, :]
    blocks = jnp.einsum(
        "pcs,pcj->sj",
        picks.astype(jnp.bfloat16),
        arrived[:, :, :1536],
        preferred_element_type=jnp.float32,
    )
    normals = to_grid(blocks, span_x, span_y, depth)
    normal_x, normal_y, normal_z = normals[0], normals[1], normals[2]
    along_x = with_halo(normal_x, ((GX, 0),), 1)
    along_y = with_halo(normal_y, ((GY, 1),), 1)
    total = along_x[2:] - along_x[:-2]
    total = total + (along_y[:, 2:] - along_y[:, :-2])
    total = total + (next_along_z(normal_z) - prior_along_z(normal_z))
    source = -0.5 * total
    inverse = 1.0 / (6.0 + screen)
    residual = source - operate(coarse_guess, screen)
    precond = residual * inverse
    image = operate(precond, screen)
    scaled = image * inverse
    scaled_image = operate(scaled, screen)
    sums = over_axes(
        jnp.stack(
            [
                jnp.sum(residual * precond),
                jnp.sum(precond * image),
                jnp.sum(image * scaled),
                jnp.sum(scaled * scaled_image),
            ]
        ),
        GX_GY,
    )
    gamma, delta, energy, curvature = sums[0], sums[1], sums[2], sums[3]
    alpha = gamma / delta
    gamma_next = alpha * alpha * energy - gamma
    ratio = gamma_next / gamma
    grow = 1.0 + ratio
    delta_next = grow * grow * delta - 2.0 * grow * alpha * energy + alpha * alpha * curvature
    alpha_next = gamma_next / delta_next
    solution = coarse_guess + alpha * precond
    residual = residual - alpha * image
    direction = residual * inverse + ratio * precond
    along = image - alpha * scaled_image + ratio * image
    solution = solution + alpha_next * direction
    residual = residual - alpha_next * along
    return (solution, residual)


def solution(mesh):
    split = Mesh(mesh.devices.reshape(4, 2, 4, 4), ("gx_0", "gx_1", "gy_0", "gy_1"))
    placed = (P(GX_GY, None), P(GX_GY, None), P(GX_GY), P(GX, GY, None), P(GX, GY, None))
    return jax.shard_map(
        body,
        mesh=split,
        in_specs=placed,
        out_specs=(P(GX, GY, None), P(GX, GY, None)),
        check_vma=False,
    )
```

```python
import jax
import jax.numpy as jnp
from jax import lax
from jax.sharding import Mesh
from jax.sharding import PartitionSpec as P
from jax.experimental import pallas as pl
from jax.experimental.pallas import tpu as pltpu

GX_GY = ("gx_0", "gx_1", "gy_0", "gy_1")
GX = ("gx_0", "gx_1")
GY = ("gy_0", "gy_1")


def shifted(piece, axis, pairs, dim):
    if dim == 1:
        flat = piece.reshape(piece.shape[0], piece.shape[2])
        return lax.ppermute(flat, axis, pairs).reshape(piece.shape)
    return lax.ppermute(piece, axis, pairs)


def extended(shard, sides, width):
    edges = {}
    for axis, dim in sides:
        count, length = (lax.axis_size(axis), shard.shape[dim])
        up = [(i, (i + 1) % count) for i in range(count - 1)]
        last = lax.slice_in_dim(shard, length - width, length, axis=dim)
        first = lax.slice_in_dim(shard, 0, width, axis=dim)
        edges[dim] = (
            shifted(last, axis, up, dim),
            shifted(first, axis, [(b, a) for a, b in up], dim),
        )
    done = []
    for _, dim in sides:
        low, high = edges[dim]
        around = [(width, width) if d in done else (0, 0) for d in range(shard.ndim)]
        shard = jnp.concatenate([jnp.pad(low, around), shard, jnp.pad(high, around)], axis=dim)
        done.append(dim)
    return shard


def over_axes(shard, axes):
    for axis in axes:
        shard = lax.psum(shard, axis)
    return shard


def with_halo(block, sides, width):
    for axis, dim in sides:
        count = lax.axis_size(axis)
        forward = [(i, i + 1) for i in range(count - 1)]
        backward = [(target, source) for source, target in forward]
        low = shifted(
            lax.slice_in_dim(block, block.shape[dim] - width, None, axis=dim), axis, forward, dim
        )
        high = shifted(lax.slice_in_dim(block, 0, width, axis=dim), axis, backward, dim)
        block = jnp.concatenate([low, block, high], axis=dim)
    return block


def build_send(bricks, brick_target, brick_slot, peers, capacity):
    target = brick_target[:, 0]
    onehot = (target[:, None] == jnp.arange(peers, dtype=jnp.int32)[None, :]).astype(jnp.int32)
    earlier = jnp.cumsum(onehot, axis=0) - onehot
    order = jnp.sum(earlier * onehot, axis=1)
    place = target * capacity + order
    high = lax.shift_right_logical(brick_slot, 5).astype(jnp.bfloat16)
    low = (brick_slot & 31).astype(jnp.bfloat16)
    lanes = jnp.arange(128, dtype=jnp.int32)[None, :]
    zero = jnp.zeros((), jnp.bfloat16)
    tag = jnp.where(lanes == 0, high[:, None], jnp.where(lanes == 1, low[:, None], zero))
    rows = jnp.concatenate([bricks, tag], axis=1)
    chosen = place[None, None, :] == (
        jnp.arange(peers, dtype=jnp.int32)[:, None, None] * capacity
        + jnp.arange(capacity, dtype=jnp.int32)[None, :, None]
    )
    payload = jnp.einsum(
        "pck,kj->pcj", chosen.astype(jnp.bfloat16), rows, preferred_element_type=jnp.float32
    )
    return payload.astype(jnp.bfloat16)


def next_along_z(field):
    edge = jnp.zeros(field.shape[:-1] + (1,), field.dtype)
    return jnp.concatenate([field[..., 1:], edge], axis=-1)


def prior_along_z(field):
    edge = jnp.zeros(field.shape[:-1] + (1,), field.dtype)
    return jnp.concatenate([edge, field[..., :-1]], axis=-1)


def operate(field, screen):
    padded = extended(field, ((GX, 0), (GY, 1)), 1)
    beside = padded[2:, 1:-1] + padded[:-2, 1:-1]
    beside = beside + padded[1:-1, 2:] + padded[1:-1, :-2]
    beside = beside + next_along_z(field) + prior_along_z(field)
    return (6.0 + screen) * field - beside


def component_grid(blocks, comp, span_x, span_y, span_z):
    part_blocks = blocks[:, comp, :].reshape(span_x, span_y, span_z, 8, 8, 8)
    grid = part_blocks.transpose(0, 3, 1, 4, 2, 5)
    return grid.reshape(span_x * 8, span_y * 8, span_z * 8)


def relayout_kernel(blk_ref, out_ref):
    sub = lax.broadcasted_iota(jnp.int32, (8, 128), 0)
    lane = lax.broadcasted_iota(jnp.int32, (8, 128), 1)
    grp = (lane // 8) % 8
    low_half = lane < 64
    swaps = []
    for m in (4, 2, 1):
        first = ((sub & m) == 0) & ((grp & m) != 0)
        second = ((sub & m) != 0) & ((grp & m) == 0)
        swaps.append((m, first, second))

    def transpose_groups(x):
        for m, first, second in swaps:
            a = pltpu.roll(pltpu.roll(x, 8 - m, 0), 8 * m, 1)
            b = pltpu.roll(pltpu.roll(x, m, 0), 128 - 8 * m, 1)
            x = jnp.where(first, a, jnp.where(second, b, x))
        return x

    def step(ly, carry):
        row = pl.multiple_of(ly * 16, 16)
        y = pl.multiple_of(ly * 8, 8)
        top = blk_ref[pl.ds(row, 8), :]
        bottom = blk_ref[pl.ds(row + 8, 8), :]
        for c in range(3):
            for uh in range(4):
                col = (c * 4 + uh) * 128
                s0 = top[:, col:col + 128]
                s1 = bottom[:, col:col + 128]
                u0 = jnp.where(low_half, s0, pltpu.roll(s1, 64, 1))
                u1 = jnp.where(low_half, pltpu.roll(s0, 64, 1), s1)
                out_ref[c, uh * 2, pl.ds(y, 8), :] = transpose_groups(u0)
                out_ref[c, uh * 2 + 1, pl.ds(y, 8), :] = transpose_groups(u1)
        return carry

    lax.fori_loop(0, 8, step, 0)


def to_grid(blocks, span_x, span_y, depth):
    cells = 3 * span_x * span_y * 64 * depth
    return pl.pallas_call(
        relayout_kernel,
        out_shape=jax.ShapeDtypeStruct((3, span_x * 8, span_y * 8, depth), jnp.float32),
        grid=(span_x,),
        in_specs=[pl.BlockSpec((span_y * 16, blocks.shape[1]), lambda i: (i, 0))],
        out_specs=pl.BlockSpec((3, 8, span_y * 8, depth), lambda i: (0, i, 0, 0)),
        cost_estimate=pl.CostEstimate(flops=20 * cells, bytes_accessed=8 * cells, transcendentals=0),
    )(blocks)


def body(bricks, brick_target, brick_slot, screen, coarse_guess):
    peers = lax.axis_size(GX_GY)
    capacity = max(2, 3 * bricks.shape[0] // peers)
    payload = build_send(bricks, brick_target, brick_slot, peers, capacity)
    arrived = lax.all_to_all(payload, GX_GY, split_axis=0, concat_axis=0, tiled=True)
    tag = arrived[:, :, 1536:1538].astype(jnp.int32)
    landed = tag[:, :, 0] * 32 + tag[:, :, 1]
    width_x, width_y, depth = screen.shape
    span_x = width_x // 8
    span_y = width_y // 8
    span_z = depth // 8
    picks = landed[:, :, None] == jnp.arange(span_x * span_y * span_z, dtype=jnp.int32)[None, None, :]
    blocks = jnp.einsum(
        "pcs,pcj->sj",
        picks.astype(jnp.bfloat16),
        arrived[:, :, :1536],
        preferred_element_type=jnp.float32,
    )
    normals = to_grid(blocks, span_x, span_y, depth)
    normal_x, normal_y, normal_z = normals[0], normals[1], normals[2]
    along_x = with_halo(normal_x, ((GX, 0),), 1)
    along_y = with_halo(normal_y, ((GY, 1),), 1)
    total = along_x[2:] - along_x[:-2]
    total = total + (along_y[:, 2:] - along_y[:, :-2])
    total = total + (next_along_z(normal_z) - prior_along_z(normal_z))
    source = -0.5 * total
    inverse = 1.0 / (6.0 + screen)
    residual = source - operate(coarse_guess, screen)
    precond = residual * inverse
    image = operate(precond, screen)
    scaled = image * inverse
    scaled_image = operate(scaled, screen)
    sums = over_axes(
        jnp.stack(
            [
                jnp.sum(residual * precond),
                jnp.sum(precond * image),
                jnp.sum(image * scaled),
                jnp.sum(scaled * scaled_image),
            ]
        ),
        GX_GY,
    )
    gamma, delta, energy, curvature = sums[0], sums[1], sums[2], sums[3]
    alpha = gamma / delta
    gamma_next = alpha * alpha * energy - gamma
    ratio = gamma_next / gamma
    grow = 1.0 + ratio
    delta_next = grow * grow * delta - 2.0 * grow * alpha * energy + alpha * alpha * curvature
    alpha_next = gamma_next / delta_next
    solution = coarse_guess + alpha * precond
    residual = residual - alpha * image
    direction = residual * inverse + ratio * precond
    along = image - alpha * scaled_image + ratio * image
    solution = solution + alpha_next * direction
    residual = residual - alpha_next * along
    return (solution, residual)


def solution(mesh):
    split = Mesh(mesh.devices.reshape(4, 2, 4, 4), ("gx_0", "gx_1", "gy_0", "gy_1"))
    placed = (P(GX_GY, None), P(GX_GY, None), P(GX_GY), P(GX, GY, None), P(GX, GY, None))
    return jax.shard_map(
        body,
        mesh=split,
        in_specs=placed,
        out_specs=(P(GX, GY, None), P(GX, GY, None)),
        check_vma=False,
    )
```

```python
import jax
import jax.numpy as jnp
from jax import lax
from jax.sharding import Mesh
from jax.sharding import PartitionSpec as P
from jax.experimental import pallas as pl
from jax.experimental.pallas import tpu as pltpu

GX_GY = ("gx_0", "gx_1", "gy_0", "gy_1")
GX = ("gx_0", "gx_1")
GY = ("gy_0", "gy_1")


def shifted(piece, axis, pairs, dim):
    if dim == 1:
        flat = piece.reshape(piece.shape[0], piece.shape[2])
        return lax.ppermute(flat, axis, pairs).reshape(piece.shape)
    return lax.ppermute(piece, axis, pairs)


def extended(shard, sides, width):
    edges = {}
    for axis, dim in sides:
        count, length = (lax.axis_size(axis), shard.shape[dim])
        up = [(i, (i + 1) % count) for i in range(count - 1)]
        last = lax.slice_in_dim(shard, length - width, length, axis=dim)
        first = lax.slice_in_dim(shard, 0, width, axis=dim)
        edges[dim] = (
            shifted(last, axis, up, dim),
            shifted(first, axis, [(b, a) for a, b in up], dim),
        )
    done = []
    for _, dim in sides:
        low, high = edges[dim]
        around = [(width, width) if d in done else (0, 0) for d in range(shard.ndim)]
        shard = jnp.concatenate([jnp.pad(low, around), shard, jnp.pad(high, around)], axis=dim)
        done.append(dim)
    return shard


def over_axes(shard, axes):
    for axis in axes:
        shard = lax.psum(shard, axis)
    return shard


def with_halo(block, sides, width):
    for axis, dim in sides:
        count = lax.axis_size(axis)
        forward = [(i, i + 1) for i in range(count - 1)]
        backward = [(target, source) for source, target in forward]
        low = shifted(
            lax.slice_in_dim(block, block.shape[dim] - width, None, axis=dim), axis, forward, dim
        )
        high = shifted(lax.slice_in_dim(block, 0, width, axis=dim), axis, backward, dim)
        block = jnp.concatenate([low, block, high], axis=dim)
    return block


def build_send(bricks, brick_target, brick_slot, peers, capacity):
    target = brick_target[:, 0]
    onehot = (target[:, None] == jnp.arange(peers, dtype=jnp.int32)[None, :]).astype(jnp.int32)
    earlier = jnp.cumsum(onehot, axis=0) - onehot
    order = jnp.sum(earlier * onehot, axis=1)
    place = target * capacity + order
    high = lax.shift_right_logical(brick_slot, 5).astype(jnp.bfloat16)
    low = (brick_slot & 31).astype(jnp.bfloat16)
    lanes = jnp.arange(128, dtype=jnp.int32)[None, :]
    zero = jnp.zeros((), jnp.bfloat16)
    tag = jnp.where(lanes == 0, high[:, None], jnp.where(lanes == 1, low[:, None], zero))
    rows = jnp.concatenate([bricks, tag], axis=1)
    chosen = place[None, :] == jnp.arange(peers * capacity, dtype=jnp.int32)[:, None]
    payload = jnp.einsum(
        "pk,kj->pj", chosen.astype(jnp.bfloat16), rows, preferred_element_type=jnp.float32
    ).reshape(peers, capacity, rows.shape[1])
    return payload.astype(jnp.bfloat16)


def next_along_z(field):
    edge = jnp.zeros(field.shape[:-1] + (1,), field.dtype)
    return jnp.concatenate([field[..., 1:], edge], axis=-1)


def prior_along_z(field):
    edge = jnp.zeros(field.shape[:-1] + (1,), field.dtype)
    return jnp.concatenate([edge, field[..., :-1]], axis=-1)


def operate(field, screen):
    padded = extended(field, ((GX, 0), (GY, 1)), 1)
    beside = padded[2:, 1:-1] + padded[:-2, 1:-1]
    beside = beside + padded[1:-1, 2:] + padded[1:-1, :-2]
    beside = beside + next_along_z(field) + prior_along_z(field)
    return (6.0 + screen) * field - beside


def component_grid(blocks, comp, span_x, span_y, span_z):
    part_blocks = blocks[:, comp, :].reshape(span_x, span_y, span_z, 8, 8, 8)
    grid = part_blocks.transpose(0, 3, 1, 4, 2, 5)
    return grid.reshape(span_x * 8, span_y * 8, span_z * 8)


def relayout_kernel(blk_ref, out_ref):
    sub = lax.broadcasted_iota(jnp.int32, (8, 128), 0)
    lane = lax.broadcasted_iota(jnp.int32, (8, 128), 1)
    grp = (lane // 8) % 8
    low_half = lane < 64
    swaps = []
    for m in (4, 2, 1):
        first = ((sub & m) == 0) & ((grp & m) != 0)
        second = ((sub & m) != 0) & ((grp & m) == 0)
        swaps.append((m, first, second))

    def transpose_groups(x):
        for m, first, second in swaps:
            a = pltpu.roll(pltpu.roll(x, 8 - m, 0), 8 * m, 1)
            b = pltpu.roll(pltpu.roll(x, m, 0), 128 - 8 * m, 1)
            x = jnp.where(first, a, jnp.where(second, b, x))
        return x

    def step(ly, carry):
        row = pl.multiple_of(ly * 16, 16)
        y = pl.multiple_of(ly * 8, 8)
        top = blk_ref[pl.ds(row, 8), :]
        bottom = blk_ref[pl.ds(row + 8, 8), :]
        for c in range(3):
            for uh in range(4):
                col = (c * 4 + uh) * 128
                s0 = top[:, col:col + 128]
                s1 = bottom[:, col:col + 128]
                u0 = jnp.where(low_half, s0, pltpu.roll(s1, 64, 1))
                u1 = jnp.where(low_half, pltpu.roll(s0, 64, 1), s1)
                out_ref[c, uh * 2, pl.ds(y, 8), :] = transpose_groups(u0)
                out_ref[c, uh * 2 + 1, pl.ds(y, 8), :] = transpose_groups(u1)
        return carry

    lax.fori_loop(0, 8, step, 0)


def to_grid(blocks, span_x, span_y, depth):
    cells = 3 * span_x * span_y * 64 * depth
    return pl.pallas_call(
        relayout_kernel,
        out_shape=jax.ShapeDtypeStruct((3, span_x * 8, span_y * 8, depth), jnp.float32),
        grid=(span_x,),
        in_specs=[pl.BlockSpec((span_y * 16, blocks.shape[1]), lambda i: (i, 0))],
        out_specs=pl.BlockSpec((3, 8, span_y * 8, depth), lambda i: (0, i, 0, 0)),
        cost_estimate=pl.CostEstimate(flops=20 * cells, bytes_accessed=8 * cells, transcendentals=0),
    )(blocks)


def body(bricks, brick_target, brick_slot, screen, coarse_guess):
    peers = lax.axis_size(GX_GY)
    capacity = max(2, 3 * bricks.shape[0] // peers)
    payload = build_send(bricks, brick_target, brick_slot, peers, capacity)
    arrived = lax.all_to_all(payload, GX_GY, split_axis=0, concat_axis=0, tiled=True)
    tag = arrived[:, :, 1536:1538].astype(jnp.int32)
    landed = tag[:, :, 0] * 32 + tag[:, :, 1]
    width_x, width_y, depth = screen.shape
    span_x = width_x // 8
    span_y = width_y // 8
    span_z = depth // 8
    picks = landed[:, :, None] == jnp.arange(span_x * span_y * span_z, dtype=jnp.int32)[None, None, :]
    blocks = jnp.einsum(
        "pcs,pcj->sj",
        picks.astype(jnp.bfloat16),
        arrived[:, :, :1536],
        preferred_element_type=jnp.float32,
    )
    normals = to_grid(blocks, span_x, span_y, depth)
    normal_x, normal_y, normal_z = normals[0], normals[1], normals[2]
    along_x = with_halo(normal_x, ((GX, 0),), 1)
    along_y = with_halo(normal_y, ((GY, 1),), 1)
    total = along_x[2:] - along_x[:-2]
    total = total + (along_y[:, 2:] - along_y[:, :-2])
    total = total + (next_along_z(normal_z) - prior_along_z(normal_z))
    source = -0.5 * total
    inverse = 1.0 / (6.0 + screen)
    residual = source - operate(coarse_guess, screen)
    precond = residual * inverse
    image = operate(precond, screen)
    scaled = image * inverse
    scaled_image = operate(scaled, screen)
    sums = over_axes(
        jnp.stack(
            [
                jnp.sum(residual * precond),
                jnp.sum(precond * image),
                jnp.sum(image * scaled),
                jnp.sum(scaled * scaled_image),
            ]
        ),
        GX_GY,
    )
    gamma, delta, energy, curvature = sums[0], sums[1], sums[2], sums[3]
    alpha = gamma / delta
    gamma_next = alpha * alpha * energy - gamma
    ratio = gamma_next / gamma
    grow = 1.0 + ratio
    delta_next = grow * grow * delta - 2.0 * grow * alpha * energy + alpha * alpha * curvature
    alpha_next = gamma_next / delta_next
    solution = coarse_guess + alpha * precond
    residual = residual - alpha * image
    direction = residual * inverse + ratio * precond
    along = image - alpha * scaled_image + ratio * image
    solution = solution + alpha_next * direction
    residual = residual - alpha_next * along
    return (solution, residual)


def solution(mesh):
    split = Mesh(mesh.devices.reshape(4, 2, 4, 4), ("gx_0", "gx_1", "gy_0", "gy_1"))
    placed = (P(GX_GY, None), P(GX_GY, None), P(GX_GY), P(GX, GY, None), P(GX, GY, None))
    return jax.shard_map(
        body,
        mesh=split,
        in_specs=placed,
        out_specs=(P(GX, GY, None), P(GX, GY, None)),
        check_vma=False,
    )
```

```python
import jax
import jax.numpy as jnp
from jax import lax
from jax.sharding import Mesh
from jax.sharding import PartitionSpec as P
from jax.experimental import pallas as pl
from jax.experimental.pallas import tpu as pltpu

GX_GY = ("gx_0", "gx_1", "gy_0", "gy_1")
GX = ("gx_0", "gx_1")
GY = ("gy_0", "gy_1")


def shifted(piece, axis, pairs, dim):
    if dim == 1:
        flat = piece.reshape(piece.shape[0], piece.shape[2])
        return lax.ppermute(flat, axis, pairs).reshape(piece.shape)
    return lax.ppermute(piece, axis, pairs)


def extended(shard, sides, width):
    edges = {}
    for axis, dim in sides:
        count, length = (lax.axis_size(axis), shard.shape[dim])
        up = [(i, (i + 1) % count) for i in range(count - 1)]
        last = lax.slice_in_dim(shard, length - width, length, axis=dim)
        first = lax.slice_in_dim(shard, 0, width, axis=dim)
        edges[dim] = (
            shifted(last, axis, up, dim),
            shifted(first, axis, [(b, a) for a, b in up], dim),
        )
    done = []
    for _, dim in sides:
        low, high = edges[dim]
        around = [(width, width) if d in done else (0, 0) for d in range(shard.ndim)]
        shard = jnp.concatenate([jnp.pad(low, around), shard, jnp.pad(high, around)], axis=dim)
        done.append(dim)
    return shard


def over_axes(shard, axes):
    for axis in axes:
        shard = lax.psum(shard, axis)
    return shard


def with_halo(block, sides, width):
    for axis, dim in sides:
        count = lax.axis_size(axis)
        forward = [(i, i + 1) for i in range(count - 1)]
        backward = [(target, source) for source, target in forward]
        low = shifted(
            lax.slice_in_dim(block, block.shape[dim] - width, None, axis=dim), axis, forward, dim
        )
        high = shifted(lax.slice_in_dim(block, 0, width, axis=dim), axis, backward, dim)
        block = jnp.concatenate([low, block, high], axis=dim)
    return block


def build_send(bricks, brick_target, brick_slot, peers, capacity):
    target = brick_target[:, 0]
    onehot = (target[:, None] == jnp.arange(peers, dtype=jnp.int32)[None, :]).astype(jnp.int32)
    earlier = jnp.cumsum(onehot, axis=0) - onehot
    order = jnp.sum(earlier * onehot, axis=1)
    place = target * capacity + order
    high = lax.shift_right_logical(brick_slot, 5).astype(jnp.bfloat16)
    low = (brick_slot & 31).astype(jnp.bfloat16)
    lanes = jnp.arange(128, dtype=jnp.int32)[None, :]
    zero = jnp.zeros((), jnp.bfloat16)
    tag = jnp.where(lanes == 0, high[:, None], jnp.where(lanes == 1, low[:, None], zero))
    rows = jnp.concatenate([bricks, tag], axis=1)
    chosen = place[None, :] == jnp.arange(peers * capacity, dtype=jnp.int32)[:, None]
    payload = jnp.einsum(
        "pk,kj->pj", chosen.astype(jnp.bfloat16), rows, preferred_element_type=jnp.bfloat16
    ).reshape(peers, capacity, rows.shape[1])
    return payload.astype(jnp.bfloat16)


def next_along_z(field):
    edge = jnp.zeros(field.shape[:-1] + (1,), field.dtype)
    return jnp.concatenate([field[..., 1:], edge], axis=-1)


def prior_along_z(field):
    edge = jnp.zeros(field.shape[:-1] + (1,), field.dtype)
    return jnp.concatenate([edge, field[..., :-1]], axis=-1)


def operate(field, screen):
    padded = extended(field, ((GX, 0), (GY, 1)), 1)
    beside = padded[2:, 1:-1] + padded[:-2, 1:-1]
    beside = beside + padded[1:-1, 2:] + padded[1:-1, :-2]
    beside = beside + next_along_z(field) + prior_along_z(field)
    return (6.0 + screen) * field - beside


def component_grid(blocks, comp, span_x, span_y, span_z):
    part_blocks = blocks[:, comp, :].reshape(span_x, span_y, span_z, 8, 8, 8)
    grid = part_blocks.transpose(0, 3, 1, 4, 2, 5)
    return grid.reshape(span_x * 8, span_y * 8, span_z * 8)


def relayout_kernel(blk_ref, out_ref):
    sub = lax.broadcasted_iota(jnp.int32, (8, 128), 0)
    lane = lax.broadcasted_iota(jnp.int32, (8, 128), 1)
    grp = (lane // 8) % 8
    low_half = lane < 64
    swaps = []
    for m in (4, 2, 1):
        first = ((sub & m) == 0) & ((grp & m) != 0)
        second = ((sub & m) != 0) & ((grp & m) == 0)
        swaps.append((m, first, second))

    def transpose_groups(x):
        for m, first, second in swaps:
            a = pltpu.roll(pltpu.roll(x, 8 - m, 0), 8 * m, 1)
            b = pltpu.roll(pltpu.roll(x, m, 0), 128 - 8 * m, 1)
            x = jnp.where(first, a, jnp.where(second, b, x))
        return x

    def step(ly, carry):
        row = pl.multiple_of(ly * 16, 16)
        y = pl.multiple_of(ly * 8, 8)
        top = blk_ref[pl.ds(row, 8), :]
        bottom = blk_ref[pl.ds(row + 8, 8), :]
        for c in range(3):
            for uh in range(4):
                col = (c * 4 + uh) * 128
                s0 = top[:, col:col + 128]
                s1 = bottom[:, col:col + 128]
                u0 = jnp.where(low_half, s0, pltpu.roll(s1, 64, 1))
                u1 = jnp.where(low_half, pltpu.roll(s0, 64, 1), s1)
                out_ref[c, uh * 2, pl.ds(y, 8), :] = transpose_groups(u0)
                out_ref[c, uh * 2 + 1, pl.ds(y, 8), :] = transpose_groups(u1)
        return carry

    lax.fori_loop(0, 8, step, 0)


def to_grid(blocks, span_x, span_y, depth):
    cells = 3 * span_x * span_y * 64 * depth
    return pl.pallas_call(
        relayout_kernel,
        out_shape=jax.ShapeDtypeStruct((3, span_x * 8, span_y * 8, depth), jnp.float32),
        grid=(span_x,),
        in_specs=[pl.BlockSpec((span_y * 16, blocks.shape[1]), lambda i: (i, 0))],
        out_specs=pl.BlockSpec((3, 8, span_y * 8, depth), lambda i: (0, i, 0, 0)),
        cost_estimate=pl.CostEstimate(flops=20 * cells, bytes_accessed=8 * cells, transcendentals=0),
    )(blocks)


def body(bricks, brick_target, brick_slot, screen, coarse_guess):
    peers = lax.axis_size(GX_GY)
    capacity = max(2, 3 * bricks.shape[0] // peers)
    payload = build_send(bricks, brick_target, brick_slot, peers, capacity)
    arrived = lax.all_to_all(payload, GX_GY, split_axis=0, concat_axis=0, tiled=True)
    tag = arrived[:, :, 1536:1538].astype(jnp.int32)
    landed = tag[:, :, 0] * 32 + tag[:, :, 1]
    width_x, width_y, depth = screen.shape
    span_x = width_x // 8
    span_y = width_y // 8
    span_z = depth // 8
    picks = landed[:, :, None] == jnp.arange(span_x * span_y * span_z, dtype=jnp.int32)[None, None, :]
    blocks = jnp.einsum(
        "pcs,pcj->sj",
        picks.astype(jnp.bfloat16),
        arrived[:, :, :1536],
        preferred_element_type=jnp.float32,
    )
    normals = to_grid(blocks, span_x, span_y, depth)
    normal_x, normal_y, normal_z = normals[0], normals[1], normals[2]
    along_x = with_halo(normal_x, ((GX, 0),), 1)
    along_y = with_halo(normal_y, ((GY, 1),), 1)
    total = along_x[2:] - along_x[:-2]
    total = total + (along_y[:, 2:] - along_y[:, :-2])
    total = total + (next_along_z(normal_z) - prior_along_z(normal_z))
    source = -0.5 * total
    inverse = 1.0 / (6.0 + screen)
    residual = source - operate(coarse_guess, screen)
    precond = residual * inverse
    image = operate(precond, screen)
    scaled = image * inverse
    scaled_image = operate(scaled, screen)
    sums = over_axes(
        jnp.stack(
            [
                jnp.sum(residual * precond),
                jnp.sum(precond * image),
                jnp.sum(image * scaled),
                jnp.sum(scaled * scaled_image),
            ]
        ),
        GX_GY,
    )
    gamma, delta, energy, curvature = sums[0], sums[1], sums[2], sums[3]
    alpha = gamma / delta
    gamma_next = alpha * alpha * energy - gamma
    ratio = gamma_next / gamma
    grow = 1.0 + ratio
    delta_next = grow * grow * delta - 2.0 * grow * alpha * energy + alpha * alpha * curvature
    alpha_next = gamma_next / delta_next
    solution = coarse_guess + alpha * precond
    residual = residual - alpha * image
    direction = residual * inverse + ratio * precond
    along = image - alpha * scaled_image + ratio * image
    solution = solution + alpha_next * direction
    residual = residual - alpha_next * along
    return (solution, residual)


def solution(mesh):
    split = Mesh(mesh.devices.reshape(4, 2, 4, 4), ("gx_0", "gx_1", "gy_0", "gy_1"))
    placed = (P(GX_GY, None), P(GX_GY, None), P(GX_GY), P(GX, GY, None), P(GX, GY, None))
    return jax.shard_map(
        body,
        mesh=split,
        in_specs=placed,
        out_specs=(P(GX, GY, None), P(GX, GY, None)),
        check_vma=False,
    )
```
